32 devices in a mesh: groups: 2 (over x), heads: 4 (over y, core), seq: 4 (over z).
Axes of the slice: x: 2, y: 2, z: 4, core: 2. Of those that a mesh axis runs over, the one named last changes fastest.
Arguments:
- lin_query: bfloat16 [4096, 4096], P(('groups', 'seq'), 'heads'), parts along dimension 0, may hold values from -6 to 6
- lin_key: bfloat16 [4096, 4096], P(('groups', 'seq'), 'heads'), parts along dimension 0, may hold values from -6 to 6
- lin_value: bfloat16 [4096, 4096], P(('groups', 'seq'), 'heads'), parts along dimension 0, may hold values from -6 to 6
- log_decay: float32 [4096, 32], P(('groups', 'seq'), 'heads'), parts along dimension 0, may hold values from -1 to 0
- stream: bfloat16 [4096, 6144], P(('groups', 'seq'), 'heads'), parts along dimension 0, may hold values from -400 to 400
- out_weight: bfloat16 [4096, 6144], P('heads', 'seq'), may hold values from -0.125 to 0.125
- norm_gain: bfloat16 [6144], P('heads'), may hold values from 0.5 to 1.5
- query_weight: bfloat16 [6144, 4096], P('seq', 'heads'), may hold values from -12 to 12
- kv_weight: bfloat16 [4, 6144, 256], P(None, 'seq'), may hold values from -1 to 1
Outputs:
- stream_next: bfloat16 [4096, 6144], P(('groups', 'seq'), 'heads'), parts along dimension 0
- attended: bfloat16 [4096, 4096], P(('groups', 'seq'), 'heads'), parts along dimension 0
The draws below stay inside these ranges and needn't reach their ends.
There are 2 independent parts, one for each index of `groups`. The reference program is written for one: setup_inputs(seed, part) draws one part's arguments, and reference() takes and returns one part's arrays. A program takes and returns all parts, laid end to end along the dimension named above; an argument that names none is the same for every part. Nothing has to cross between parts.
All inputs are finite; a program needn't handle non-finite values.
Results may differ from the reference program's by a relative error of at most 0.019.
Values may be sent and summed in bfloat16 or wider, within the bound.
No kernel may reach another device: no remote copies, remote signals or barrier semaphores. Data moves between devices by JAX's collectives and lax.ppermute only.
A program may use at most 128 MiB of HBM per device.

```python
import math
import jax
import jax.numpy as jnp
from jax import lax

D = 6144
QUERY_HEADS = 32
KVH = 4
DH = 128
BLOCK = 256
TOK_DEV = 512
SEQUENCE_LENGTH = 2048
N_HEADS = 4


def draw_log_decay(key, part):
    fast_mask = jax.random.randint(jax.random.fold_in(key, 1), (QUERY_HEADS,), 0, 2) == 0
    ruggedness = jax.random.uniform(jax.random.fold_in(key, 5), (SEQUENCE_LENGTH, QUERY_HEADS), jnp.float32, 0.4, 1.6)
    fast_rate = jnp.exp(jax.random.uniform(jax.random.fold_in(key, 2), (QUERY_HEADS,), jnp.float32, math.log(1.0 / 50.0), math.log(1.0 / 30.0)))
    slow_rate = jnp.exp(jax.random.uniform(jax.random.fold_in(key, 3), (QUERY_HEADS,), jnp.float32, math.log(0.05), math.log(0.4))) / SEQUENCE_LENGTH
    baseline_rate = jnp.where(fast_mask, fast_rate, slow_rate)
    block_count = SEQUENCE_LENGTH // TOK_DEV
    block_multiplier = jnp.exp(jax.random.uniform(jax.random.fold_in(key, 4), (block_count, QUERY_HEADS), jnp.float32, math.log(0.25), math.log(4.0)))
    block_multiplier = jnp.repeat(block_multiplier, TOK_DEV, axis=0)
    spike_location = jax.random.randint(jax.random.fold_in(key, 6), (3,), 0, SEQUENCE_LENGTH)
    spike_struck = jnp.any(jnp.arange(SEQUENCE_LENGTH)[:, None] == spike_location[None, :], axis=1)
    spike_falloff = jnp.log(jax.random.uniform(jax.random.fold_in(key, 7), (SEQUENCE_LENGTH, QUERY_HEADS), jnp.float32, 0.55, 0.8))
    outcome_value = -(baseline_rate[None, :] * block_multiplier * ruggedness) + jnp.where(spike_struck[:, None], spike_falloff, 0.0)
    return outcome_value.astype(jnp.float32)


def draw_stream(key, part):
    col_index = jnp.arange(D).astype(jnp.float32)
    col_scale = 3.0 ** (col_index / D) * jnp.exp(jax.random.uniform(jax.random.fold_in(key, 1), (D,), jnp.float32, 0.0, math.log(10.0))) / 3.0
    row_scale = jnp.exp(jax.random.uniform(jax.random.fold_in(key, 5), (SEQUENCE_LENGTH,), jnp.float32, 0.0, math.log(10.0))) / 4.0
    outcome_value = jax.random.normal(jax.random.fold_in(key, 2), (SEQUENCE_LENGTH, D), jnp.float32) * row_scale[:, None] * col_scale[None, :]
    return jnp.clip(outcome_value, -400.0, 400.0).astype(jnp.bfloat16)


def shared_key_weight(key):
    key_weight = jax.random.normal(jax.random.fold_in(key, 101), (KVH, D, DH), jnp.float32) / math.sqrt(D)
    return key_weight


def draw_kv_weight(key, part):
    key_weight = shared_key_weight(key)
    value_weight = jax.random.normal(jax.random.fold_in(key, 102), (KVH, D, DH), jnp.float32) / math.sqrt(D)
    return jnp.clip(jnp.concatenate([key_weight, value_weight], axis=2), -1.0, 1.0).astype(jnp.bfloat16)


def draw_query_weight(key, part):
    independent = jax.random.normal(jax.random.fold_in(key, 103), (D, QUERY_HEADS * DH), jnp.float32) / math.sqrt(D)
    outcome_value = independent
    return jnp.clip(outcome_value, -12.0, 12.0).astype(jnp.bfloat16)


def raised(array, own_key, source, target, blocks, factor):
    owner, partner = [(jnp.arange(array.shape[position]) // (array.shape[position] // blocks)).reshape([-1 if axis == position else 1 for axis in range(array.ndim)]) for position in (source, target)]
    chosen = jax.random.permutation(own_key, blocks)[partner]
    strong = (owner == chosen) | (owner == (partner + blocks // 2) % blocks)
    return jnp.where(strong, factor * array, array)


def shard_levels(stream_key, dims, cuts, least, largest):
    def one(dim, shards_of):
        heights = jax.random.uniform(jax.random.fold_in(jax.random.fold_in(stream_key, 6), dim), (shards_of,), jnp.float32, least / len(cuts), largest / len(cuts))
        return jnp.repeat(jnp.exp(heights), dims[dim] // shards_of).reshape((-1,) + (1,) * (len(dims) - dim - 1))

    level = one(*cuts[0])
    for cut in cuts[1:]:
        level = level * one(*cut)
    return level


def noise(stream_key, dims, scale, bound, cuts=(), dtype=jnp.bfloat16):
    drawn = jax.random.normal(stream_key, dims, jnp.float32) * scale
    if len(cuts) > 0:
        drawn = shard_levels(stream_key, dims, cuts, -0.22, 0.18) * drawn
    return jnp.clip(drawn, min=-bound, max=bound).astype(dtype)


def noise_with(key, extent, scale, reach, pieces, heavy, held_as=jnp.bfloat16):
    values = scale * jax.random.normal(key, extent, jnp.float32)
    if pieces:
        values = values * shard_levels(key, extent, pieces, -0.22, 0.18)
    return jnp.clip(raised(values, jax.random.fold_in(key, 3), *heavy), -reach, reach).astype(held_as)


def setup_inputs(seed: int = 0, part: int = 0) -> dict:
    arg_keys = jax.random.split(jax.random.key(seed), 10)
    own_keys = jax.random.split(jax.random.fold_in(arg_keys[9], part), 10)
    return {
        "lin_query": noise(own_keys[0], (SEQUENCE_LENGTH, QUERY_HEADS * DH), 1.0, 6.0, ((0, 4), (1, 4))),
        "lin_key": noise(own_keys[1], (SEQUENCE_LENGTH, QUERY_HEADS * DH), 1.0, 6.0, ((0, 4), (1, 4))),
        "lin_value": noise(own_keys[2], (SEQUENCE_LENGTH, QUERY_HEADS * DH), 1.0, 6.0, ((0, 4), (1, 4))),
        "log_decay": draw_log_decay(jax.random.fold_in(jax.random.fold_in(arg_keys[9], part), 71), part),
        "stream": draw_stream(jax.random.fold_in(jax.random.fold_in(arg_keys[9], part), 71), part),
        "out_weight": noise_with(arg_keys[5], (QUERY_HEADS * DH, D), (QUERY_HEADS * DH) ** -0.5, 0.125, ((0, 4), (1, 4)), (0, 1, 4, 2.0)),
        "norm_gain": jnp.clip(1.0 + 0.1 * jax.random.normal(arg_keys[6], (D,), jnp.float32), 0.5, 1.5).astype(jnp.bfloat16),
        "query_weight": draw_query_weight(jax.random.fold_in(arg_keys[9], 71), part),
        "kv_weight": draw_kv_weight(jax.random.fold_in(arg_keys[9], 71), part),
    }


def lightning_block(kv_state, block_inputs):
    query_blk, key_blk, value_blk, decay_blk = block_inputs
    query_f = query_blk.astype(jnp.float32)
    key_f = key_blk.astype(jnp.float32)
    value_f = value_blk.astype(jnp.float32)
    local_cum = jnp.cumsum(decay_blk, axis=0)
    causal_mask = (jnp.arange(BLOCK)[:, None] >= jnp.arange(BLOCK)[None, :])[:, :, None]
    decay_diff = local_cum[:, None, :] - local_cum[None, :, :]
    decays = jnp.where(causal_mask, jnp.exp(jnp.where(causal_mask, decay_diff, 0.0)), 0.0)
    scores = jnp.einsum('thd,shd->hts', query_f, key_f, precision=lax.Precision.HIGHEST)
    weights = (scores * jnp.transpose(decays, (2, 0, 1))).astype(jnp.bfloat16)
    intra_out = jnp.einsum('hts,shd->thd', weights.astype(jnp.float32), value_f, precision=lax.Precision.HIGHEST)
    inter_out = jnp.einsum('thd,hde->the', query_f * jnp.exp(local_cum)[:, :, None], kv_state, precision=lax.Precision.HIGHEST)
    tail_decay = jnp.exp(local_cum[-1][None, :] - local_cum)
    kv_state = jnp.exp(local_cum[-1])[:, None, None] * kv_state + jnp.einsum('shd,she->hde', key_f * tail_decay[:, :, None], value_f, precision=lax.Precision.HIGHEST)
    return (kv_state, intra_out + inter_out)

def reference(lin_query, lin_key, lin_value, log_decay, stream, out_weight, norm_gain, query_weight, kv_weight):
    nblocks = SEQUENCE_LENGTH // BLOCK
    block_shape = (nblocks, BLOCK, QUERY_HEADS, DH)
    inputs = (lin_query.reshape(block_shape), lin_key.reshape(block_shape), lin_value.reshape(block_shape), log_decay.reshape(nblocks, BLOCK, QUERY_HEADS))
    _, lin_raw = lax.scan(lightning_block, jnp.zeros((QUERY_HEADS, DH, DH), jnp.float32), inputs)
    lin_raw = lin_raw.reshape(SEQUENCE_LENGTH, QUERY_HEADS, DH)
    lin_out = (lin_raw * lax.rsqrt(lax.optimization_barrier(jnp.mean(lin_raw * lin_raw, axis=-1, keepdims=True)) + 1e-06)).astype(jnp.bfloat16).reshape(SEQUENCE_LENGTH, QUERY_HEADS * DH)
    group_rows = QUERY_HEADS * DH // N_HEADS
    branch = jnp.zeros((SEQUENCE_LENGTH, D), jnp.float32)
    for head_group in range(N_HEADS):
        lo_row = head_group * group_rows
        partial_sum = jnp.dot(lin_out[:, lo_row:lo_row + group_rows], out_weight[lo_row:lo_row + group_rows], preferred_element_type=jnp.float32).astype(jnp.bfloat16)
        partial_sum = lax.optimization_barrier(partial_sum)
        branch = branch + partial_sum.astype(jnp.float32)
    mixed_sum = stream.astype(jnp.float32) + branch
    stream_next = mixed_sum.astype(jnp.bfloat16)
    mean_sq = lax.optimization_barrier(jnp.mean(mixed_sum * mixed_sum, axis=1))
    normed = (mixed_sum * lax.rsqrt(mean_sq + 1e-05)[:, None] * norm_gain.astype(jnp.float32)[None, :]).astype(jnp.bfloat16)
    queries = jnp.dot(normed, query_weight, preferred_element_type=jnp.float32).astype(jnp.bfloat16)
    queries = jnp.transpose(queries.reshape(SEQUENCE_LENGTH, QUERY_HEADS, DH), (1, 0, 2))
    keys_values = lax.map(lambda weight_g: jnp.dot(normed, weight_g, preferred_element_type=jnp.float32).astype(jnp.bfloat16), kv_weight)
    score_scale = float(DH) ** (-0.5)
    causal_mask = jnp.arange(SEQUENCE_LENGTH)[:, None] >= jnp.arange(SEQUENCE_LENGTH)[None, :]

    def one_head(head_inputs):
        query_h, kv_group = head_inputs
        kv_head = lax.dynamic_index_in_dim(keys_values, kv_group, 0, keepdims=False)
        scores = jnp.dot(query_h, kv_head[:, :DH].T, preferred_element_type=jnp.float32) * score_scale
        scores = jnp.where(causal_mask, scores, -1e+30)
        row_max = lax.optimization_barrier(jnp.max(scores, axis=1, keepdims=True))
        expos = jnp.where(causal_mask, jnp.exp(scores - row_max), 0.0)
        prob_bf16 = expos.astype(jnp.bfloat16)
        weighted = jnp.dot(prob_bf16, kv_head[:, DH:], preferred_element_type=jnp.float32)
        return (weighted / lax.optimization_barrier(jnp.sum(expos, axis=1, keepdims=True))).astype(jnp.bfloat16)
    groups_of = (jnp.arange(QUERY_HEADS) // (QUERY_HEADS // KVH)).astype(jnp.int32)
    attended = lax.map(one_head, (queries, groups_of))
    attended = jnp.transpose(attended, (1, 0, 2)).reshape(SEQUENCE_LENGTH, QUERY_HEADS * DH)
    return (stream_next, attended)
```

```python
import jax
import jax.numpy as jnp
from jax import lax
from jax.sharding import PartitionSpec as P

D = 6144
QUERY_HEADS = 32
KVH = 4
DH = 128
BLOCK = 256


def from_behind(value, axis, steps):
    count = lax.axis_size(axis)
    leading, last = (max(0, -steps), min(count, count - steps))
    return lax.ppermute(value, axis, [(source, source + steps) for source in range(leading, last)])


def lightning_block(kv_state, block_inputs):
    query_blk, key_blk, value_blk, decay_blk = block_inputs
    block_len = query_blk.shape[0]
    local_cum = jnp.cumsum(decay_blk, axis=0)
    causal_mask = (jnp.arange(block_len)[:, None] >= jnp.arange(block_len)[None, :])[:, :, None]
    decay_diff = local_cum[:, None, :] - local_cum[None, :, :]
    decays = jnp.where(causal_mask, jnp.exp(jnp.where(causal_mask, decay_diff, 0.0)), 0.0)
    scores = jnp.einsum("thd,shd->hts", query_blk, key_blk, preferred_element_type=jnp.float32)
    weights = (scores * jnp.transpose(decays, (2, 0, 1))).astype(jnp.bfloat16)
    intra_out = jnp.einsum("hts,shd->thd", weights, value_blk, preferred_element_type=jnp.float32)
    query_f = query_blk.astype(jnp.float32)
    inter_out = jnp.einsum(
        "thd,hde->the",
        query_f * jnp.exp(local_cum)[:, :, None],
        kv_state,
        precision=lax.Precision.HIGHEST,
    )
    tail_decay = jnp.exp(local_cum[-1][None, :] - local_cum)
    key_f = key_blk.astype(jnp.float32) * tail_decay[:, :, None]
    kv_state = jnp.exp(local_cum[-1])[:, None, None] * kv_state + jnp.einsum(
        "shd,she->hde", key_f, value_blk.astype(jnp.float32), precision=lax.Precision.HIGHEST
    )
    return (kv_state, intra_out + inter_out)


def shards_base(
    lin_query, lin_key, lin_value, log_decay, stream, out_weight, norm_gain, query_weight, kv_weight
):
    tok_rows = lin_query.shape[0]
    heads_here = log_decay.shape[1]
    head_width = heads_here * DH
    nblocks = tok_rows // BLOCK
    block_shape = (nblocks, BLOCK, heads_here, DH)
    inputs = (
        lin_query.reshape(block_shape),
        lin_key.reshape(block_shape),
        lin_value.reshape(block_shape),
        log_decay.reshape(nblocks, BLOCK, heads_here),
    )
    start_state = jnp.zeros((heads_here, DH, DH), jnp.float32)
    local_state, local_out = lax.scan(lightning_block, start_state, inputs)
    local_out = local_out.reshape(tok_rows, heads_here, DH)
    decay_total = jnp.sum(log_decay, axis=0)
    totals, states = (
        lax.all_gather(decay_total[None].astype(jnp.bfloat16), "seq", axis=0, tiled=True).astype(
            jnp.float32
        ),
        lax.all_gather(local_state[None].astype(jnp.bfloat16), "seq", axis=0, tiled=True).astype(
            jnp.float32
        ),
    )
    position = lax.axis_index("seq")
    device_order = jnp.arange(totals.shape[0])
    earlier = (device_order < position)[:, None]
    before = jnp.sum(jnp.where(earlier, totals, 0.0), axis=0)
    inclusive = jnp.cumsum(totals, axis=0)
    factors = jnp.where(earlier, jnp.exp(jnp.where(earlier, before[None, :] - inclusive, 0.0)), 0.0)
    incoming = jnp.einsum("jh,jhde->hde", factors, states, precision=lax.Precision.HIGHEST)
    running = jnp.cumsum(log_decay, axis=0)
    query_f = (
        lin_query.reshape(tok_rows, heads_here, DH).astype(jnp.float32)
        * jnp.exp(running)[:, :, None]
    )
    carried = jnp.einsum("thd,hde->the", query_f, incoming, precision=lax.Precision.HIGHEST)
    lin_raw = local_out + carried
    lin_out = (
        (lin_raw * lax.rsqrt(jnp.mean(lin_raw * lin_raw, axis=-1, keepdims=True) + 1e-06))
        .astype(jnp.bfloat16)
        .reshape(tok_rows, head_width)
    )
    branch = jnp.dot(
        lin_out,
        lax.all_gather(out_weight, "seq", axis=1, tiled=True),
        preferred_element_type=jnp.float32,
    )
    kv_group = lax.axis_index("heads") * heads_here // (QUERY_HEADS // KVH)
    kv_mine = lax.dynamic_index_in_dim(kv_weight, kv_group, 0, keepdims=False)
    query_rows, kv_rows = (
        lax.all_gather(query_weight, "seq", axis=0, tiled=True),
        lax.all_gather(kv_mine, "seq", axis=0, tiled=True),
    )
    projection = jnp.concatenate([query_rows, kv_rows], axis=1)
    own_sum = lax.psum_scatter(
        branch.astype(jnp.bfloat16), "heads", scatter_dimension=1, tiled=True
    ).astype(jnp.float32)
    mixed_sum = stream.astype(jnp.float32) + own_sum
    stream_next = mixed_sum.astype(jnp.bfloat16)
    total_sq = lax.psum(jnp.sum(mixed_sum * mixed_sum, axis=1), "heads")
    normed = (
        mixed_sum
        * lax.rsqrt(total_sq / D + 1e-05)[:, None]
        * norm_gain.astype(jnp.float32)[None, :]
    ).astype(jnp.bfloat16)
    projected = jnp.dot(
        lax.all_gather(normed, "heads", axis=1, tiled=True),
        projection,
        preferred_element_type=jnp.float32,
    )
    projected = projected.astype(jnp.bfloat16)
    queries = projected[:, :head_width].reshape(tok_rows, heads_here, DH)
    keys_values = projected[:, head_width:]
    position = lax.axis_index("seq")
    query_pos = position * tok_rows + jnp.arange(tok_rows)
    score_scale = float(DH) ** (-0.5)

    def attend(state_in, kv_block, key_start):
        old_max, row_total, weighted = state_in
        key_count = kv_block.shape[0]
        key_part = kv_block[:, :DH]
        value_part = kv_block[:, DH:]
        scores = (
            jnp.einsum("thd,sd->hts", queries, key_part, preferred_element_type=jnp.float32)
            * score_scale
        )
        key_pos = key_start + jnp.arange(key_count)
        allowed = ((key_pos[None, :] <= query_pos[:, None]) & (key_pos[None, :] >= 0))[None, :, :]
        scores = jnp.where(allowed, scores, -1e30)
        new_max = jnp.maximum(old_max, jnp.max(scores, axis=-1))
        expos = jnp.where(allowed, jnp.exp(scores - new_max[:, :, None]), 0.0)
        rescale = jnp.exp(old_max - new_max)
        row_total = row_total * rescale + jnp.sum(expos, axis=-1)
        prob_bf16 = expos.astype(jnp.bfloat16)
        weighted = weighted * rescale[:, :, None] + jnp.einsum(
            "hts,sd->htd", prob_bf16, value_part, preferred_element_type=jnp.float32
        )
        return (new_max, row_total, weighted)

    initial = (
        jnp.full((heads_here, tok_rows), -1e30, jnp.float32),
        jnp.zeros((heads_here, tok_rows), jnp.float32),
        jnp.zeros((heads_here, tok_rows, DH), jnp.float32),
    )
    first_state = attend(initial, keys_values, position * tok_rows)
    seq_count = lax.axis_size("seq")

    def cycle_turn(turn_index, loop_state):
        moving, inner_state = loop_state
        moving = from_behind(moving, "seq", 1)
        source = position - turn_index
        return (moving, attend(inner_state, moving, source * tok_rows))

    _, final_state = lax.fori_loop(1, seq_count, cycle_turn, (keys_values, first_state))
    _, row_total, weighted = final_state
    attended = (
        jnp.transpose(weighted / row_total[:, :, None], (1, 0, 2))
        .reshape(tok_rows, head_width)
        .astype(jnp.bfloat16)
    )
    return (stream_next, attended)


def lightning_local(lin_query, lin_key, lin_value, log_decay):
    tok_rows = lin_query.shape[0]
    heads_here = log_decay.shape[1]
    nblocks = tok_rows // BLOCK
    shape4 = (tok_rows, heads_here, DH)
    q4, k4, v4 = (x.reshape(shape4) for x in (lin_query, lin_key, lin_value))
    state = jnp.zeros((heads_here, DH, DH), jnp.float32)
    outs = []
    for blk in range(nblocks):
        rows = slice(blk * BLOCK, (blk + 1) * BLOCK)
        state, out = lightning_block(state, (q4[rows], k4[rows], v4[rows], log_decay[rows]))
        outs.append(out)
    local_out = jnp.concatenate(outs, axis=0)
    decay_total = jnp.sum(log_decay, axis=0)
    totals = lax.all_gather(decay_total[None].astype(jnp.bfloat16), "seq", axis=0, tiled=True)
    states = lax.all_gather(state[None].astype(jnp.bfloat16), "seq", axis=0, tiled=True)
    totals = totals.astype(jnp.float32)
    states = states.astype(jnp.float32)
    position = lax.axis_index("seq")
    device_order = jnp.arange(totals.shape[0])
    earlier = (device_order < position)[:, None]
    before = jnp.sum(jnp.where(earlier, totals, 0.0), axis=0)
    inclusive = jnp.cumsum(totals, axis=0)
    factors = jnp.where(earlier, jnp.exp(jnp.where(earlier, before[None, :] - inclusive, 0.0)), 0.0)
    incoming = jnp.einsum("jh,jhde->hde", factors, states, precision=lax.Precision.HIGHEST)
    running = jnp.cumsum(log_decay, axis=0)
    query_f = q4.astype(jnp.float32) * jnp.exp(running)[:, :, None]
    carried = jnp.einsum("thd,hde->the", query_f, incoming, precision=lax.Precision.HIGHEST)
    lin_raw = local_out + carried
    lin_out = (
        (lin_raw * lax.rsqrt(jnp.mean(lin_raw * lin_raw, axis=-1, keepdims=True) + 1e-06))
        .astype(jnp.bfloat16)
        .reshape(tok_rows, heads_here * DH)
    )
    return lin_out


def attend_block(queries, query_pos, state_in, kv_block, key_start):
    old_max, row_total, weighted = state_in
    key_count = kv_block.shape[0]
    key_part = kv_block[:, :DH]
    value_part = kv_block[:, DH:]
    score_scale = float(DH) ** (-0.5)
    scores = (
        jnp.einsum("thd,sd->hts", queries, key_part, preferred_element_type=jnp.float32)
        * score_scale
    )
    key_pos = key_start + jnp.arange(key_count)
    allowed = (key_pos[None, :] <= query_pos[:, None])[None, :, :]
    scores = jnp.where(allowed, scores, -1e30)
    new_max = jnp.maximum(old_max, jnp.max(scores, axis=-1))
    expos = jnp.where(allowed, jnp.exp(scores - new_max[:, :, None]), 0.0)
    rescale = jnp.exp(old_max - new_max)
    row_total = row_total * rescale + jnp.sum(expos, axis=-1)
    prob_bf16 = expos.astype(jnp.bfloat16)
    weighted = weighted * rescale[:, :, None] + jnp.einsum(
        "hts,sd->htd", prob_bf16, value_part, preferred_element_type=jnp.float32
    )
    return (new_max, row_total, weighted)


def shards_fast(
    lin_query, lin_key, lin_value, log_decay, stream, out_weight, norm_gain, query_weight, kv_weight
):
    n_heads = lax.axis_size("heads")
    n_seq = lax.axis_size("seq")
    tok_rows = lin_query.shape[0]
    heads_here = log_decay.shape[1]
    head_width = heads_here * DH
    mine_a = lax.axis_index("heads")
    mine_b = lax.axis_index("seq")
    swap = [(x * n_seq + y, y * n_seq + x) for x in range(n_heads) for y in range(n_seq)]
    stream_t = lax.ppermute(stream, ("heads", "seq"), swap)

    lin_out = lightning_local(lin_query, lin_key, lin_value, log_decay)
    lin_all = lax.all_gather(lin_out, "seq", axis=0, tiled=True)
    part = jnp.dot(lin_all, out_weight, preferred_element_type=jnp.float32).astype(jnp.bfloat16)
    own_sum = lax.psum_scatter(part, "heads", scatter_dimension=0, tiled=True)
    mixed_sum = stream_t.astype(jnp.float32) + own_sum.astype(jnp.float32)
    stream_next = lax.ppermute(mixed_sum.astype(jnp.bfloat16), ("heads", "seq"), swap)
    total_sq = lax.psum(jnp.sum(mixed_sum * mixed_sum, axis=1), "seq")
    cols = mixed_sum.shape[1]
    gain_all = lax.all_gather(norm_gain, "heads", axis=0, tiled=True)
    gain_b = lax.dynamic_slice_in_dim(gain_all, mine_b * cols, cols)
    normed = (
        mixed_sum
        * lax.rsqrt(total_sq / D + 1e-05)[:, None]
        * gain_b.astype(jnp.float32)[None, :]
    ).astype(jnp.bfloat16)
    normed_all = lax.all_gather(normed, "heads", axis=0, tiled=True)
    kv_group = mine_a * heads_here // (QUERY_HEADS // KVH)
    kv_mine = lax.dynamic_index_in_dim(kv_weight, kv_group, 0, keepdims=False)
    projection = jnp.concatenate([query_weight, kv_mine], axis=1)
    part2 = jnp.dot(normed_all, projection, preferred_element_type=jnp.float32).astype(
        jnp.bfloat16
    )
    queries = lax.psum_scatter(part2[:, :head_width], "seq", scatter_dimension=0, tiled=True)
    keys_values = lax.psum(part2[:, head_width:], "seq")
    queries = queries.reshape(tok_rows, heads_here, DH)
    query_pos = mine_b * tok_rows + jnp.arange(tok_rows)
    state = (
        jnp.full((heads_here, tok_rows), -1e30, jnp.float32),
        jnp.zeros((heads_here, tok_rows), jnp.float32),
        jnp.zeros((heads_here, tok_rows, DH), jnp.float32),
    )
    for blk in range(n_seq):
        kv_block = keys_values[blk * tok_rows : (blk + 1) * tok_rows]
        state = attend_block(queries, query_pos, state, kv_block, blk * tok_rows)
    _, row_total, weighted = state
    attended = (
        jnp.transpose(weighted / row_total[:, :, None], (1, 0, 2))
        .reshape(tok_rows, head_width)
        .astype(jnp.bfloat16)
    )
    return (stream_next, attended)


def solution(mesh):
    n_heads = mesh.shape["heads"]
    n_seq = mesh.shape["seq"]
    fast_ok = n_heads == n_seq and QUERY_HEADS % n_heads == 0
    if fast_ok:
        heads_here = QUERY_HEADS // n_heads
        fast_ok = (QUERY_HEADS // KVH) % heads_here == 0 and D % n_seq == 0
    shards = shards_fast if fast_ok else shards_base

    return jax.shard_map(
        shards,
        mesh=mesh,
        in_specs=(
            P(("groups", "seq"), "heads"),
            P(("groups", "seq"), "heads"),
            P(("groups", "seq"), "heads"),
            P(("groups", "seq"), "heads"),
            P(("groups", "seq"), "heads"),
            P("heads", "seq"),
            P("heads"),
            P("seq", "heads"),
            P(None, "seq", None),
        ),
        out_specs=(P(("groups", "seq"), "heads"), P(("groups", "seq"), "heads")),
        check_vma=False,
    )
```

```python
import jax
import jax.numpy as jnp
from jax import lax
from jax.sharding import PartitionSpec as P

D = 6144
QUERY_HEADS = 32
KVH = 4
DH = 128
BLOCK = 256


def from_behind(value, axis, steps):
    count = lax.axis_size(axis)
    leading, last = (max(0, -steps), min(count, count - steps))
    return lax.ppermute(value, axis, [(source, source + steps) for source in range(leading, last)])


def lightning_block(kv_state, block_inputs):
    query_blk, key_blk, value_blk, decay_blk = block_inputs
    block_len = query_blk.shape[0]
    local_cum = jnp.cumsum(decay_blk, axis=0)
    causal_mask = (jnp.arange(block_len)[:, None] >= jnp.arange(block_len)[None, :])[:, :, None]
    decay_diff = local_cum[:, None, :] - local_cum[None, :, :]
    decays = jnp.where(causal_mask, jnp.exp(jnp.where(causal_mask, decay_diff, 0.0)), 0.0)
    scores = jnp.einsum("thd,shd->hts", query_blk, key_blk, preferred_element_type=jnp.float32)
    weights = (scores * jnp.transpose(decays, (2, 0, 1))).astype(jnp.bfloat16)
    intra_out = jnp.einsum("hts,shd->thd", weights, value_blk, preferred_element_type=jnp.float32)
    query_f = query_blk.astype(jnp.float32)
    inter_out = jnp.einsum(
        "thd,hde->the",
        query_f * jnp.exp(local_cum)[:, :, None],
        kv_state,
        precision=lax.Precision.HIGHEST,
    )
    tail_decay = jnp.exp(local_cum[-1][None, :] - local_cum)
    key_f = key_blk.astype(jnp.float32) * tail_decay[:, :, None]
    kv_state = jnp.exp(local_cum[-1])[:, None, None] * kv_state + jnp.einsum(
        "shd,she->hde", key_f, value_blk.astype(jnp.float32), precision=lax.Precision.HIGHEST
    )
    return (kv_state, intra_out + inter_out)


def shards_base(
    lin_query, lin_key, lin_value, log_decay, stream, out_weight, norm_gain, query_weight, kv_weight
):
    tok_rows = lin_query.shape[0]
    heads_here = log_decay.shape[1]
    head_width = heads_here * DH
    nblocks = tok_rows // BLOCK
    block_shape = (nblocks, BLOCK, heads_here, DH)
    inputs = (
        lin_query.reshape(block_shape),
        lin_key.reshape(block_shape),
        lin_value.reshape(block_shape),
        log_decay.reshape(nblocks, BLOCK, heads_here),
    )
    start_state = jnp.zeros((heads_here, DH, DH), jnp.float32)
    local_state, local_out = lax.scan(lightning_block, start_state, inputs)
    local_out = local_out.reshape(tok_rows, heads_here, DH)
    decay_total = jnp.sum(log_decay, axis=0)
    totals, states = (
        lax.all_gather(decay_total[None].astype(jnp.bfloat16), "seq", axis=0, tiled=True).astype(
            jnp.float32
        ),
        lax.all_gather(local_state[None].astype(jnp.bfloat16), "seq", axis=0, tiled=True).astype(
            jnp.float32
        ),
    )
    position = lax.axis_index("seq")
    device_order = jnp.arange(totals.shape[0])
    earlier = (device_order < position)[:, None]
    before = jnp.sum(jnp.where(earlier, totals, 0.0), axis=0)
    inclusive = jnp.cumsum(totals, axis=0)
    factors = jnp.where(earlier, jnp.exp(jnp.where(earlier, before[None, :] - inclusive, 0.0)), 0.0)
    incoming = jnp.einsum("jh,jhde->hde", factors, states, precision=lax.Precision.HIGHEST)
    running = jnp.cumsum(log_decay, axis=0)
    query_f = (
        lin_query.reshape(tok_rows, heads_here, DH).astype(jnp.float32)
        * jnp.exp(running)[:, :, None]
    )
    carried = jnp.einsum("thd,hde->the", query_f, incoming, precision=lax.Precision.HIGHEST)
    lin_raw = local_out + carried
    lin_out = (
        (lin_raw * lax.rsqrt(jnp.mean(lin_raw * lin_raw, axis=-1, keepdims=True) + 1e-06))
        .astype(jnp.bfloat16)
        .reshape(tok_rows, head_width)
    )
    branch = jnp.dot(
        lin_out,
        lax.all_gather(out_weight, "seq", axis=1, tiled=True),
        preferred_element_type=jnp.float32,
    )
    kv_group = lax.axis_index("heads") * heads_here // (QUERY_HEADS // KVH)
    kv_mine = lax.dynamic_index_in_dim(kv_weight, kv_group, 0, keepdims=False)
    query_rows, kv_rows = (
        lax.all_gather(query_weight, "seq", axis=0, tiled=True),
        lax.all_gather(kv_mine, "seq", axis=0, tiled=True),
    )
    projection = jnp.concatenate([query_rows, kv_rows], axis=1)
    own_sum = lax.psum_scatter(
        branch.astype(jnp.bfloat16), "heads", scatter_dimension=1, tiled=True
    ).astype(jnp.float32)
    mixed_sum = stream.astype(jnp.float32) + own_sum
    stream_next = mixed_sum.astype(jnp.bfloat16)
    total_sq = lax.psum(jnp.sum(mixed_sum * mixed_sum, axis=1), "heads")
    normed = (
        mixed_sum
        * lax.rsqrt(total_sq / D + 1e-05)[:, None]
        * norm_gain.astype(jnp.float32)[None, :]
    ).astype(jnp.bfloat16)
    projected = jnp.dot(
        lax.all_gather(normed, "heads", axis=1, tiled=True),
        projection,
        preferred_element_type=jnp.float32,
    )
    projected = projected.astype(jnp.bfloat16)
    queries = projected[:, :head_width].reshape(tok_rows, heads_here, DH)
    keys_values = projected[:, head_width:]
    position = lax.axis_index("seq")
    query_pos = position * tok_rows + jnp.arange(tok_rows)
    score_scale = float(DH) ** (-0.5)

    def attend(state_in, kv_block, key_start):
        old_max, row_total, weighted = state_in
        key_count = kv_block.shape[0]
        key_part = kv_block[:, :DH]
        value_part = kv_block[:, DH:]
        scores = (
            jnp.einsum("thd,sd->hts", queries, key_part, preferred_element_type=jnp.float32)
            * score_scale
        )
        key_pos = key_start + jnp.arange(key_count)
        allowed = ((key_pos[None, :] <= query_pos[:, None]) & (key_pos[None, :] >= 0))[None, :, :]
        scores = jnp.where(allowed, scores, -1e30)
        new_max = jnp.maximum(old_max, jnp.max(scores, axis=-1))
        expos = jnp.where(allowed, jnp.exp(scores - new_max[:, :, None]), 0.0)
        rescale = jnp.exp(old_max - new_max)
        row_total = row_total * rescale + jnp.sum(expos, axis=-1)
        prob_bf16 = expos.astype(jnp.bfloat16)
        weighted = weighted * rescale[:, :, None] + jnp.einsum(
            "hts,sd->htd", prob_bf16, value_part, preferred_element_type=jnp.float32
        )
        return (new_max, row_total, weighted)

    initial = (
        jnp.full((heads_here, tok_rows), -1e30, jnp.float32),
        jnp.zeros((heads_here, tok_rows), jnp.float32),
        jnp.zeros((heads_here, tok_rows, DH), jnp.float32),
    )
    first_state = attend(initial, keys_values, position * tok_rows)
    seq_count = lax.axis_size("seq")

    def cycle_turn(turn_index, loop_state):
        moving, inner_state = loop_state
        moving = from_behind(moving, "seq", 1)
        source = position - turn_index
        return (moving, attend(inner_state, moving, source * tok_rows))

    _, final_state = lax.fori_loop(1, seq_count, cycle_turn, (keys_values, first_state))
    _, row_total, weighted = final_state
    attended = (
        jnp.transpose(weighted / row_total[:, :, None], (1, 0, 2))
        .reshape(tok_rows, head_width)
        .astype(jnp.bfloat16)
    )
    return (stream_next, attended)


def lightning_local(lin_query, lin_key, lin_value, log_decay):
    tok_rows = lin_query.shape[0]
    heads_here = log_decay.shape[1]
    nblocks = tok_rows // BLOCK
    shape4 = (tok_rows, heads_here, DH)
    q4, k4, v4 = (x.reshape(shape4) for x in (lin_query, lin_key, lin_value))
    state = jnp.zeros((heads_here, DH, DH), jnp.float32)
    outs = []
    for blk in range(nblocks):
        rows = slice(blk * BLOCK, (blk + 1) * BLOCK)
        state, out = lightning_block(state, (q4[rows], k4[rows], v4[rows], log_decay[rows]))
        outs.append(out)
    local_out = jnp.concatenate(outs, axis=0)
    decay_total = jnp.sum(log_decay, axis=0)
    packed = jnp.concatenate([state.reshape(-1), decay_total]).astype(jnp.bfloat16)
    gathered = lax.all_gather(packed, "seq", axis=0, tiled=False).astype(jnp.float32)
    state_size = state.size
    states = gathered[:, :state_size].reshape((-1,) + state.shape)
    totals = gathered[:, state_size:]
    position = lax.axis_index("seq")
    device_order = jnp.arange(totals.shape[0])
    earlier = (device_order < position)[:, None]
    before = jnp.sum(jnp.where(earlier, totals, 0.0), axis=0)
    inclusive = jnp.cumsum(totals, axis=0)
    factors = jnp.where(earlier, jnp.exp(jnp.where(earlier, before[None, :] - inclusive, 0.0)), 0.0)
    incoming = jnp.einsum("jh,jhde->hde", factors, states, precision=lax.Precision.HIGHEST)
    running = jnp.cumsum(log_decay, axis=0)
    query_f = q4.astype(jnp.float32) * jnp.exp(running)[:, :, None]
    carried = jnp.einsum("thd,hde->the", query_f, incoming, precision=lax.Precision.HIGHEST)
    lin_raw = local_out + carried
    lin_out = (
        (lin_raw * lax.rsqrt(jnp.mean(lin_raw * lin_raw, axis=-1, keepdims=True) + 1e-06))
        .astype(jnp.bfloat16)
        .reshape(tok_rows, heads_here * DH)
    )
    return lin_out


def attend_block(queries, query_pos, state_in, kv_block, key_start):
    old_max, row_total, weighted = state_in
    key_count = kv_block.shape[0]
    key_part = kv_block[:, :DH]
    value_part = kv_block[:, DH:]
    score_scale = float(DH) ** (-0.5)
    scores = (
        jnp.einsum("thd,sd->hts", queries, key_part, preferred_element_type=jnp.float32)
        * score_scale
    )
    key_pos = key_start + jnp.arange(key_count)
    allowed = ((key_pos[None, :] <= query_pos[:, None]) & (key_pos[None, :] >= 0))[None, :, :]
    scores = jnp.where(allowed, scores, -1e30)
    new_max = jnp.maximum(old_max, jnp.max(scores, axis=-1))
    expos = jnp.where(allowed, jnp.exp(scores - new_max[:, :, None]), 0.0)
    rescale = jnp.exp(old_max - new_max)
    row_total = row_total * rescale + jnp.sum(expos, axis=-1)
    prob_bf16 = expos.astype(jnp.bfloat16)
    weighted = weighted * rescale[:, :, None] + jnp.einsum(
        "hts,sd->htd", prob_bf16, value_part, preferred_element_type=jnp.float32
    )
    return (new_max, row_total, weighted)


def shards_fast(
    lin_query, lin_key, lin_value, log_decay, stream, out_weight, norm_gain, query_weight, kv_weight
):
    n_heads = lax.axis_size("heads")
    n_seq = lax.axis_size("seq")
    tok_rows = lin_query.shape[0]
    heads_here = log_decay.shape[1]
    head_width = heads_here * DH
    mine_a = lax.axis_index("heads")
    mine_b = lax.axis_index("seq")
    swap = [(x * n_seq + y, y * n_seq + x) for x in range(n_heads) for y in range(n_seq)]
    stream_t = lax.ppermute(stream, ("heads", "seq"), swap)

    lin_out = lightning_local(lin_query, lin_key, lin_value, log_decay)
    lin_all = lax.all_gather(lin_out, "seq", axis=0, tiled=True)
    part = jnp.dot(lin_all, out_weight, preferred_element_type=jnp.float32).astype(jnp.bfloat16)
    own_sum = lax.psum_scatter(part, "heads", scatter_dimension=0, tiled=True)
    mixed_sum = stream_t.astype(jnp.float32) + own_sum.astype(jnp.float32)
    stream_next = lax.ppermute(mixed_sum.astype(jnp.bfloat16), ("heads", "seq"), swap)
    total_sq = lax.psum(jnp.sum(mixed_sum * mixed_sum, axis=1), "seq")
    cols = mixed_sum.shape[1]
    gain_all = lax.all_gather(norm_gain, "heads", axis=0, tiled=True)
    gain_b = lax.dynamic_slice_in_dim(gain_all, mine_b * cols, cols)
    normed = (
        mixed_sum
        * lax.rsqrt(total_sq / D + 1e-05)[:, None]
        * gain_b.astype(jnp.float32)[None, :]
    ).astype(jnp.bfloat16)
    normed_all = lax.all_gather(normed, "heads", axis=0, tiled=True)
    kv_group = mine_a * heads_here // (QUERY_HEADS // KVH)
    kv_mine = lax.dynamic_index_in_dim(kv_weight, kv_group, 0, keepdims=False)
    projection = jnp.concatenate([query_weight, kv_mine], axis=1)
    part2 = jnp.dot(normed_all, projection, preferred_element_type=jnp.float32).astype(
        jnp.bfloat16
    )
    reduced = lax.psum_scatter(part2, "seq", scatter_dimension=0, tiled=True)
    queries = reduced[:, :head_width].reshape(tok_rows, heads_here, DH)
    kv_own = reduced[:, head_width:]
    query_pos = mine_b * tok_rows + jnp.arange(tok_rows)
    state = (
        jnp.full((heads_here, tok_rows), -1e30, jnp.float32),
        jnp.zeros((heads_here, tok_rows), jnp.float32),
        jnp.zeros((heads_here, tok_rows, DH), jnp.float32),
    )
    earlier_kv = [from_behind(kv_own, "seq", dist) for dist in range(1, n_seq)]
    state = attend_block(queries, query_pos, state, kv_own, mine_b * tok_rows)
    for dist in range(1, n_seq):
        key_start = (mine_b - dist) * tok_rows
        state = attend_block(queries, query_pos, state, earlier_kv[dist - 1], key_start)
    _, row_total, weighted = state
    attended = (
        jnp.transpose(weighted / row_total[:, :, None], (1, 0, 2))
        .reshape(tok_rows, head_width)
        .astype(jnp.bfloat16)
    )
    return (stream_next, attended)


def solution(mesh):
    n_heads = mesh.shape["heads"]
    n_seq = mesh.shape["seq"]
    fast_ok = n_heads == n_seq and QUERY_HEADS % n_heads == 0
    if fast_ok:
        heads_here = QUERY_HEADS // n_heads
        fast_ok = (QUERY_HEADS // KVH) % heads_here == 0 and D % n_seq == 0
    shards = shards_fast if fast_ok else shards_base

    return jax.shard_map(
        shards,
        mesh=mesh,
        in_specs=(
            P(("groups", "seq"), "heads"),
            P(("groups", "seq"), "heads"),
            P(("groups", "seq"), "heads"),
            P(("groups", "seq"), "heads"),
            P(("groups", "seq"), "heads"),
            P("heads", "seq"),
            P("heads"),
            P("seq", "heads"),
            P(None, "seq", None),
        ),
        out_specs=(P(("groups", "seq"), "heads"), P(("groups", "seq"), "heads")),
        check_vma=False,
    )
```

```python
import jax
import jax.numpy as jnp
from jax import lax
from jax.sharding import PartitionSpec as P

D = 6144
QUERY_HEADS = 32
KVH = 4
DH = 128
BLOCK = 256


def from_behind(value, axis, steps):
    count = lax.axis_size(axis)
    leading, last = (max(0, -steps), min(count, count - steps))
    return lax.ppermute(value, axis, [(source, source + steps) for source in range(leading, last)])


def lightning_block(kv_state, block_inputs):
    query_blk, key_blk, value_blk, decay_blk = block_inputs
    block_len = query_blk.shape[0]
    local_cum = jnp.cumsum(decay_blk, axis=0)
    causal_mask = (jnp.arange(block_len)[:, None] >= jnp.arange(block_len)[None, :])[:, :, None]
    decay_diff = local_cum[:, None, :] - local_cum[None, :, :]
    decays = jnp.where(causal_mask, jnp.exp(jnp.where(causal_mask, decay_diff, 0.0)), 0.0)
    scores = jnp.einsum("thd,shd->hts", query_blk, key_blk, preferred_element_type=jnp.float32)
    weights = (scores * jnp.transpose(decays, (2, 0, 1))).astype(jnp.bfloat16)
    intra_out = jnp.einsum("hts,shd->thd", weights, value_blk, preferred_element_type=jnp.float32)
    query_f = query_blk.astype(jnp.float32)
    inter_out = jnp.einsum(
        "thd,hde->the",
        query_f * jnp.exp(local_cum)[:, :, None],
        kv_state,
        precision=lax.Precision.HIGHEST,
    )
    tail_decay = jnp.exp(local_cum[-1][None, :] - local_cum)
    key_f = key_blk.astype(jnp.float32) * tail_decay[:, :, None]
    kv_state = jnp.exp(local_cum[-1])[:, None, None] * kv_state + jnp.einsum(
        "shd,she->hde", key_f, value_blk.astype(jnp.float32), precision=lax.Precision.HIGHEST
    )
    return (kv_state, intra_out + inter_out)


def shards_base(
    lin_query, lin_key, lin_value, log_decay, stream, out_weight, norm_gain, query_weight, kv_weight
):
    tok_rows = lin_query.shape[0]
    heads_here = log_decay.shape[1]
    head_width = heads_here * DH
    nblocks = tok_rows // BLOCK
    block_shape = (nblocks, BLOCK, heads_here, DH)
    inputs = (
        lin_query.reshape(block_shape),
        lin_key.reshape(block_shape),
        lin_value.reshape(block_shape),
        log_decay.reshape(nblocks, BLOCK, heads_here),
    )
    start_state = jnp.zeros((heads_here, DH, DH), jnp.float32)
    local_state, local_out = lax.scan(lightning_block, start_state, inputs)
    local_out = local_out.reshape(tok_rows, heads_here, DH)
    decay_total = jnp.sum(log_decay, axis=0)
    totals, states = (
        lax.all_gather(decay_total[None].astype(jnp.bfloat16), "seq", axis=0, tiled=True).astype(
            jnp.float32
        ),
        lax.all_gather(local_state[None].astype(jnp.bfloat16), "seq", axis=0, tiled=True).astype(
            jnp.float32
        ),
    )
    position = lax.axis_index("seq")
    device_order = jnp.arange(totals.shape[0])
    earlier = (device_order < position)[:, None]
    before = jnp.sum(jnp.where(earlier, totals, 0.0), axis=0)
    inclusive = jnp.cumsum(totals, axis=0)
    factors = jnp.where(earlier, jnp.exp(jnp.where(earlier, before[None, :] - inclusive, 0.0)), 0.0)
    incoming = jnp.einsum("jh,jhde->hde", factors, states, precision=lax.Precision.HIGHEST)
    running = jnp.cumsum(log_decay, axis=0)
    query_f = (
        lin_query.reshape(tok_rows, heads_here, DH).astype(jnp.float32)
        * jnp.exp(running)[:, :, None]
    )
    carried = jnp.einsum("thd,hde->the", query_f, incoming, precision=lax.Precision.HIGHEST)
    lin_raw = local_out + carried
    lin_out = (
        (lin_raw * lax.rsqrt(jnp.mean(lin_raw * lin_raw, axis=-1, keepdims=True) + 1e-06))
        .astype(jnp.bfloat16)
        .reshape(tok_rows, head_width)
    )
    branch = jnp.dot(
        lin_out,
        lax.all_gather(out_weight, "seq", axis=1, tiled=True),
        preferred_element_type=jnp.float32,
    )
    kv_group = lax.axis_index("heads") * heads_here // (QUERY_HEADS // KVH)
    kv_mine = lax.dynamic_index_in_dim(kv_weight, kv_group, 0, keepdims=False)
    query_rows, kv_rows = (
        lax.all_gather(query_weight, "seq", axis=0, tiled=True),
        lax.all_gather(kv_mine, "seq", axis=0, tiled=True),
    )
    projection = jnp.concatenate([query_rows, kv_rows], axis=1)
    own_sum = lax.psum_scatter(
        branch.astype(jnp.bfloat16), "heads", scatter_dimension=1, tiled=True
    ).astype(jnp.float32)
    mixed_sum = stream.astype(jnp.float32) + own_sum
    stream_next = mixed_sum.astype(jnp.bfloat16)
    total_sq = lax.psum(jnp.sum(mixed_sum * mixed_sum, axis=1), "heads")
    normed = (
        mixed_sum
        * lax.rsqrt(total_sq / D + 1e-05)[:, None]
        * norm_gain.astype(jnp.float32)[None, :]
    ).astype(jnp.bfloat16)
    projected = jnp.dot(
        lax.all_gather(normed, "heads", axis=1, tiled=True),
        projection,
        preferred_element_type=jnp.float32,
    )
    projected = projected.astype(jnp.bfloat16)
    queries = projected[:, :head_width].reshape(tok_rows, heads_here, DH)
    keys_values = projected[:, head_width:]
    position = lax.axis_index("seq")
    query_pos = position * tok_rows + jnp.arange(tok_rows)
    score_scale = float(DH) ** (-0.5)

    def attend(state_in, kv_block, key_start):
        old_max, row_total, weighted = state_in
        key_count = kv_block.shape[0]
        key_part = kv_block[:, :DH]
        value_part = kv_block[:, DH:]
        scores = (
            jnp.einsum("thd,sd->hts", queries, key_part, preferred_element_type=jnp.float32)
            * score_scale
        )
        key_pos = key_start + jnp.arange(key_count)
        allowed = ((key_pos[None, :] <= query_pos[:, None]) & (key_pos[None, :] >= 0))[None, :, :]
        scores = jnp.where(allowed, scores, -1e30)
        new_max = jnp.maximum(old_max, jnp.max(scores, axis=-1))
        expos = jnp.where(allowed, jnp.exp(scores - new_max[:, :, None]), 0.0)
        rescale = jnp.exp(old_max - new_max)
        row_total = row_total * rescale + jnp.sum(expos, axis=-1)
        prob_bf16 = expos.astype(jnp.bfloat16)
        weighted = weighted * rescale[:, :, None] + jnp.einsum(
            "hts,sd->htd", prob_bf16, value_part, preferred_element_type=jnp.float32
        )
        return (new_max, row_total, weighted)

    initial = (
        jnp.full((heads_here, tok_rows), -1e30, jnp.float32),
        jnp.zeros((heads_here, tok_rows), jnp.float32),
        jnp.zeros((heads_here, tok_rows, DH), jnp.float32),
    )
    first_state = attend(initial, keys_values, position * tok_rows)
    seq_count = lax.axis_size("seq")

    def cycle_turn(turn_index, loop_state):
        moving, inner_state = loop_state
        moving = from_behind(moving, "seq", 1)
        source = position - turn_index
        return (moving, attend(inner_state, moving, source * tok_rows))

    _, final_state = lax.fori_loop(1, seq_count, cycle_turn, (keys_values, first_state))
    _, row_total, weighted = final_state
    attended = (
        jnp.transpose(weighted / row_total[:, :, None], (1, 0, 2))
        .reshape(tok_rows, head_width)
        .astype(jnp.bfloat16)
    )
    return (stream_next, attended)


def lightning_local(lin_query, lin_key, lin_value, log_decay):
    tok_rows = lin_query.shape[0]
    heads_here = log_decay.shape[1]
    nblocks = tok_rows // BLOCK
    shape4 = (tok_rows, heads_here, DH)
    q4, k4, v4 = (x.reshape(shape4) for x in (lin_query, lin_key, lin_value))
    state = jnp.zeros((heads_here, DH, DH), jnp.float32)
    outs = []
    for blk in range(nblocks):
        rows = slice(blk * BLOCK, (blk + 1) * BLOCK)
        state, out = lightning_block(state, (q4[rows], k4[rows], v4[rows], log_decay[rows]))
        outs.append(out)
    local_out = jnp.concatenate(outs, axis=0)
    decay_total = jnp.sum(log_decay, axis=0)
    totals = lax.all_gather(decay_total[None].astype(jnp.bfloat16), "seq", axis=0, tiled=True)
    states = lax.all_gather(state[None].astype(jnp.bfloat16), "seq", axis=0, tiled=True)
    totals = totals.astype(jnp.float32)
    states = states.astype(jnp.float32)
    position = lax.axis_index("seq")
    device_order = jnp.arange(totals.shape[0])
    earlier = (device_order < position)[:, None]
    before = jnp.sum(jnp.where(earlier, totals, 0.0), axis=0)
    inclusive = jnp.cumsum(totals, axis=0)
    factors = jnp.where(earlier, jnp.exp(jnp.where(earlier, before[None, :] - inclusive, 0.0)), 0.0)
    incoming = jnp.einsum("jh,jhde->hde", factors, states, precision=lax.Precision.HIGHEST)
    running = jnp.cumsum(log_decay, axis=0)
    query_f = q4.astype(jnp.float32) * jnp.exp(running)[:, :, None]
    carried = jnp.einsum("thd,hde->the", query_f, incoming, precision=lax.Precision.HIGHEST)
    lin_raw = local_out + carried
    lin_out = (
        (lin_raw * lax.rsqrt(jnp.mean(lin_raw * lin_raw, axis=-1, keepdims=True) + 1e-06))
        .astype(jnp.bfloat16)
        .reshape(tok_rows, heads_here * DH)
    )
    return lin_out


def attend_block(queries, query_pos, state_in, kv_block, key_start):
    old_max, row_total, weighted = state_in
    key_count = kv_block.shape[0]
    key_part = kv_block[:, :DH]
    value_part = kv_block[:, DH:]
    score_scale = float(DH) ** (-0.5)
    scores = (
        jnp.einsum("thd,sd->hts", queries, key_part, preferred_element_type=jnp.float32)
        * score_scale
    )
    key_pos = key_start + jnp.arange(key_count)
    allowed = ((key_pos[None, :] <= query_pos[:, None]) & (key_pos[None, :] >= 0))[None, :, :]
    scores = jnp.where(allowed, scores, -1e30)
    new_max = jnp.maximum(old_max, jnp.max(scores, axis=-1))
    expos = jnp.where(allowed, jnp.exp(scores - new_max[:, :, None]), 0.0)
    rescale = jnp.exp(old_max - new_max)
    row_total = row_total * rescale + jnp.sum(expos, axis=-1)
    prob_bf16 = expos.astype(jnp.bfloat16)
    weighted = weighted * rescale[:, :, None] + jnp.einsum(
        "hts,sd->htd", prob_bf16, value_part, preferred_element_type=jnp.float32
    )
    return (new_max, row_total, weighted)


def shards_fast(
    lin_query, lin_key, lin_value, log_decay, stream, out_weight, norm_gain, query_weight, kv_weight
):
    n_heads = lax.axis_size("heads")
    n_seq = lax.axis_size("seq")
    tok_rows = lin_query.shape[0]
    heads_here = log_decay.shape[1]
    head_width = heads_here * DH
    mine_a = lax.axis_index("heads")
    mine_b = lax.axis_index("seq")
    swap = [(x * n_seq + y, y * n_seq + x) for x in range(n_heads) for y in range(n_seq)]
    stream_t = lax.ppermute(stream, ("heads", "seq"), swap)

    lin_out = lightning_local(lin_query, lin_key, lin_value, log_decay)
    lin_all = lax.all_gather(lin_out, "seq", axis=0, tiled=True)
    part = jnp.dot(lin_all, out_weight, preferred_element_type=jnp.float32).astype(jnp.bfloat16)
    own_sum = lax.psum_scatter(part, "heads", scatter_dimension=0, tiled=True)
    mixed_sum = stream_t.astype(jnp.float32) + own_sum.astype(jnp.float32)
    stream_next = lax.ppermute(mixed_sum.astype(jnp.bfloat16), ("heads", "seq"), swap)
    total_sq = lax.psum(jnp.sum(mixed_sum * mixed_sum, axis=1), "seq")
    cols = mixed_sum.shape[1]
    gain_all = lax.all_gather(norm_gain, "heads", axis=0, tiled=True)
    gain_b = lax.dynamic_slice_in_dim(gain_all, mine_b * cols, cols)
    normed = (
        mixed_sum
        * lax.rsqrt(total_sq / D + 1e-05)[:, None]
        * gain_b.astype(jnp.float32)[None, :]
    ).astype(jnp.bfloat16)
    normed_all = lax.all_gather(normed, "heads", axis=0, tiled=True)
    kv_group = mine_a * heads_here // (QUERY_HEADS // KVH)
    kv_mine = lax.dynamic_index_in_dim(kv_weight, kv_group, 0, keepdims=False)
    q_part = jnp.dot(normed_all, query_weight, preferred_element_type=jnp.float32)
    kv_part = jnp.dot(normed_all, kv_mine, preferred_element_type=jnp.float32)
    queries = lax.psum_scatter(
        q_part.astype(jnp.bfloat16), "seq", scatter_dimension=0, tiled=True
    ).reshape(tok_rows, heads_here, DH)
    kv_own = lax.psum_scatter(kv_part.astype(jnp.bfloat16), "seq", scatter_dimension=0, tiled=True)
    query_pos = mine_b * tok_rows + jnp.arange(tok_rows)
    state = (
        jnp.full((heads_here, tok_rows), -1e30, jnp.float32),
        jnp.zeros((heads_here, tok_rows), jnp.float32),
        jnp.zeros((heads_here, tok_rows, DH), jnp.float32),
    )
    earlier_kv = [from_behind(kv_own, "seq", dist) for dist in range(1, n_seq)]
    state = attend_block(queries, query_pos, state, kv_own, mine_b * tok_rows)
    for dist in range(1, n_seq):
        key_start = (mine_b - dist) * tok_rows
        state = attend_block(queries, query_pos, state, earlier_kv[dist - 1], key_start)
    _, row_total, weighted = state
    attended = (
        jnp.transpose(weighted / row_total[:, :, None], (1, 0, 2))
        .reshape(tok_rows, head_width)
        .astype(jnp.bfloat16)
    )
    return (stream_next, attended)


def solution(mesh):
    n_heads = mesh.shape["heads"]
    n_seq = mesh.shape["seq"]
    fast_ok = n_heads == n_seq and QUERY_HEADS % n_heads == 0
    if fast_ok:
        heads_here = QUERY_HEADS // n_heads
        fast_ok = (QUERY_HEADS // KVH) % heads_here == 0 and D % n_seq == 0
    shards = shards_fast if fast_ok else shards_base

    return jax.shard_map(
        shards,
        mesh=mesh,
        in_specs=(
            P(("groups", "seq"), "heads"),
            P(("groups", "seq"), "heads"),
            P(("groups", "seq"), "heads"),
            P(("groups", "seq"), "heads"),
            P(("groups", "seq"), "heads"),
            P("heads", "seq"),
            P("heads"),
            P("seq", "heads"),
            P(None, "seq", None),
        ),
        out_specs=(P(("groups", "seq"), "heads"), P(("groups", "seq"), "heads")),
        check_vma=False,
    )
```

```python
import jax
import jax.numpy as jnp
from jax import lax
from jax.sharding import PartitionSpec as P

D = 6144
QUERY_HEADS = 32
KVH = 4
DH = 128
BLOCK = 256


def from_behind(value, axis, steps):
    count = lax.axis_size(axis)
    leading, last = (max(0, -steps), min(count, count - steps))
    return lax.ppermute(value, axis, [(source, source + steps) for source in range(leading, last)])


def lightning_block(kv_state, block_inputs):
    query_blk, key_blk, value_blk, decay_blk = block_inputs
    block_len = query_blk.shape[0]
    local_cum = jnp.cumsum(decay_blk, axis=0)
    causal_mask = (jnp.arange(block_len)[:, None] >= jnp.arange(block_len)[None, :])[:, :, None]
    decay_diff = local_cum[:, None, :] - local_cum[None, :, :]
    decays = jnp.where(causal_mask, jnp.exp(jnp.where(causal_mask, decay_diff, 0.0)), 0.0)
    scores = jnp.einsum("thd,shd->hts", query_blk, key_blk, preferred_element_type=jnp.float32)
    weights = (scores * jnp.transpose(decays, (2, 0, 1))).astype(jnp.bfloat16)
    intra_out = jnp.einsum("hts,shd->thd", weights, value_blk, preferred_element_type=jnp.float32)
    query_f = query_blk.astype(jnp.float32)
    inter_out = jnp.einsum(
        "thd,hde->the",
        query_f * jnp.exp(local_cum)[:, :, None],
        kv_state,
        precision=lax.Precision.HIGHEST,
    )
    tail_decay = jnp.exp(local_cum[-1][None, :] - local_cum)
    key_f = key_blk.astype(jnp.float32) * tail_decay[:, :, None]
    kv_state = jnp.exp(local_cum[-1])[:, None, None] * kv_state + jnp.einsum(
        "shd,she->hde", key_f, value_blk.astype(jnp.float32), precision=lax.Precision.HIGHEST
    )
    return (kv_state, intra_out + inter_out)


def shards_base(
    lin_query, lin_key, lin_value, log_decay, stream, out_weight, norm_gain, query_weight, kv_weight
):
    tok_rows = lin_query.shape[0]
    heads_here = log_decay.shape[1]
    head_width = heads_here * DH
    nblocks = tok_rows // BLOCK
    block_shape = (nblocks, BLOCK, heads_here, DH)
    inputs = (
        lin_query.reshape(block_shape),
        lin_key.reshape(block_shape),
        lin_value.reshape(block_shape),
        log_decay.reshape(nblocks, BLOCK, heads_here),
    )
    start_state = jnp.zeros((heads_here, DH, DH), jnp.float32)
    local_state, local_out = lax.scan(lightning_block, start_state, inputs)
    local_out = local_out.reshape(tok_rows, heads_here, DH)
    decay_total = jnp.sum(log_decay, axis=0)
    totals, states = (
        lax.all_gather(decay_total[None].astype(jnp.bfloat16), "seq", axis=0, tiled=True).astype(
            jnp.float32
        ),
        lax.all_gather(local_state[None].astype(jnp.bfloat16), "seq", axis=0, tiled=True).astype(
            jnp.float32
        ),
    )
    position = lax.axis_index("seq")
    device_order = jnp.arange(totals.shape[0])
    earlier = (device_order < position)[:, None]
    before = jnp.sum(jnp.where(earlier, totals, 0.0), axis=0)
    inclusive = jnp.cumsum(totals, axis=0)
    factors = jnp.where(earlier, jnp.exp(jnp.where(earlier, before[None, :] - inclusive, 0.0)), 0.0)
    incoming = jnp.einsum("jh,jhde->hde", factors, states, precision=lax.Precision.HIGHEST)
    running = jnp.cumsum(log_decay, axis=0)
    query_f = (
        lin_query.reshape(tok_rows, heads_here, DH).astype(jnp.float32)
        * jnp.exp(running)[:, :, None]
    )
    carried = jnp.einsum("thd,hde->the", query_f, incoming, precision=lax.Precision.HIGHEST)
    lin_raw = local_out + carried
    lin_out = (
        (lin_raw * lax.rsqrt(jnp.mean(lin_raw * lin_raw, axis=-1, keepdims=True) + 1e-06))
        .astype(jnp.bfloat16)
        .reshape(tok_rows, head_width)
    )
    branch = jnp.dot(
        lin_out,
        lax.all_gather(out_weight, "seq", axis=1, tiled=True),
        preferred_element_type=jnp.float32,
    )
    kv_group = lax.axis_index("heads") * heads_here // (QUERY_HEADS // KVH)
    kv_mine = lax.dynamic_index_in_dim(kv_weight, kv_group, 0, keepdims=False)
    query_rows, kv_rows = (
        lax.all_gather(query_weight, "seq", axis=0, tiled=True),
        lax.all_gather(kv_mine, "seq", axis=0, tiled=True),
    )
    projection = jnp.concatenate([query_rows, kv_rows], axis=1)
    own_sum = lax.psum_scatter(
        branch.astype(jnp.bfloat16), "heads", scatter_dimension=1, tiled=True
    ).astype(jnp.float32)
    mixed_sum = stream.astype(jnp.float32) + own_sum
    stream_next = mixed_sum.astype(jnp.bfloat16)
    total_sq = lax.psum(jnp.sum(mixed_sum * mixed_sum, axis=1), "heads")
    normed = (
        mixed_sum
        * lax.rsqrt(total_sq / D + 1e-05)[:, None]
        * norm_gain.astype(jnp.float32)[None, :]
    ).astype(jnp.bfloat16)
    projected = jnp.dot(
        lax.all_gather(normed, "heads", axis=1, tiled=True),
        projection,
        preferred_element_type=jnp.float32,
    )
    projected = projected.astype(jnp.bfloat16)
    queries = projected[:, :head_width].reshape(tok_rows, heads_here, DH)
    keys_values = projected[:, head_width:]
    position = lax.axis_index("seq")
    query_pos = position * tok_rows + jnp.arange(tok_rows)
    score_scale = float(DH) ** (-0.5)

    def attend(state_in, kv_block, key_start):
        old_max, row_total, weighted = state_in
        key_count = kv_block.shape[0]
        key_part = kv_block[:, :DH]
        value_part = kv_block[:, DH:]
        scores = (
            jnp.einsum("thd,sd->hts", queries, key_part, preferred_element_type=jnp.float32)
            * score_scale
        )
        key_pos = key_start + jnp.arange(key_count)
        allowed = ((key_pos[None, :] <= query_pos[:, None]) & (key_pos[None, :] >= 0))[None, :, :]
        scores = jnp.where(allowed, scores, -1e30)
        new_max = jnp.maximum(old_max, jnp.max(scores, axis=-1))
        expos = jnp.where(allowed, jnp.exp(scores - new_max[:, :, None]), 0.0)
        rescale = jnp.exp(old_max - new_max)
        row_total = row_total * rescale + jnp.sum(expos, axis=-1)
        prob_bf16 = expos.astype(jnp.bfloat16)
        weighted = weighted * rescale[:, :, None] + jnp.einsum(
            "hts,sd->htd", prob_bf16, value_part, preferred_element_type=jnp.float32
        )
        return (new_max, row_total, weighted)

    initial = (
        jnp.full((heads_here, tok_rows), -1e30, jnp.float32),
        jnp.zeros((heads_here, tok_rows), jnp.float32),
        jnp.zeros((heads_here, tok_rows, DH), jnp.float32),
    )
    first_state = attend(initial, keys_values, position * tok_rows)
    seq_count = lax.axis_size("seq")

    def cycle_turn(turn_index, loop_state):
        moving, inner_state = loop_state
        moving = from_behind(moving, "seq", 1)
        source = position - turn_index
        return (moving, attend(inner_state, moving, source * tok_rows))

    _, final_state = lax.fori_loop(1, seq_count, cycle_turn, (keys_values, first_state))
    _, row_total, weighted = final_state
    attended = (
        jnp.transpose(weighted / row_total[:, :, None], (1, 0, 2))
        .reshape(tok_rows, head_width)
        .astype(jnp.bfloat16)
    )
    return (stream_next, attended)


def lightning_local(lin_query, lin_key, lin_value, log_decay):
    tok_rows = lin_query.shape[0]
    heads_here = log_decay.shape[1]
    nblocks = tok_rows // BLOCK
    shape4 = (tok_rows, heads_here, DH)
    q4, k4, v4 = (x.reshape(shape4) for x in (lin_query, lin_key, lin_value))
    state = jnp.zeros((heads_here, DH, DH), jnp.float32)
    outs = []
    for blk in range(nblocks):
        rows = slice(blk * BLOCK, (blk + 1) * BLOCK)
        state, out = lightning_block(state, (q4[rows], k4[rows], v4[rows], log_decay[rows]))
        outs.append(out)
    local_out = jnp.concatenate(outs, axis=0)
    decay_total = jnp.sum(log_decay, axis=0)
    pad_rows = 16
    total_rows = jnp.broadcast_to(decay_total[:, None, None], (heads_here, pad_rows, DH))
    packed = jnp.concatenate([state, total_rows], axis=1).astype(jnp.bfloat16)
    gathered = lax.all_gather(packed[None], "seq", axis=0, tiled=True).astype(jnp.float32)
    states = gathered[:, :, :DH, :]
    totals = gathered[:, :, DH, 0]
    position = lax.axis_index("seq")
    device_order = jnp.arange(totals.shape[0])
    earlier = (device_order < position)[:, None]
    before = jnp.sum(jnp.where(earlier, totals, 0.0), axis=0)
    inclusive = jnp.cumsum(totals, axis=0)
    factors = jnp.where(earlier, jnp.exp(jnp.where(earlier, before[None, :] - inclusive, 0.0)), 0.0)
    incoming = jnp.einsum("jh,jhde->hde", factors, states, precision=lax.Precision.HIGHEST)
    running = jnp.cumsum(log_decay, axis=0)
    query_f = q4.astype(jnp.float32) * jnp.exp(running)[:, :, None]
    carried = jnp.einsum("thd,hde->the", query_f, incoming, precision=lax.Precision.HIGHEST)
    lin_raw = local_out + carried
    lin_out = (
        (lin_raw * lax.rsqrt(jnp.mean(lin_raw * lin_raw, axis=-1, keepdims=True) + 1e-06))
        .astype(jnp.bfloat16)
        .reshape(tok_rows, heads_here * DH)
    )
    return lin_out


def attend_block(queries, query_pos, state_in, kv_block, key_start):
    old_max, row_total, weighted = state_in
    key_count = kv_block.shape[0]
    key_part = kv_block[:, :DH]
    value_part = kv_block[:, DH:]
    score_scale = float(DH) ** (-0.5)
    scores = (
        jnp.einsum("thd,sd->hts", queries, key_part, preferred_element_type=jnp.float32)
        * score_scale
    )
    key_pos = key_start + jnp.arange(key_count)
    allowed = ((key_pos[None, :] <= query_pos[:, None]) & (key_pos[None, :] >= 0))[None, :, :]
    scores = jnp.where(allowed, scores, -1e30)
    new_max = jnp.maximum(old_max, jnp.max(scores, axis=-1))
    expos = jnp.where(allowed, jnp.exp(scores - new_max[:, :, None]), 0.0)
    rescale = jnp.exp(old_max - new_max)
    row_total = row_total * rescale + jnp.sum(expos, axis=-1)
    prob_bf16 = expos.astype(jnp.bfloat16)
    weighted = weighted * rescale[:, :, None] + jnp.einsum(
        "hts,sd->htd", prob_bf16, value_part, preferred_element_type=jnp.float32
    )
    return (new_max, row_total, weighted)


def shards_fast(
    lin_query, lin_key, lin_value, log_decay, stream, out_weight, norm_gain, query_weight, kv_weight
):
    n_heads = lax.axis_size("heads")
    n_seq = lax.axis_size("seq")
    tok_rows = lin_query.shape[0]
    heads_here = log_decay.shape[1]
    head_width = heads_here * DH
    mine_a = lax.axis_index("heads")
    mine_b = lax.axis_index("seq")
    swap = [(x * n_seq + y, y * n_seq + x) for x in range(n_heads) for y in range(n_seq)]
    stream_t = lax.ppermute(stream, ("heads", "seq"), swap)

    lin_out = lightning_local(lin_query, lin_key, lin_value, log_decay)
    lin_all = lax.all_gather(lin_out, "seq", axis=0, tiled=True)
    part = jnp.dot(lin_all, out_weight, preferred_element_type=jnp.float32).astype(jnp.bfloat16)
    own_sum = lax.psum_scatter(part, "heads", scatter_dimension=0, tiled=True)
    mixed_sum = stream_t.astype(jnp.float32) + own_sum.astype(jnp.float32)
    stream_next = lax.ppermute(mixed_sum.astype(jnp.bfloat16), ("heads", "seq"), swap)
    total_sq = lax.psum(jnp.sum(mixed_sum * mixed_sum, axis=1), "seq")
    cols = mixed_sum.shape[1]
    gain_all = lax.all_gather(norm_gain, "heads", axis=0, tiled=True)
    gain_b = lax.dynamic_slice_in_dim(gain_all, mine_b * cols, cols)
    normed = (
        mixed_sum
        * lax.rsqrt(total_sq / D + 1e-05)[:, None]
        * gain_b.astype(jnp.float32)[None, :]
    ).astype(jnp.bfloat16)
    normed_all = lax.all_gather(normed, "heads", axis=0, tiled=True)
    kv_group = mine_a * heads_here // (QUERY_HEADS // KVH)
    kv_mine = lax.dynamic_index_in_dim(kv_weight, kv_group, 0, keepdims=False)
    q_part = jnp.dot(normed_all, query_weight, preferred_element_type=jnp.float32)
    kv_part = jnp.dot(normed_all, kv_mine, preferred_element_type=jnp.float32)
    queries = lax.psum_scatter(
        q_part.astype(jnp.bfloat16), "seq", scatter_dimension=0, tiled=True
    ).reshape(tok_rows, heads_here, DH)
    kv_own = lax.psum_scatter(kv_part.astype(jnp.bfloat16), "seq", scatter_dimension=0, tiled=True)
    query_pos = mine_b * tok_rows + jnp.arange(tok_rows)
    state = (
        jnp.full((heads_here, tok_rows), -1e30, jnp.float32),
        jnp.zeros((heads_here, tok_rows), jnp.float32),
        jnp.zeros((heads_here, tok_rows, DH), jnp.float32),
    )
    earlier_kv = [from_behind(kv_own, "seq", dist) for dist in range(1, n_seq)]
    state = attend_block(queries, query_pos, state, kv_own, mine_b * tok_rows)
    for dist in range(1, n_seq):
        key_start = (mine_b - dist) * tok_rows
        state = attend_block(queries, query_pos, state, earlier_kv[dist - 1], key_start)
    _, row_total, weighted = state
    attended = (
        jnp.transpose(weighted / row_total[:, :, None], (1, 0, 2))
        .reshape(tok_rows, head_width)
        .astype(jnp.bfloat16)
    )
    return (stream_next, attended)


def solution(mesh):
    n_heads = mesh.shape["heads"]
    n_seq = mesh.shape["seq"]
    fast_ok = n_heads == n_seq and QUERY_HEADS % n_heads == 0
    if fast_ok:
        heads_here = QUERY_HEADS // n_heads
        fast_ok = (QUERY_HEADS // KVH) % heads_here == 0 and D % n_seq == 0
    shards = shards_fast if fast_ok else shards_base

    return jax.shard_map(
        shards,
        mesh=mesh,
        in_specs=(
            P(("groups", "seq"), "heads"),
            P(("groups", "seq"), "heads"),
            P(("groups", "seq"), "heads"),
            P(("groups", "seq"), "heads"),
            P(("groups", "seq"), "heads"),
            P("heads", "seq"),
            P("heads"),
            P("seq", "heads"),
            P(None, "seq", None),
        ),
        out_specs=(P(("groups", "seq"), "heads"), P(("groups", "seq"), "heads")),
        check_vma=False,
    )
```

```python
import jax
import jax.numpy as jnp
from jax import lax
from jax.sharding import PartitionSpec as P

D = 6144
QUERY_HEADS = 32
KVH = 4
DH = 128
BLOCK = 256


def from_behind(value, axis, steps):
    count = lax.axis_size(axis)
    leading, last = (max(0, -steps), min(count, count - steps))
    return lax.ppermute(value, axis, [(source, source + steps) for source in range(leading, last)])


def lightning_block(kv_state, block_inputs):
    query_blk, key_blk, value_blk, decay_blk = block_inputs
    block_len = query_blk.shape[0]
    local_cum = jnp.cumsum(decay_blk, axis=0)
    causal_mask = (jnp.arange(block_len)[:, None] >= jnp.arange(block_len)[None, :])[:, :, None]
    decay_diff = local_cum[:, None, :] - local_cum[None, :, :]
    decays = jnp.where(causal_mask, jnp.exp(jnp.where(causal_mask, decay_diff, 0.0)), 0.0)
    scores = jnp.einsum("thd,shd->hts", query_blk, key_blk, preferred_element_type=jnp.float32)
    weights = (scores * jnp.transpose(decays, (2, 0, 1))).astype(jnp.bfloat16)
    intra_out = jnp.einsum("hts,shd->thd", weights, value_blk, preferred_element_type=jnp.float32)
    query_f = query_blk.astype(jnp.float32)
    inter_out = jnp.einsum(
        "thd,hde->the",
        query_f * jnp.exp(local_cum)[:, :, None],
        kv_state,
        precision=lax.Precision.HIGHEST,
    )
    tail_decay = jnp.exp(local_cum[-1][None, :] - local_cum)
    key_f = key_blk.astype(jnp.float32) * tail_decay[:, :, None]
    kv_state = jnp.exp(local_cum[-1])[:, None, None] * kv_state + jnp.einsum(
        "shd,she->hde", key_f, value_blk.astype(jnp.float32), precision=lax.Precision.HIGHEST
    )
    return (kv_state, intra_out + inter_out)


def shards_base(
    lin_query, lin_key, lin_value, log_decay, stream, out_weight, norm_gain, query_weight, kv_weight
):
    tok_rows = lin_query.shape[0]
    heads_here = log_decay.shape[1]
    head_width = heads_here * DH
    nblocks = tok_rows // BLOCK
    block_shape = (nblocks, BLOCK, heads_here, DH)
    inputs = (
        lin_query.reshape(block_shape),
        lin_key.reshape(block_shape),
        lin_value.reshape(block_shape),
        log_decay.reshape(nblocks, BLOCK, heads_here),
    )
    start_state = jnp.zeros((heads_here, DH, DH), jnp.float32)
    local_state, local_out = lax.scan(lightning_block, start_state, inputs)
    local_out = local_out.reshape(tok_rows, heads_here, DH)
    decay_total = jnp.sum(log_decay, axis=0)
    totals, states = (
        lax.all_gather(decay_total[None].astype(jnp.bfloat16), "seq", axis=0, tiled=True).astype(
            jnp.float32
        ),
        lax.all_gather(local_state[None].astype(jnp.bfloat16), "seq", axis=0, tiled=True).astype(
            jnp.float32
        ),
    )
    position = lax.axis_index("seq")
    device_order = jnp.arange(totals.shape[0])
    earlier = (device_order < position)[:, None]
    before = jnp.sum(jnp.where(earlier, totals, 0.0), axis=0)
    inclusive = jnp.cumsum(totals, axis=0)
    factors = jnp.where(earlier, jnp.exp(jnp.where(earlier, before[None, :] - inclusive, 0.0)), 0.0)
    incoming = jnp.einsum("jh,jhde->hde", factors, states, precision=lax.Precision.HIGHEST)
    running = jnp.cumsum(log_decay, axis=0)
    query_f = (
        lin_query.reshape(tok_rows, heads_here, DH).astype(jnp.float32)
        * jnp.exp(running)[:, :, None]
    )
    carried = jnp.einsum("thd,hde->the", query_f, incoming, precision=lax.Precision.HIGHEST)
    lin_raw = local_out + carried
    lin_out = (
        (lin_raw * lax.rsqrt(jnp.mean(lin_raw * lin_raw, axis=-1, keepdims=True) + 1e-06))
        .astype(jnp.bfloat16)
        .reshape(tok_rows, head_width)
    )
    branch = jnp.dot(
        lin_out,
        lax.all_gather(out_weight, "seq", axis=1, tiled=True),
        preferred_element_type=jnp.float32,
    )
    kv_group = lax.axis_index("heads") * heads_here // (QUERY_HEADS // KVH)
    kv_mine = lax.dynamic_index_in_dim(kv_weight, kv_group, 0, keepdims=False)
    query_rows, kv_rows = (
        lax.all_gather(query_weight, "seq", axis=0, tiled=True),
        lax.all_gather(kv_mine, "seq", axis=0, tiled=True),
    )
    projection = jnp.concatenate([query_rows, kv_rows], axis=1)
    own_sum = lax.psum_scatter(
        branch.astype(jnp.bfloat16), "heads", scatter_dimension=1, tiled=True
    ).astype(jnp.float32)
    mixed_sum = stream.astype(jnp.float32) + own_sum
    stream_next = mixed_sum.astype(jnp.bfloat16)
    total_sq = lax.psum(jnp.sum(mixed_sum * mixed_sum, axis=1), "heads")
    normed = (
        mixed_sum
        * lax.rsqrt(total_sq / D + 1e-05)[:, None]
        * norm_gain.astype(jnp.float32)[None, :]
    ).astype(jnp.bfloat16)
    projected = jnp.dot(
        lax.all_gather(normed, "heads", axis=1, tiled=True),
        projection,
        preferred_element_type=jnp.float32,
    )
    projected = projected.astype(jnp.bfloat16)
    queries = projected[:, :head_width].reshape(tok_rows, heads_here, DH)
    keys_values = projected[:, head_width:]
    position = lax.axis_index("seq")
    query_pos = position * tok_rows + jnp.arange(tok_rows)
    score_scale = float(DH) ** (-0.5)

    def attend(state_in, kv_block, key_start):
        old_max, row_total, weighted = state_in
        key_count = kv_block.shape[0]
        key_part = kv_block[:, :DH]
        value_part = kv_block[:, DH:]
        scores = (
            jnp.einsum("thd,sd->hts", queries, key_part, preferred_element_type=jnp.float32)
            * score_scale
        )
        key_pos = key_start + jnp.arange(key_count)
        allowed = ((key_pos[None, :] <= query_pos[:, None]) & (key_pos[None, :] >= 0))[None, :, :]
        scores = jnp.where(allowed, scores, -1e30)
        new_max = jnp.maximum(old_max, jnp.max(scores, axis=-1))
        expos = jnp.where(allowed, jnp.exp(scores - new_max[:, :, None]), 0.0)
        rescale = jnp.exp(old_max - new_max)
        row_total = row_total * rescale + jnp.sum(expos, axis=-1)
        prob_bf16 = expos.astype(jnp.bfloat16)
        weighted = weighted * rescale[:, :, None] + jnp.einsum(
            "hts,sd->htd", prob_bf16, value_part, preferred_element_type=jnp.float32
        )
        return (new_max, row_total, weighted)

    initial = (
        jnp.full((heads_here, tok_rows), -1e30, jnp.float32),
        jnp.zeros((heads_here, tok_rows), jnp.float32),
        jnp.zeros((heads_here, tok_rows, DH), jnp.float32),
    )
    first_state = attend(initial, keys_values, position * tok_rows)
    seq_count = lax.axis_size("seq")

    def cycle_turn(turn_index, loop_state):
        moving, inner_state = loop_state
        moving = from_behind(moving, "seq", 1)
        source = position - turn_index
        return (moving, attend(inner_state, moving, source * tok_rows))

    _, final_state = lax.fori_loop(1, seq_count, cycle_turn, (keys_values, first_state))
    _, row_total, weighted = final_state
    attended = (
        jnp.transpose(weighted / row_total[:, :, None], (1, 0, 2))
        .reshape(tok_rows, head_width)
        .astype(jnp.bfloat16)
    )
    return (stream_next, attended)


def lightning_local(lin_query, lin_key, lin_value, log_decay):
    tok_rows = lin_query.shape[0]
    heads_here = log_decay.shape[1]
    nblocks = tok_rows // BLOCK
    shape4 = (tok_rows, heads_here, DH)
    q4, k4, v4 = (x.reshape(shape4) for x in (lin_query, lin_key, lin_value))
    state = jnp.zeros((heads_here, DH, DH), jnp.float32)
    outs = []
    for blk in range(nblocks):
        rows = slice(blk * BLOCK, (blk + 1) * BLOCK)
        state, out = lightning_block(state, (q4[rows], k4[rows], v4[rows], log_decay[rows]))
        outs.append(out)
    local_out = jnp.concatenate(outs, axis=0)
    decay_total = jnp.sum(log_decay, axis=0)
    pad_rows = 16
    total_rows = jnp.broadcast_to(decay_total[:, None, None], (heads_here, pad_rows, DH))
    packed = jnp.concatenate([state, total_rows], axis=1).astype(jnp.bfloat16)
    gathered = lax.all_gather(packed[None], "seq", axis=0, tiled=True).astype(jnp.float32)
    states = gathered[:, :, :DH, :]
    totals = gathered[:, :, DH, 0]
    position = lax.axis_index("seq")
    device_order = jnp.arange(totals.shape[0])
    earlier = (device_order < position)[:, None]
    before = jnp.sum(jnp.where(earlier, totals, 0.0), axis=0)
    inclusive = jnp.cumsum(totals, axis=0)
    factors = jnp.where(earlier, jnp.exp(jnp.where(earlier, before[None, :] - inclusive, 0.0)), 0.0)
    incoming = jnp.einsum("jh,jhde->hde", factors, states, precision=lax.Precision.HIGHEST)
    running = jnp.cumsum(log_decay, axis=0)
    query_f = q4.astype(jnp.float32) * jnp.exp(running)[:, :, None]
    carried = jnp.einsum("thd,hde->the", query_f, incoming, precision=lax.Precision.HIGHEST)
    lin_raw = local_out + carried
    lin_out = (
        (lin_raw * lax.rsqrt(jnp.mean(lin_raw * lin_raw, axis=-1, keepdims=True) + 1e-06))
        .astype(jnp.bfloat16)
        .reshape(tok_rows, heads_here * DH)
    )
    return lin_out


def heads_reduce_scatter(part, n_heads):
    if n_heads != 4:
        return lax.psum_scatter(part, "heads", scatter_dimension=0, tiled=True).astype(jnp.float32)
    mine = lax.axis_index("heads")
    core = mine % 2
    chip = mine // 2
    rows = part.shape[0] // n_heads
    grid = part.reshape(2, 2, rows, part.shape[1])
    keep1 = lax.dynamic_index_in_dim(grid, core, axis=1, keepdims=False)
    send1 = lax.dynamic_index_in_dim(grid, 1 - core, axis=1, keepdims=False)
    recv1 = lax.ppermute(send1, "heads", [(i, i ^ 1) for i in range(n_heads)])
    chip_sum = keep1.astype(jnp.float32) + recv1.astype(jnp.float32)
    keep2 = lax.dynamic_index_in_dim(chip_sum, chip, axis=0, keepdims=False)
    send2 = lax.dynamic_index_in_dim(chip_sum, 1 - chip, axis=0, keepdims=False)
    recv2 = lax.ppermute(send2.astype(jnp.bfloat16), "heads", [(i, i ^ 2) for i in range(n_heads)])
    return keep2 + recv2.astype(jnp.float32)


def attend_block(queries, query_pos, state_in, kv_block, key_start):
    old_max, row_total, weighted = state_in
    key_count = kv_block.shape[0]
    key_part = kv_block[:, :DH]
    value_part = kv_block[:, DH:]
    score_scale = float(DH) ** (-0.5)
    scores = (
        jnp.einsum("thd,sd->hts", queries, key_part, preferred_element_type=jnp.float32)
        * score_scale
    )
    key_pos = key_start + jnp.arange(key_count)
    allowed = ((key_pos[None, :] <= query_pos[:, None]) & (key_pos[None, :] >= 0))[None, :, :]
    scores = jnp.where(allowed, scores, -1e30)
    new_max = jnp.maximum(old_max, jnp.max(scores, axis=-1))
    expos = jnp.where(allowed, jnp.exp(scores - new_max[:, :, None]), 0.0)
    rescale = jnp.exp(old_max - new_max)
    row_total = row_total * rescale + jnp.sum(expos, axis=-1)
    prob_bf16 = expos.astype(jnp.bfloat16)
    weighted = weighted * rescale[:, :, None] + jnp.einsum(
        "hts,sd->htd", prob_bf16, value_part, preferred_element_type=jnp.float32
    )
    return (new_max, row_total, weighted)


def shards_fast(
    lin_query, lin_key, lin_value, log_decay, stream, out_weight, norm_gain, query_weight, kv_weight
):
    n_heads = lax.axis_size("heads")
    n_seq = lax.axis_size("seq")
    tok_rows = lin_query.shape[0]
    heads_here = log_decay.shape[1]
    head_width = heads_here * DH
    mine_a = lax.axis_index("heads")
    mine_b = lax.axis_index("seq")
    swap = [(x * n_seq + y, y * n_seq + x) for x in range(n_heads) for y in range(n_seq)]
    stream_t = lax.ppermute(stream, ("heads", "seq"), swap)

    lin_out = lightning_local(lin_query, lin_key, lin_value, log_decay)
    lin_all = lax.all_gather(lin_out, "seq", axis=0, tiled=True)
    part = jnp.dot(lin_all, out_weight, preferred_element_type=jnp.float32).astype(jnp.bfloat16)
    own_sum = heads_reduce_scatter(part, n_heads)
    mixed_sum = stream_t.astype(jnp.float32) + own_sum
    stream_next = lax.ppermute(mixed_sum.astype(jnp.bfloat16), ("heads", "seq"), swap)
    total_sq = lax.psum(jnp.sum(mixed_sum * mixed_sum, axis=1), "seq")
    cols = mixed_sum.shape[1]
    gain_all = lax.all_gather(norm_gain, "heads", axis=0, tiled=True)
    gain_b = lax.dynamic_slice_in_dim(gain_all, mine_b * cols, cols)
    normed = (
        mixed_sum
        * lax.rsqrt(total_sq / D + 1e-05)[:, None]
        * gain_b.astype(jnp.float32)[None, :]
    ).astype(jnp.bfloat16)
    normed_all = lax.all_gather(normed, "heads", axis=0, tiled=True)
    kv_group = mine_a * heads_here // (QUERY_HEADS // KVH)
    kv_mine = lax.dynamic_index_in_dim(kv_weight, kv_group, 0, keepdims=False)
    q_part = jnp.dot(normed_all, query_weight, preferred_element_type=jnp.float32)
    kv_part = jnp.dot(normed_all, kv_mine, preferred_element_type=jnp.float32)
    queries = lax.psum_scatter(
        q_part.astype(jnp.bfloat16), "seq", scatter_dimension=0, tiled=True
    ).reshape(tok_rows, heads_here, DH)
    kv_own = lax.psum_scatter(kv_part.astype(jnp.bfloat16), "seq", scatter_dimension=0, tiled=True)
    query_pos = mine_b * tok_rows + jnp.arange(tok_rows)
    state = (
        jnp.full((heads_here, tok_rows), -1e30, jnp.float32),
        jnp.zeros((heads_here, tok_rows), jnp.float32),
        jnp.zeros((heads_here, tok_rows, DH), jnp.float32),
    )
    earlier_kv = [from_behind(kv_own, "seq", dist) for dist in range(1, n_seq)]
    state = attend_block(queries, query_pos, state, kv_own, mine_b * tok_rows)
    for dist in range(1, n_seq):
        key_start = (mine_b - dist) * tok_rows
        state = attend_block(queries, query_pos, state, earlier_kv[dist - 1], key_start)
    _, row_total, weighted = state
    attended = (
        jnp.transpose(weighted / row_total[:, :, None], (1, 0, 2))
        .reshape(tok_rows, head_width)
        .astype(jnp.bfloat16)
    )
    return (stream_next, attended)


def solution(mesh):
    n_heads = mesh.shape["heads"]
    n_seq = mesh.shape["seq"]
    fast_ok = n_heads == n_seq and QUERY_HEADS % n_heads == 0
    if fast_ok:
        heads_here = QUERY_HEADS // n_heads
        fast_ok = (QUERY_HEADS // KVH) % heads_here == 0 and D % n_seq == 0
    shards = shards_fast if fast_ok else shards_base

    return jax.shard_map(
        shards,
        mesh=mesh,
        in_specs=(
            P(("groups", "seq"), "heads"),
            P(("groups", "seq"), "heads"),
            P(("groups", "seq"), "heads"),
            P(("groups", "seq"), "heads"),
            P(("groups", "seq"), "heads"),
            P("heads", "seq"),
            P("heads"),
            P("seq", "heads"),
            P(None, "seq", None),
        ),
        out_specs=(P(("groups", "seq"), "heads"), P(("groups", "seq"), "heads")),
        check_vma=False,
    )
```

```python
import jax
import jax.numpy as jnp
from jax import lax
from jax.sharding import PartitionSpec as P

D = 6144
QUERY_HEADS = 32
KVH = 4
DH = 128
BLOCK = 256


def from_behind(value, axis, steps):
    count = lax.axis_size(axis)
    leading, last = (max(0, -steps), min(count, count - steps))
    return lax.ppermute(value, axis, [(source, source + steps) for source in range(leading, last)])


def lightning_block(kv_state, block_inputs):
    query_blk, key_blk, value_blk, decay_blk = block_inputs
    block_len = query_blk.shape[0]
    local_cum = jnp.cumsum(decay_blk, axis=0)
    causal_mask = (jnp.arange(block_len)[:, None] >= jnp.arange(block_len)[None, :])[:, :, None]
    decay_diff = local_cum[:, None, :] - local_cum[None, :, :]
    decays = jnp.where(causal_mask, jnp.exp(jnp.where(causal_mask, decay_diff, 0.0)), 0.0)
    scores = jnp.einsum("thd,shd->hts", query_blk, key_blk, preferred_element_type=jnp.float32)
    weights = (scores * jnp.transpose(decays, (2, 0, 1))).astype(jnp.bfloat16)
    intra_out = jnp.einsum("hts,shd->thd", weights, value_blk, preferred_element_type=jnp.float32)
    query_f = query_blk.astype(jnp.float32)
    inter_out = jnp.einsum(
        "thd,hde->the",
        query_f * jnp.exp(local_cum)[:, :, None],
        kv_state,
        precision=lax.Precision.HIGHEST,
    )
    tail_decay = jnp.exp(local_cum[-1][None, :] - local_cum)
    key_f = key_blk.astype(jnp.float32) * tail_decay[:, :, None]
    kv_state = jnp.exp(local_cum[-1])[:, None, None] * kv_state + jnp.einsum(
        "shd,she->hde", key_f, value_blk.astype(jnp.float32), precision=lax.Precision.HIGHEST
    )
    return (kv_state, intra_out + inter_out)


def shards_base(
    lin_query, lin_key, lin_value, log_decay, stream, out_weight, norm_gain, query_weight, kv_weight
):
    tok_rows = lin_query.shape[0]
    heads_here = log_decay.shape[1]
    head_width = heads_here * DH
    nblocks = tok_rows // BLOCK
    block_shape = (nblocks, BLOCK, heads_here, DH)
    inputs = (
        lin_query.reshape(block_shape),
        lin_key.reshape(block_shape),
        lin_value.reshape(block_shape),
        log_decay.reshape(nblocks, BLOCK, heads_here),
    )
    start_state = jnp.zeros((heads_here, DH, DH), jnp.float32)
    local_state, local_out = lax.scan(lightning_block, start_state, inputs)
    local_out = local_out.reshape(tok_rows, heads_here, DH)
    decay_total = jnp.sum(log_decay, axis=0)
    totals, states = (
        lax.all_gather(decay_total[None].astype(jnp.bfloat16), "seq", axis=0, tiled=True).astype(
            jnp.float32
        ),
        lax.all_gather(local_state[None].astype(jnp.bfloat16), "seq", axis=0, tiled=True).astype(
            jnp.float32
        ),
    )
    position = lax.axis_index("seq")
    device_order = jnp.arange(totals.shape[0])
    earlier = (device_order < position)[:, None]
    before = jnp.sum(jnp.where(earlier, totals, 0.0), axis=0)
    inclusive = jnp.cumsum(totals, axis=0)
    factors = jnp.where(earlier, jnp.exp(jnp.where(earlier, before[None, :] - inclusive, 0.0)), 0.0)
    incoming = jnp.einsum("jh,jhde->hde", factors, states, precision=lax.Precision.HIGHEST)
    running = jnp.cumsum(log_decay, axis=0)
    query_f = (
        lin_query.reshape(tok_rows, heads_here, DH).astype(jnp.float32)
        * jnp.exp(running)[:, :, None]
    )
    carried = jnp.einsum("thd,hde->the", query_f, incoming, precision=lax.Precision.HIGHEST)
    lin_raw = local_out + carried
    lin_out = (
        (lin_raw * lax.rsqrt(jnp.mean(lin_raw * lin_raw, axis=-1, keepdims=True) + 1e-06))
        .astype(jnp.bfloat16)
        .reshape(tok_rows, head_width)
    )
    branch = jnp.dot(
        lin_out,
        lax.all_gather(out_weight, "seq", axis=1, tiled=True),
        preferred_element_type=jnp.float32,
    )
    kv_group = lax.axis_index("heads") * heads_here // (QUERY_HEADS // KVH)
    kv_mine = lax.dynamic_index_in_dim(kv_weight, kv_group, 0, keepdims=False)
    query_rows, kv_rows = (
        lax.all_gather(query_weight, "seq", axis=0, tiled=True),
        lax.all_gather(kv_mine, "seq", axis=0, tiled=True),
    )
    projection = jnp.concatenate([query_rows, kv_rows], axis=1)
    own_sum = lax.psum_scatter(
        branch.astype(jnp.bfloat16), "heads", scatter_dimension=1, tiled=True
    ).astype(jnp.float32)
    mixed_sum = stream.astype(jnp.float32) + own_sum
    stream_next = mixed_sum.astype(jnp.bfloat16)
    total_sq = lax.psum(jnp.sum(mixed_sum * mixed_sum, axis=1), "heads")
    normed = (
        mixed_sum
        * lax.rsqrt(total_sq / D + 1e-05)[:, None]
        * norm_gain.astype(jnp.float32)[None, :]
    ).astype(jnp.bfloat16)
    projected = jnp.dot(
        lax.all_gather(normed, "heads", axis=1, tiled=True),
        projection,
        preferred_element_type=jnp.float32,
    )
    projected = projected.astype(jnp.bfloat16)
    queries = projected[:, :head_width].reshape(tok_rows, heads_here, DH)
    keys_values = projected[:, head_width:]
    position = lax.axis_index("seq")
    query_pos = position * tok_rows + jnp.arange(tok_rows)
    score_scale = float(DH) ** (-0.5)

    def attend(state_in, kv_block, key_start):
        old_max, row_total, weighted = state_in
        key_count = kv_block.shape[0]
        key_part = kv_block[:, :DH]
        value_part = kv_block[:, DH:]
        scores = (
            jnp.einsum("thd,sd->hts", queries, key_part, preferred_element_type=jnp.float32)
            * score_scale
        )
        key_pos = key_start + jnp.arange(key_count)
        allowed = ((key_pos[None, :] <= query_pos[:, None]) & (key_pos[None, :] >= 0))[None, :, :]
        scores = jnp.where(allowed, scores, -1e30)
        new_max = jnp.maximum(old_max, jnp.max(scores, axis=-1))
        expos = jnp.where(allowed, jnp.exp(scores - new_max[:, :, None]), 0.0)
        rescale = jnp.exp(old_max - new_max)
        row_total = row_total * rescale + jnp.sum(expos, axis=-1)
        prob_bf16 = expos.astype(jnp.bfloat16)
        weighted = weighted * rescale[:, :, None] + jnp.einsum(
            "hts,sd->htd", prob_bf16, value_part, preferred_element_type=jnp.float32
        )
        return (new_max, row_total, weighted)

    initial = (
        jnp.full((heads_here, tok_rows), -1e30, jnp.float32),
        jnp.zeros((heads_here, tok_rows), jnp.float32),
        jnp.zeros((heads_here, tok_rows, DH), jnp.float32),
    )
    first_state = attend(initial, keys_values, position * tok_rows)
    seq_count = lax.axis_size("seq")

    def cycle_turn(turn_index, loop_state):
        moving, inner_state = loop_state
        moving = from_behind(moving, "seq", 1)
        source = position - turn_index
        return (moving, attend(inner_state, moving, source * tok_rows))

    _, final_state = lax.fori_loop(1, seq_count, cycle_turn, (keys_values, first_state))
    _, row_total, weighted = final_state
    attended = (
        jnp.transpose(weighted / row_total[:, :, None], (1, 0, 2))
        .reshape(tok_rows, head_width)
        .astype(jnp.bfloat16)
    )
    return (stream_next, attended)


def lightning_local(lin_query, lin_key, lin_value, log_decay):
    tok_rows = lin_query.shape[0]
    heads_here = log_decay.shape[1]
    nblocks = tok_rows // BLOCK
    shape4 = (tok_rows, heads_here, DH)
    q4, k4, v4 = (x.reshape(shape4) for x in (lin_query, lin_key, lin_value))
    state = jnp.zeros((heads_here, DH, DH), jnp.float32)
    outs = []
    for blk in range(nblocks):
        rows = slice(blk * BLOCK, (blk + 1) * BLOCK)
        state, out = lightning_block(state, (q4[rows], k4[rows], v4[rows], log_decay[rows]))
        outs.append(out)
    local_out = jnp.concatenate(outs, axis=0)
    decay_total = jnp.sum(log_decay, axis=0)
    pad_rows = 16
    total_rows = jnp.broadcast_to(decay_total[:, None, None], (heads_here, pad_rows, DH))
    packed = jnp.concatenate([state, total_rows], axis=1).astype(jnp.bfloat16)
    gathered = lax.all_gather(packed[None], "seq", axis=0, tiled=True)
    gathered = gathered.astype(jnp.float32)
    states = gathered[:, :, :DH, :]
    totals = gathered[:, :, DH, 0]
    position = lax.axis_index("seq")
    device_order = jnp.arange(totals.shape[0])
    earlier = (device_order < position)[:, None]
    before = jnp.sum(jnp.where(earlier, totals, 0.0), axis=0)
    inclusive = jnp.cumsum(totals, axis=0)
    factors = jnp.where(earlier, jnp.exp(jnp.where(earlier, before[None, :] - inclusive, 0.0)), 0.0)
    incoming = jnp.einsum("jh,jhde->hde", factors, states, precision=lax.Precision.HIGHEST)
    running = jnp.cumsum(log_decay, axis=0)
    query_f = q4.astype(jnp.float32) * jnp.exp(running)[:, :, None]
    carried = jnp.einsum("thd,hde->the", query_f, incoming, precision=lax.Precision.HIGHEST)
    lin_raw = local_out + carried
    lin_out = (
        (lin_raw * lax.rsqrt(jnp.mean(lin_raw * lin_raw, axis=-1, keepdims=True) + 1e-06))
        .astype(jnp.bfloat16)
        .reshape(tok_rows, heads_here * DH)
    )
    return lin_out


def heads_reduce_scatter(part, n_heads):
    if n_heads != 4:
        return lax.psum_scatter(part, "heads", scatter_dimension=0, tiled=True).astype(jnp.float32)
    mine = lax.axis_index("heads")
    core = mine % 2
    chip = mine // 2
    rows = part.shape[0] // n_heads
    grid = part.reshape(2, 2, rows, part.shape[1])
    keep1 = lax.dynamic_index_in_dim(grid, core, axis=1, keepdims=False)
    send1 = lax.dynamic_index_in_dim(grid, 1 - core, axis=1, keepdims=False)
    recv1 = lax.ppermute(send1, "heads", [(i, i ^ 1) for i in range(n_heads)])
    chip_sum = keep1.astype(jnp.float32) + recv1.astype(jnp.float32)
    keep2 = lax.dynamic_index_in_dim(chip_sum, chip, axis=0, keepdims=False)
    send2 = lax.dynamic_index_in_dim(chip_sum, 1 - chip, axis=0, keepdims=False)
    recv2 = lax.ppermute(send2.astype(jnp.bfloat16), "heads", [(i, i ^ 2) for i in range(n_heads)])
    return keep2 + recv2.astype(jnp.float32)


def attend_block(queries, query_pos, state_in, kv_block, key_start):
    old_max, row_total, weighted = state_in
    key_count = kv_block.shape[0]
    key_part = kv_block[:, :DH]
    value_part = kv_block[:, DH:]
    score_scale = float(DH) ** (-0.5)
    scores = (
        jnp.einsum("thd,sd->hts", queries, key_part, preferred_element_type=jnp.float32)
        * score_scale
    )
    key_pos = key_start + jnp.arange(key_count)
    allowed = ((key_pos[None, :] <= query_pos[:, None]) & (key_pos[None, :] >= 0))[None, :, :]
    scores = jnp.where(allowed, scores, -1e30)
    new_max = jnp.maximum(old_max, jnp.max(scores, axis=-1))
    expos = jnp.where(allowed, jnp.exp(scores - new_max[:, :, None]), 0.0)
    rescale = jnp.exp(old_max - new_max)
    row_total = row_total * rescale + jnp.sum(expos, axis=-1)
    prob_bf16 = expos.astype(jnp.bfloat16)
    weighted = weighted * rescale[:, :, None] + jnp.einsum(
        "hts,sd->htd", prob_bf16, value_part, preferred_element_type=jnp.float32
    )
    return (new_max, row_total, weighted)


def shards_fast(*args):
    return shards_fast_body(*args)


def shards_fast_body(
    lin_query, lin_key, lin_value, log_decay, stream, out_weight, norm_gain, query_weight, kv_weight
):
    n_heads = lax.axis_size("heads")
    n_seq = lax.axis_size("seq")
    tok_rows = lin_query.shape[0]
    heads_here = log_decay.shape[1]
    head_width = heads_here * DH
    mine_a = lax.axis_index("heads")
    mine_b = lax.axis_index("seq")
    swap = [(x * n_seq + y, y * n_seq + x) for x in range(n_heads) for y in range(n_seq)]
    gain_rows = jnp.broadcast_to(norm_gain[None, :], (16, norm_gain.shape[0]))
    packed = lax.ppermute(
        jnp.concatenate([stream, gain_rows], axis=0), ("heads", "seq"), swap
    )
    stream_t = packed[:tok_rows]
    gain_b = packed[tok_rows]

    lin_out = lightning_local(lin_query, lin_key, lin_value, log_decay)
    halves = []
    half_rows = tok_rows // 2
    for half in range(2):
        lin_all = lax.all_gather(
            lin_out[half * half_rows : (half + 1) * half_rows], "seq", axis=0, tiled=True
        )
        part = jnp.dot(lin_all, out_weight, preferred_element_type=jnp.float32)
        halves.append(heads_reduce_scatter(part.astype(jnp.bfloat16), n_heads))
    own_sum = jnp.concatenate(halves, axis=0)
    mixed_sum = stream_t.astype(jnp.float32) + own_sum
    stream_next = lax.ppermute(mixed_sum.astype(jnp.bfloat16), ("heads", "seq"), swap)
    total_sq = lax.psum(jnp.sum(mixed_sum * mixed_sum, axis=1), "seq")
    normed = (
        mixed_sum
        * lax.rsqrt(total_sq / D + 1e-05)[:, None]
        * gain_b.astype(jnp.float32)[None, :]
    ).astype(jnp.bfloat16)
    normed_all = lax.all_gather(normed, "heads", axis=0, tiled=True)
    kv_group = mine_a * heads_here // (QUERY_HEADS // KVH)
    kv_mine = lax.dynamic_index_in_dim(kv_weight, kv_group, 0, keepdims=False)
    q_part = jnp.dot(normed_all, query_weight, preferred_element_type=jnp.float32)
    kv_part = jnp.dot(normed_all, kv_mine, preferred_element_type=jnp.float32)
    queries = lax.psum_scatter(
        q_part.astype(jnp.bfloat16), "seq", scatter_dimension=0, tiled=True
    ).reshape(tok_rows, heads_here, DH)
    kv_own = lax.psum_scatter(kv_part.astype(jnp.bfloat16), "seq", scatter_dimension=0, tiled=True)
    query_pos = mine_b * tok_rows + jnp.arange(tok_rows)
    state = (
        jnp.full((heads_here, tok_rows), -1e30, jnp.float32),
        jnp.zeros((heads_here, tok_rows), jnp.float32),
        jnp.zeros((heads_here, tok_rows, DH), jnp.float32),
    )
    earlier_kv = [from_behind(kv_own, "seq", dist) for dist in range(1, n_seq)]
    state = attend_block(queries, query_pos, state, kv_own, mine_b * tok_rows)
    for dist in range(1, n_seq):
        key_start = (mine_b - dist) * tok_rows
        state = attend_block(queries, query_pos, state, earlier_kv[dist - 1], key_start)
    _, row_total, weighted = state
    attended = (
        jnp.transpose(weighted / row_total[:, :, None], (1, 0, 2))
        .reshape(tok_rows, head_width)
        .astype(jnp.bfloat16)
    )
    return (stream_next, attended)


def solution(mesh):
    n_heads = mesh.shape["heads"]
    n_seq = mesh.shape["seq"]
    fast_ok = n_heads == n_seq and QUERY_HEADS % n_heads == 0
    if fast_ok:
        heads_here = QUERY_HEADS // n_heads
        fast_ok = (QUERY_HEADS // KVH) % heads_here == 0 and D % n_seq == 0
    shards = shards_fast if fast_ok else shards_base

    return jax.shard_map(
        shards,
        mesh=mesh,
        in_specs=(
            P(("groups", "seq"), "heads"),
            P(("groups", "seq"), "heads"),
            P(("groups", "seq"), "heads"),
            P(("groups", "seq"), "heads"),
            P(("groups", "seq"), "heads"),
            P("heads", "seq"),
            P("heads"),
            P("seq", "heads"),
            P(None, "seq", None),
        ),
        out_specs=(P(("groups", "seq"), "heads"), P(("groups", "seq"), "heads")),
        check_vma=False,
    )
```

```python
import jax
import jax.numpy as jnp
from jax import lax
from jax.sharding import PartitionSpec as P

D = 6144
QUERY_HEADS = 32
KVH = 4
DH = 128
BLOCK = 256


def from_behind(value, axis, steps):
    count = lax.axis_size(axis)
    leading, last = (max(0, -steps), min(count, count - steps))
    return lax.ppermute(value, axis, [(source, source + steps) for source in range(leading, last)])


def lightning_block(kv_state, block_inputs):
    query_blk, key_blk, value_blk, decay_blk = block_inputs
    block_len = query_blk.shape[0]
    local_cum = jnp.cumsum(decay_blk, axis=0)
    causal_mask = (jnp.arange(block_len)[:, None] >= jnp.arange(block_len)[None, :])[:, :, None]
    decay_diff = local_cum[:, None, :] - local_cum[None, :, :]
    decays = jnp.where(causal_mask, jnp.exp(jnp.where(causal_mask, decay_diff, 0.0)), 0.0)
    scores = jnp.einsum("thd,shd->hts", query_blk, key_blk, preferred_element_type=jnp.float32)
    weights = (scores * jnp.transpose(decays, (2, 0, 1))).astype(jnp.bfloat16)
    intra_out = jnp.einsum("hts,shd->thd", weights, value_blk, preferred_element_type=jnp.float32)
    query_f = query_blk.astype(jnp.float32)
    inter_out = jnp.einsum(
        "thd,hde->the",
        query_f * jnp.exp(local_cum)[:, :, None],
        kv_state,
        precision=lax.Precision.HIGHEST,
    )
    tail_decay = jnp.exp(local_cum[-1][None, :] - local_cum)
    key_f = key_blk.astype(jnp.float32) * tail_decay[:, :, None]
    kv_state = jnp.exp(local_cum[-1])[:, None, None] * kv_state + jnp.einsum(
        "shd,she->hde", key_f, value_blk.astype(jnp.float32), precision=lax.Precision.HIGHEST
    )
    return (kv_state, intra_out + inter_out)


def shards_base(
    lin_query, lin_key, lin_value, log_decay, stream, out_weight, norm_gain, query_weight, kv_weight
):
    tok_rows = lin_query.shape[0]
    heads_here = log_decay.shape[1]
    head_width = heads_here * DH
    nblocks = tok_rows // BLOCK
    block_shape = (nblocks, BLOCK, heads_here, DH)
    inputs = (
        lin_query.reshape(block_shape),
        lin_key.reshape(block_shape),
        lin_value.reshape(block_shape),
        log_decay.reshape(nblocks, BLOCK, heads_here),
    )
    start_state = jnp.zeros((heads_here, DH, DH), jnp.float32)
    local_state, local_out = lax.scan(lightning_block, start_state, inputs)
    local_out = local_out.reshape(tok_rows, heads_here, DH)
    decay_total = jnp.sum(log_decay, axis=0)
    totals, states = (
        lax.all_gather(decay_total[None].astype(jnp.bfloat16), "seq", axis=0, tiled=True).astype(
            jnp.float32
        ),
        lax.all_gather(local_state[None].astype(jnp.bfloat16), "seq", axis=0, tiled=True).astype(
            jnp.float32
        ),
    )
    position = lax.axis_index("seq")
    device_order = jnp.arange(totals.shape[0])
    earlier = (device_order < position)[:, None]
    before = jnp.sum(jnp.where(earlier, totals, 0.0), axis=0)
    inclusive = jnp.cumsum(totals, axis=0)
    factors = jnp.where(earlier, jnp.exp(jnp.where(earlier, before[None, :] - inclusive, 0.0)), 0.0)
    incoming = jnp.einsum("jh,jhde->hde", factors, states, precision=lax.Precision.HIGHEST)
    running = jnp.cumsum(log_decay, axis=0)
    query_f = (
        lin_query.reshape(tok_rows, heads_here, DH).astype(jnp.float32)
        * jnp.exp(running)[:, :, None]
    )
    carried = jnp.einsum("thd,hde->the", query_f, incoming, precision=lax.Precision.HIGHEST)
    lin_raw = local_out + carried
    lin_out = (
        (lin_raw * lax.rsqrt(jnp.mean(lin_raw * lin_raw, axis=-1, keepdims=True) + 1e-06))
        .astype(jnp.bfloat16)
        .reshape(tok_rows, head_width)
    )
    branch = jnp.dot(
        lin_out,
        lax.all_gather(out_weight, "seq", axis=1, tiled=True),
        preferred_element_type=jnp.float32,
    )
    kv_group = lax.axis_index("heads") * heads_here // (QUERY_HEADS // KVH)
    kv_mine = lax.dynamic_index_in_dim(kv_weight, kv_group, 0, keepdims=False)
    query_rows, kv_rows = (
        lax.all_gather(query_weight, "seq", axis=0, tiled=True),
        lax.all_gather(kv_mine, "seq", axis=0, tiled=True),
    )
    projection = jnp.concatenate([query_rows, kv_rows], axis=1)
    own_sum = lax.psum_scatter(
        branch.astype(jnp.bfloat16), "heads", scatter_dimension=1, tiled=True
    ).astype(jnp.float32)
    mixed_sum = stream.astype(jnp.float32) + own_sum
    stream_next = mixed_sum.astype(jnp.bfloat16)
    total_sq = lax.psum(jnp.sum(mixed_sum * mixed_sum, axis=1), "heads")
    normed = (
        mixed_sum
        * lax.rsqrt(total_sq / D + 1e-05)[:, None]
        * norm_gain.astype(jnp.float32)[None, :]
    ).astype(jnp.bfloat16)
    projected = jnp.dot(
        lax.all_gather(normed, "heads", axis=1, tiled=True),
        projection,
        preferred_element_type=jnp.float32,
    )
    projected = projected.astype(jnp.bfloat16)
    queries = projected[:, :head_width].reshape(tok_rows, heads_here, DH)
    keys_values = projected[:, head_width:]
    position = lax.axis_index("seq")
    query_pos = position * tok_rows + jnp.arange(tok_rows)
    score_scale = float(DH) ** (-0.5)

    def attend(state_in, kv_block, key_start):
        old_max, row_total, weighted = state_in
        key_count = kv_block.shape[0]
        key_part = kv_block[:, :DH]
        value_part = kv_block[:, DH:]
        scores = (
            jnp.einsum("thd,sd->hts", queries, key_part, preferred_element_type=jnp.float32)
            * score_scale
        )
        key_pos = key_start + jnp.arange(key_count)
        allowed = ((key_pos[None, :] <= query_pos[:, None]) & (key_pos[None, :] >= 0))[None, :, :]
        scores = jnp.where(allowed, scores, -1e30)
        new_max = jnp.maximum(old_max, jnp.max(scores, axis=-1))
        expos = jnp.where(allowed, jnp.exp(scores - new_max[:, :, None]), 0.0)
        rescale = jnp.exp(old_max - new_max)
        row_total = row_total * rescale + jnp.sum(expos, axis=-1)
        prob_bf16 = expos.astype(jnp.bfloat16)
        weighted = weighted * rescale[:, :, None] + jnp.einsum(
            "hts,sd->htd", prob_bf16, value_part, preferred_element_type=jnp.float32
        )
        return (new_max, row_total, weighted)

    initial = (
        jnp.full((heads_here, tok_rows), -1e30, jnp.float32),
        jnp.zeros((heads_here, tok_rows), jnp.float32),
        jnp.zeros((heads_here, tok_rows, DH), jnp.float32),
    )
    first_state = attend(initial, keys_values, position * tok_rows)
    seq_count = lax.axis_size("seq")

    def cycle_turn(turn_index, loop_state):
        moving, inner_state = loop_state
        moving = from_behind(moving, "seq", 1)
        source = position - turn_index
        return (moving, attend(inner_state, moving, source * tok_rows))

    _, final_state = lax.fori_loop(1, seq_count, cycle_turn, (keys_values, first_state))
    _, row_total, weighted = final_state
    attended = (
        jnp.transpose(weighted / row_total[:, :, None], (1, 0, 2))
        .reshape(tok_rows, head_width)
        .astype(jnp.bfloat16)
    )
    return (stream_next, attended)


def lightning_local(lin_query, lin_key, lin_value, log_decay):
    tok_rows = lin_query.shape[0]
    heads_here = log_decay.shape[1]
    nblocks = tok_rows // BLOCK
    shape4 = (tok_rows, heads_here, DH)
    q4, k4, v4 = (x.reshape(shape4) for x in (lin_query, lin_key, lin_value))
    state = jnp.zeros((heads_here, DH, DH), jnp.float32)
    outs = []
    for blk in range(nblocks):
        rows = slice(blk * BLOCK, (blk + 1) * BLOCK)
        state, out = lightning_block(state, (q4[rows], k4[rows], v4[rows], log_decay[rows]))
        outs.append(out)
    local_out = jnp.concatenate(outs, axis=0)
    decay_total = jnp.sum(log_decay, axis=0)
    pad_rows = 16
    total_rows = jnp.broadcast_to(decay_total[:, None, None], (heads_here, pad_rows, DH))
    packed = jnp.concatenate([state, total_rows], axis=1).astype(jnp.bfloat16)
    gathered = lax.all_gather(packed[None], "seq", axis=0, tiled=True)
    gathered = gathered.astype(jnp.float32)
    states = gathered[:, :, :DH, :]
    totals = gathered[:, :, DH, 0]
    position = lax.axis_index("seq")
    device_order = jnp.arange(totals.shape[0])
    earlier = (device_order < position)[:, None]
    before = jnp.sum(jnp.where(earlier, totals, 0.0), axis=0)
    inclusive = jnp.cumsum(totals, axis=0)
    factors = jnp.where(earlier, jnp.exp(jnp.where(earlier, before[None, :] - inclusive, 0.0)), 0.0)
    incoming = jnp.einsum("jh,jhde->hde", factors, states, precision=lax.Precision.HIGHEST)
    running = jnp.cumsum(log_decay, axis=0)
    query_f = q4.astype(jnp.float32) * jnp.exp(running)[:, :, None]
    carried = jnp.einsum("thd,hde->the", query_f, incoming, precision=lax.Precision.HIGHEST)
    lin_raw = local_out + carried
    lin_out = (
        (lin_raw * lax.rsqrt(jnp.mean(lin_raw * lin_raw, axis=-1, keepdims=True) + 1e-06))
        .astype(jnp.bfloat16)
        .reshape(tok_rows, heads_here * DH)
    )
    return lin_out


def heads_reduce_scatter(part, n_heads):
    if n_heads != 4:
        return lax.psum_scatter(part, "heads", scatter_dimension=0, tiled=True).astype(jnp.float32)
    mine = lax.axis_index("heads")
    core = mine % 2
    chip = mine // 2
    rows = part.shape[0] // n_heads
    grid = part.reshape(2, 2, rows, part.shape[1])
    keep1 = lax.dynamic_index_in_dim(grid, core, axis=1, keepdims=False)
    send1 = lax.dynamic_index_in_dim(grid, 1 - core, axis=1, keepdims=False)
    recv1 = lax.ppermute(send1, "heads", [(i, i ^ 1) for i in range(n_heads)])
    chip_sum = keep1.astype(jnp.float32) + recv1.astype(jnp.float32)
    keep2 = lax.dynamic_index_in_dim(chip_sum, chip, axis=0, keepdims=False)
    send2 = lax.dynamic_index_in_dim(chip_sum, 1 - chip, axis=0, keepdims=False)
    recv2 = lax.ppermute(send2.astype(jnp.bfloat16), "heads", [(i, i ^ 2) for i in range(n_heads)])
    return keep2 + recv2.astype(jnp.float32)


def attend_block(queries, query_pos, state_in, kv_block, key_start):
    old_max, row_total, weighted = state_in
    key_count = kv_block.shape[0]
    key_part = kv_block[:, :DH]
    value_part = kv_block[:, DH:]
    score_scale = float(DH) ** (-0.5)
    scores = (
        jnp.einsum("thd,sd->hts", queries, key_part, preferred_element_type=jnp.float32)
        * score_scale
    )
    key_pos = key_start + jnp.arange(key_count)
    allowed = ((key_pos[None, :] <= query_pos[:, None]) & (key_pos[None, :] >= 0))[None, :, :]
    scores = jnp.where(allowed, scores, -1e30)
    new_max = jnp.maximum(old_max, jnp.max(scores, axis=-1))
    expos = jnp.where(allowed, jnp.exp(scores - new_max[:, :, None]), 0.0)
    rescale = jnp.exp(old_max - new_max)
    row_total = row_total * rescale + jnp.sum(expos, axis=-1)
    prob_bf16 = expos.astype(jnp.bfloat16)
    weighted = weighted * rescale[:, :, None] + jnp.einsum(
        "hts,sd->htd", prob_bf16, value_part, preferred_element_type=jnp.float32
    )
    return (new_max, row_total, weighted)


def shards_fast(*args):
    return shards_fast_body(*args)


def shards_fast_body(
    lin_query, lin_key, lin_value, log_decay, stream, out_weight, norm_gain, query_weight, kv_weight
):
    n_heads = lax.axis_size("heads")
    n_seq = lax.axis_size("seq")
    tok_rows = lin_query.shape[0]
    heads_here = log_decay.shape[1]
    head_width = heads_here * DH
    mine_a = lax.axis_index("heads")
    mine_b = lax.axis_index("seq")
    swap = [(x * n_seq + y, y * n_seq + x) for x in range(n_heads) for y in range(n_seq)]
    gain_rows = jnp.broadcast_to(norm_gain[None, :], (16, norm_gain.shape[0]))
    packed = lax.ppermute(
        jnp.concatenate([stream, gain_rows], axis=0), ("heads", "seq"), swap
    )
    stream_t = packed[:tok_rows]
    gain_b = packed[tok_rows]

    lin_out = lightning_local(lin_query, lin_key, lin_value, log_decay)
    halves = []
    half_rows = tok_rows // 2
    for half in range(2):
        lin_all = lax.all_gather(
            lin_out[half * half_rows : (half + 1) * half_rows], "seq", axis=0, tiled=True
        )
        part = jnp.dot(lin_all, out_weight, preferred_element_type=jnp.float32)
        halves.append(heads_reduce_scatter(part.astype(jnp.bfloat16), n_heads))
    own_sum = jnp.concatenate(halves, axis=0)
    mixed_sum = stream_t.astype(jnp.float32) + own_sum
    stream_next = lax.ppermute(mixed_sum.astype(jnp.bfloat16), ("heads", "seq"), swap)
    total_sq = lax.psum(jnp.sum(mixed_sum * mixed_sum, axis=1), "seq")
    normed = (
        mixed_sum
        * lax.rsqrt(total_sq / D + 1e-05)[:, None]
        * gain_b.astype(jnp.float32)[None, :]
    ).astype(jnp.bfloat16)
    normed_all = lax.all_gather(normed, "heads", axis=0, tiled=True)
    kv_group = mine_a * heads_here // (QUERY_HEADS // KVH)
    kv_mine = lax.dynamic_index_in_dim(kv_weight, kv_group, 0, keepdims=False)
    q_part = jnp.dot(normed_all, query_weight, preferred_element_type=jnp.float32)
    kv_part = jnp.dot(normed_all, kv_mine, preferred_element_type=jnp.float32)
    queries = lax.psum_scatter(q_part.astype(jnp.bfloat16), "seq", scatter_dimension=0, tiled=True)
    queries = queries.reshape(tok_rows, heads_here, DH)
    kv_own = lax.psum_scatter(kv_part.astype(jnp.bfloat16), "seq", scatter_dimension=0, tiled=True)
    query_pos = mine_b * tok_rows + jnp.arange(tok_rows)
    state = (
        jnp.full((heads_here, tok_rows), -1e30, jnp.float32),
        jnp.zeros((heads_here, tok_rows), jnp.float32),
        jnp.zeros((heads_here, tok_rows, DH), jnp.float32),
    )
    earlier_kv = [from_behind(kv_own, "seq", dist) for dist in range(1, n_seq)]
    state = attend_block(queries, query_pos, state, kv_own, mine_b * tok_rows)
    for dist in range(1, n_seq):
        key_start = (mine_b - dist) * tok_rows
        state = attend_block(queries, query_pos, state, earlier_kv[dist - 1], key_start)
    _, row_total, weighted = state
    attended = (
        jnp.transpose(weighted / row_total[:, :, None], (1, 0, 2))
        .reshape(tok_rows, head_width)
        .astype(jnp.bfloat16)
    )
    return (stream_next, attended)


def solution(mesh):
    n_heads = mesh.shape["heads"]
    n_seq = mesh.shape["seq"]
    fast_ok = n_heads == n_seq and QUERY_HEADS % n_heads == 0
    if fast_ok:
        heads_here = QUERY_HEADS // n_heads
        fast_ok = (QUERY_HEADS // KVH) % heads_here == 0 and D % n_seq == 0
    shards = shards_fast if fast_ok else shards_base

    return jax.shard_map(
        shards,
        mesh=mesh,
        in_specs=(
            P(("groups", "seq"), "heads"),
            P(("groups", "seq"), "heads"),
            P(("groups", "seq"), "heads"),
            P(("groups", "seq"), "heads"),
            P(("groups", "seq"), "heads"),
            P("heads", "seq"),
            P("heads"),
            P("seq", "heads"),
            P(None, "seq", None),
        ),
        out_specs=(P(("groups", "seq"), "heads"), P(("groups", "seq"), "heads")),
        check_vma=False,
    )
```

```python
import jax
import jax.numpy as jnp
from jax import lax
from jax.sharding import PartitionSpec as P

D = 6144
QUERY_HEADS = 32
KVH = 4
DH = 128
BLOCK = 256


def from_behind(value, axis, steps):
    count = lax.axis_size(axis)
    leading, last = (max(0, -steps), min(count, count - steps))
    return lax.ppermute(value, axis, [(source, source + steps) for source in range(leading, last)])


def lightning_block(kv_state, block_inputs):
    query_blk, key_blk, value_blk, decay_blk = block_inputs
    block_len = query_blk.shape[0]
    local_cum = jnp.cumsum(decay_blk, axis=0)
    causal_mask = (jnp.arange(block_len)[:, None] >= jnp.arange(block_len)[None, :])[:, :, None]
    decay_diff = local_cum[:, None, :] - local_cum[None, :, :]
    decays = jnp.where(causal_mask, jnp.exp(jnp.where(causal_mask, decay_diff, 0.0)), 0.0)
    scores = jnp.einsum("thd,shd->hts", query_blk, key_blk, preferred_element_type=jnp.float32)
    weights = (scores * jnp.transpose(decays, (2, 0, 1))).astype(jnp.bfloat16)
    intra_out = jnp.einsum("hts,shd->thd", weights, value_blk, preferred_element_type=jnp.float32)
    query_f = query_blk.astype(jnp.float32)
    inter_out = jnp.einsum(
        "thd,hde->the",
        query_f * jnp.exp(local_cum)[:, :, None],
        kv_state,
        precision=lax.Precision.HIGHEST,
    )
    tail_decay = jnp.exp(local_cum[-1][None, :] - local_cum)
    key_f = key_blk.astype(jnp.float32) * tail_decay[:, :, None]
    kv_state = jnp.exp(local_cum[-1])[:, None, None] * kv_state + jnp.einsum(
        "shd,she->hde", key_f, value_blk.astype(jnp.float32), precision=lax.Precision.HIGHEST
    )
    return (kv_state, intra_out + inter_out)


def shards_base(
    lin_query, lin_key, lin_value, log_decay, stream, out_weight, norm_gain, query_weight, kv_weight
):
    tok_rows = lin_query.shape[0]
    heads_here = log_decay.shape[1]
    head_width = heads_here * DH
    nblocks = tok_rows // BLOCK
    block_shape = (nblocks, BLOCK, heads_here, DH)
    inputs = (
        lin_query.reshape(block_shape),
        lin_key.reshape(block_shape),
        lin_value.reshape(block_shape),
        log_decay.reshape(nblocks, BLOCK, heads_here),
    )
    start_state = jnp.zeros((heads_here, DH, DH), jnp.float32)
    local_state, local_out = lax.scan(lightning_block, start_state, inputs)
    local_out = local_out.reshape(tok_rows, heads_here, DH)
    decay_total = jnp.sum(log_decay, axis=0)
    totals, states = (
        lax.all_gather(decay_total[None].astype(jnp.bfloat16), "seq", axis=0, tiled=True).astype(
            jnp.float32
        ),
        lax.all_gather(local_state[None].astype(jnp.bfloat16), "seq", axis=0, tiled=True).astype(
            jnp.float32
        ),
    )
    position = lax.axis_index("seq")
    device_order = jnp.arange(totals.shape[0])
    earlier = (device_order < position)[:, None]
    before = jnp.sum(jnp.where(earlier, totals, 0.0), axis=0)
    inclusive = jnp.cumsum(totals, axis=0)
    factors = jnp.where(earlier, jnp.exp(jnp.where(earlier, before[None, :] - inclusive, 0.0)), 0.0)
    incoming = jnp.einsum("jh,jhde->hde", factors, states, precision=lax.Precision.HIGHEST)
    running = jnp.cumsum(log_decay, axis=0)
    query_f = (
        lin_query.reshape(tok_rows, heads_here, DH).astype(jnp.float32)
        * jnp.exp(running)[:, :, None]
    )
    carried = jnp.einsum("thd,hde->the", query_f, incoming, precision=lax.Precision.HIGHEST)
    lin_raw = local_out + carried
    lin_out = (
        (lin_raw * lax.rsqrt(jnp.mean(lin_raw * lin_raw, axis=-1, keepdims=True) + 1e-06))
        .astype(jnp.bfloat16)
        .reshape(tok_rows, head_width)
    )
    branch = jnp.dot(
        lin_out,
        lax.all_gather(out_weight, "seq", axis=1, tiled=True),
        preferred_element_type=jnp.float32,
    )
    kv_group = lax.axis_index("heads") * heads_here // (QUERY_HEADS // KVH)
    kv_mine = lax.dynamic_index_in_dim(kv_weight, kv_group, 0, keepdims=False)
    query_rows, kv_rows = (
        lax.all_gather(query_weight, "seq", axis=0, tiled=True),
        lax.all_gather(kv_mine, "seq", axis=0, tiled=True),
    )
    projection = jnp.concatenate([query_rows, kv_rows], axis=1)
    own_sum = lax.psum_scatter(
        branch.astype(jnp.bfloat16), "heads", scatter_dimension=1, tiled=True
    ).astype(jnp.float32)
    mixed_sum = stream.astype(jnp.float32) + own_sum
    stream_next = mixed_sum.astype(jnp.bfloat16)
    total_sq = lax.psum(jnp.sum(mixed_sum * mixed_sum, axis=1), "heads")
    normed = (
        mixed_sum
        * lax.rsqrt(total_sq / D + 1e-05)[:, None]
        * norm_gain.astype(jnp.float32)[None, :]
    ).astype(jnp.bfloat16)
    projected = jnp.dot(
        lax.all_gather(normed, "heads", axis=1, tiled=True),
        projection,
        preferred_element_type=jnp.float32,
    )
    projected = projected.astype(jnp.bfloat16)
    queries = projected[:, :head_width].reshape(tok_rows, heads_here, DH)
    keys_values = projected[:, head_width:]
    position = lax.axis_index("seq")
    query_pos = position * tok_rows + jnp.arange(tok_rows)
    score_scale = float(DH) ** (-0.5)

    def attend(state_in, kv_block, key_start):
        old_max, row_total, weighted = state_in
        key_count = kv_block.shape[0]
        key_part = kv_block[:, :DH]
        value_part = kv_block[:, DH:]
        scores = (
            jnp.einsum("thd,sd->hts", queries, key_part, preferred_element_type=jnp.float32)
            * score_scale
        )
        key_pos = key_start + jnp.arange(key_count)
        allowed = ((key_pos[None, :] <= query_pos[:, None]) & (key_pos[None, :] >= 0))[None, :, :]
        scores = jnp.where(allowed, scores, -1e30)
        new_max = jnp.maximum(old_max, jnp.max(scores, axis=-1))
        expos = jnp.where(allowed, jnp.exp(scores - new_max[:, :, None]), 0.0)
        rescale = jnp.exp(old_max - new_max)
        row_total = row_total * rescale + jnp.sum(expos, axis=-1)
        prob_bf16 = expos.astype(jnp.bfloat16)
        weighted = weighted * rescale[:, :, None] + jnp.einsum(
            "hts,sd->htd", prob_bf16, value_part, preferred_element_type=jnp.float32
        )
        return (new_max, row_total, weighted)

    initial = (
        jnp.full((heads_here, tok_rows), -1e30, jnp.float32),
        jnp.zeros((heads_here, tok_rows), jnp.float32),
        jnp.zeros((heads_here, tok_rows, DH), jnp.float32),
    )
    first_state = attend(initial, keys_values, position * tok_rows)
    seq_count = lax.axis_size("seq")

    def cycle_turn(turn_index, loop_state):
        moving, inner_state = loop_state
        moving = from_behind(moving, "seq", 1)
        source = position - turn_index
        return (moving, attend(inner_state, moving, source * tok_rows))

    _, final_state = lax.fori_loop(1, seq_count, cycle_turn, (keys_values, first_state))
    _, row_total, weighted = final_state
    attended = (
        jnp.transpose(weighted / row_total[:, :, None], (1, 0, 2))
        .reshape(tok_rows, head_width)
        .astype(jnp.bfloat16)
    )
    return (stream_next, attended)


def lightning_local(lin_query, lin_key, lin_value, log_decay):
    tok_rows = lin_query.shape[0]
    heads_here = log_decay.shape[1]
    nblocks = tok_rows // BLOCK
    shape4 = (tok_rows, heads_here, DH)
    q4, k4, v4 = (x.reshape(shape4) for x in (lin_query, lin_key, lin_value))
    state = jnp.zeros((heads_here, DH, DH), jnp.float32)
    outs = []
    for blk in range(nblocks):
        rows = slice(blk * BLOCK, (blk + 1) * BLOCK)
        state, out = lightning_block(state, (q4[rows], k4[rows], v4[rows], log_decay[rows]))
        outs.append(out)
    local_out = jnp.concatenate(outs, axis=0)
    decay_total = jnp.sum(log_decay, axis=0)
    pad_rows = 16
    total_rows = jnp.broadcast_to(decay_total[:, None, None], (heads_here, pad_rows, DH))
    packed = jnp.concatenate([state, total_rows], axis=1).astype(jnp.bfloat16)
    gathered = lax.all_gather(packed[None], "seq", axis=0, tiled=True)
    gathered = gathered.astype(jnp.float32)
    states = gathered[:, :, :DH, :]
    totals = gathered[:, :, DH, 0]
    position = lax.axis_index("seq")
    device_order = jnp.arange(totals.shape[0])
    earlier = (device_order < position)[:, None]
    before = jnp.sum(jnp.where(earlier, totals, 0.0), axis=0)
    inclusive = jnp.cumsum(totals, axis=0)
    factors = jnp.where(earlier, jnp.exp(jnp.where(earlier, before[None, :] - inclusive, 0.0)), 0.0)
    incoming = jnp.einsum("jh,jhde->hde", factors, states, precision=lax.Precision.HIGHEST)
    running = jnp.cumsum(log_decay, axis=0)
    query_f = q4.astype(jnp.float32) * jnp.exp(running)[:, :, None]
    carried = jnp.einsum("thd,hde->the", query_f, incoming, precision=lax.Precision.HIGHEST)
    lin_raw = local_out + carried
    lin_out = (
        (lin_raw * lax.rsqrt(jnp.mean(lin_raw * lin_raw, axis=-1, keepdims=True) + 1e-06))
        .astype(jnp.bfloat16)
        .reshape(tok_rows, heads_here * DH)
    )
    return lin_out


def heads_reduce_scatter(part, n_heads):
    if n_heads != 4:
        return lax.psum_scatter(part, "heads", scatter_dimension=0, tiled=True).astype(jnp.float32)
    mine = lax.axis_index("heads")
    core = mine % 2
    chip = mine // 2
    rows = part.shape[0] // n_heads
    grid = part.reshape(2, 2, rows, part.shape[1])
    keep1 = lax.dynamic_index_in_dim(grid, core, axis=1, keepdims=False)
    send1 = lax.dynamic_index_in_dim(grid, 1 - core, axis=1, keepdims=False)
    recv1 = lax.ppermute(send1, "heads", [(i, i ^ 1) for i in range(n_heads)])
    chip_sum = keep1.astype(jnp.float32) + recv1.astype(jnp.float32)
    keep2 = lax.dynamic_index_in_dim(chip_sum, chip, axis=0, keepdims=False)
    send2 = lax.dynamic_index_in_dim(chip_sum, 1 - chip, axis=0, keepdims=False)
    recv2 = lax.ppermute(send2.astype(jnp.bfloat16), "heads", [(i, i ^ 2) for i in range(n_heads)])
    return keep2 + recv2.astype(jnp.float32)


def attend_block(queries, query_pos, state_in, kv_block, key_start):
    old_max, row_total, weighted = state_in
    key_count = kv_block.shape[0]
    key_part = kv_block[:, :DH]
    value_part = kv_block[:, DH:]
    score_scale = float(DH) ** (-0.5)
    scores = (
        jnp.einsum("thd,sd->hts", queries, key_part, preferred_element_type=jnp.float32)
        * score_scale
    )
    key_pos = key_start + jnp.arange(key_count)
    allowed = ((key_pos[None, :] <= query_pos[:, None]) & (key_pos[None, :] >= 0))[None, :, :]
    scores = jnp.where(allowed, scores, -1e30)
    new_max = jnp.maximum(old_max, jnp.max(scores, axis=-1))
    expos = jnp.where(allowed, jnp.exp(scores - new_max[:, :, None]), 0.0)
    rescale = jnp.exp(old_max - new_max)
    row_total = row_total * rescale + jnp.sum(expos, axis=-1)
    prob_bf16 = expos.astype(jnp.bfloat16)
    weighted = weighted * rescale[:, :, None] + jnp.einsum(
        "hts,sd->htd", prob_bf16, value_part, preferred_element_type=jnp.float32
    )
    return (new_max, row_total, weighted)


def shards_fast(*args):
    return shards_fast_body(*args)


def shards_fast_body(
    lin_query, lin_key, lin_value, log_decay, stream, out_weight, norm_gain, query_weight, kv_weight
):
    n_heads = lax.axis_size("heads")
    n_seq = lax.axis_size("seq")
    tok_rows = lin_query.shape[0]
    heads_here = log_decay.shape[1]
    mine_a = lax.axis_index("heads")
    mine_b = lax.axis_index("seq")
    swap = [(x * n_seq + y, y * n_seq + x) for x in range(n_heads) for y in range(n_seq)]
    gain_rows = jnp.broadcast_to(norm_gain[None, :], (16, norm_gain.shape[0]))
    packed = lax.ppermute(
        jnp.concatenate([stream, gain_rows], axis=0), ("heads", "seq"), swap
    )
    stream_t = packed[:tok_rows]
    gain_b = packed[tok_rows]

    lin_out = lightning_local(lin_query, lin_key, lin_value, log_decay)
    halves = []
    half_rows = tok_rows // 2
    for half in range(2):
        lin_all = lax.all_gather(
            lin_out[half * half_rows : (half + 1) * half_rows], "seq", axis=0, tiled=True
        )
        part = jnp.dot(lin_all, out_weight, preferred_element_type=jnp.float32)
        halves.append(heads_reduce_scatter(part.astype(jnp.bfloat16), n_heads))
    own_sum = jnp.concatenate(halves, axis=0)
    mixed_sum = stream_t.astype(jnp.float32) + own_sum
    next_t = mixed_sum.astype(jnp.bfloat16)
    next_early = lax.ppermute(next_t[:half_rows], ("heads", "seq"), swap)
    next_late = lax.ppermute(next_t[half_rows:], ("heads", "seq"), swap)
    stream_next = jnp.concatenate([next_early, next_late], axis=0)
    total_sq = lax.psum(jnp.sum(mixed_sum * mixed_sum, axis=1), "seq")
    normed = (
        mixed_sum
        * lax.rsqrt(total_sq / D + 1e-05)[:, None]
        * gain_b.astype(jnp.float32)[None, :]
    ).astype(jnp.bfloat16)
    normed_all = lax.all_gather(normed, "heads", axis=0, tiled=True)
    kv_group = mine_a * heads_here // (QUERY_HEADS // KVH)
    kv_mine = lax.dynamic_index_in_dim(kv_weight, kv_group, 0, keepdims=False)
    q_part = jnp.dot(normed_all, query_weight, preferred_element_type=jnp.float32)
    kv_part = jnp.dot(normed_all, kv_mine, preferred_element_type=jnp.float32)
    kv_own = lax.psum_scatter(kv_part.astype(jnp.bfloat16), "seq", scatter_dimension=0, tiled=True)
    earlier_kv = [from_behind(kv_own, "seq", dist) for dist in range(1, n_seq)]
    query_pos = mine_b * tok_rows + jnp.arange(tok_rows)
    q_groups = 2 if heads_here % 2 == 0 else 1
    group_heads = heads_here // q_groups
    group_width = group_heads * DH
    pieces = []
    for group in range(q_groups):
        q_cols = q_part[:, group * group_width : (group + 1) * group_width]
        queries = lax.psum_scatter(
            q_cols.astype(jnp.bfloat16), "seq", scatter_dimension=0, tiled=True
        )
        queries = queries.reshape(tok_rows, group_heads, DH)
        state = (
            jnp.full((group_heads, tok_rows), -1e30, jnp.float32),
            jnp.zeros((group_heads, tok_rows), jnp.float32),
            jnp.zeros((group_heads, tok_rows, DH), jnp.float32),
        )
        state = attend_block(queries, query_pos, state, kv_own, mine_b * tok_rows)
        for dist in range(1, n_seq):
            key_start = (mine_b - dist) * tok_rows
            state = attend_block(queries, query_pos, state, earlier_kv[dist - 1], key_start)
        _, row_total, weighted = state
        pieces.append(
            jnp.transpose(weighted / row_total[:, :, None], (1, 0, 2))
            .reshape(tok_rows, group_width)
            .astype(jnp.bfloat16)
        )
    attended = jnp.concatenate(pieces, axis=1)
    return (stream_next, attended)


def solution(mesh):
    n_heads = mesh.shape["heads"]
    n_seq = mesh.shape["seq"]
    fast_ok = n_heads == n_seq and QUERY_HEADS % n_heads == 0
    if fast_ok:
        heads_here = QUERY_HEADS // n_heads
        fast_ok = (QUERY_HEADS // KVH) % heads_here == 0 and D % n_seq == 0
    shards = shards_fast if fast_ok else shards_base

    return jax.shard_map(
        shards,
        mesh=mesh,
        in_specs=(
            P(("groups", "seq"), "heads"),
            P(("groups", "seq"), "heads"),
            P(("groups", "seq"), "heads"),
            P(("groups", "seq"), "heads"),
            P(("groups", "seq"), "heads"),
            P("heads", "seq"),
            P("heads"),
            P("seq", "heads"),
            P(None, "seq", None),
        ),
        out_specs=(P(("groups", "seq"), "heads"), P(("groups", "seq"), "heads")),
        check_vma=False,
    )
```

```python
import jax
import jax.numpy as jnp
from jax import lax
from jax.experimental import pallas as pl
from jax.experimental.pallas import tpu as pltpu
from jax.sharding import PartitionSpec as P

D = 6144
QUERY_HEADS = 32
KVH = 4
DH = 128
BLOCK = 256


def from_behind(value, axis, steps):
    count = lax.axis_size(axis)
    leading, last = (max(0, -steps), min(count, count - steps))
    return lax.ppermute(value, axis, [(source, source + steps) for source in range(leading, last)])


def lightning_block(kv_state, block_inputs):
    query_blk, key_blk, value_blk, decay_blk = block_inputs
    block_len = query_blk.shape[0]
    local_cum = jnp.cumsum(decay_blk, axis=0)
    causal_mask = (jnp.arange(block_len)[:, None] >= jnp.arange(block_len)[None, :])[:, :, None]
    decay_diff = local_cum[:, None, :] - local_cum[None, :, :]
    decays = jnp.where(causal_mask, jnp.exp(jnp.where(causal_mask, decay_diff, 0.0)), 0.0)
    scores = jnp.einsum("thd,shd->hts", query_blk, key_blk, preferred_element_type=jnp.float32)
    weights = (scores * jnp.transpose(decays, (2, 0, 1))).astype(jnp.bfloat16)
    intra_out = jnp.einsum("hts,shd->thd", weights, value_blk, preferred_element_type=jnp.float32)
    query_f = query_blk.astype(jnp.float32)
    inter_out = jnp.einsum(
        "thd,hde->the",
        query_f * jnp.exp(local_cum)[:, :, None],
        kv_state,
        precision=lax.Precision.HIGHEST,
    )
    tail_decay = jnp.exp(local_cum[-1][None, :] - local_cum)
    key_f = key_blk.astype(jnp.float32) * tail_decay[:, :, None]
    kv_state = jnp.exp(local_cum[-1])[:, None, None] * kv_state + jnp.einsum(
        "shd,she->hde", key_f, value_blk.astype(jnp.float32), precision=lax.Precision.HIGHEST
    )
    return (kv_state, intra_out + inter_out)


def shards_base(
    lin_query, lin_key, lin_value, log_decay, stream, out_weight, norm_gain, query_weight, kv_weight
):
    tok_rows = lin_query.shape[0]
    heads_here = log_decay.shape[1]
    head_width = heads_here * DH
    nblocks = tok_rows // BLOCK
    block_shape = (nblocks, BLOCK, heads_here, DH)
    inputs = (
        lin_query.reshape(block_shape),
        lin_key.reshape(block_shape),
        lin_value.reshape(block_shape),
        log_decay.reshape(nblocks, BLOCK, heads_here),
    )
    start_state = jnp.zeros((heads_here, DH, DH), jnp.float32)
    local_state, local_out = lax.scan(lightning_block, start_state, inputs)
    local_out = local_out.reshape(tok_rows, heads_here, DH)
    decay_total = jnp.sum(log_decay, axis=0)
    totals, states = (
        lax.all_gather(decay_total[None].astype(jnp.bfloat16), "seq", axis=0, tiled=True).astype(
            jnp.float32
        ),
        lax.all_gather(local_state[None].astype(jnp.bfloat16), "seq", axis=0, tiled=True).astype(
            jnp.float32
        ),
    )
    position = lax.axis_index("seq")
    device_order = jnp.arange(totals.shape[0])
    earlier = (device_order < position)[:, None]
    before = jnp.sum(jnp.where(earlier, totals, 0.0), axis=0)
    inclusive = jnp.cumsum(totals, axis=0)
    factors = jnp.where(earlier, jnp.exp(jnp.where(earlier, before[None, :] - inclusive, 0.0)), 0.0)
    incoming = jnp.einsum("jh,jhde->hde", factors, states, precision=lax.Precision.HIGHEST)
    running = jnp.cumsum(log_decay, axis=0)
    query_f = (
        lin_query.reshape(tok_rows, heads_here, DH).astype(jnp.float32)
        * jnp.exp(running)[:, :, None]
    )
    carried = jnp.einsum("thd,hde->the", query_f, incoming, precision=lax.Precision.HIGHEST)
    lin_raw = local_out + carried
    lin_out = (
        (lin_raw * lax.rsqrt(jnp.mean(lin_raw * lin_raw, axis=-1, keepdims=True) + 1e-06))
        .astype(jnp.bfloat16)
        .reshape(tok_rows, head_width)
    )
    branch = jnp.dot(
        lin_out,
        lax.all_gather(out_weight, "seq", axis=1, tiled=True),
        preferred_element_type=jnp.float32,
    )
    kv_group = lax.axis_index("heads") * heads_here // (QUERY_HEADS // KVH)
    kv_mine = lax.dynamic_index_in_dim(kv_weight, kv_group, 0, keepdims=False)
    query_rows, kv_rows = (
        lax.all_gather(query_weight, "seq", axis=0, tiled=True),
        lax.all_gather(kv_mine, "seq", axis=0, tiled=True),
    )
    projection = jnp.concatenate([query_rows, kv_rows], axis=1)
    own_sum = lax.psum_scatter(
        branch.astype(jnp.bfloat16), "heads", scatter_dimension=1, tiled=True
    ).astype(jnp.float32)
    mixed_sum = stream.astype(jnp.float32) + own_sum
    stream_next = mixed_sum.astype(jnp.bfloat16)
    total_sq = lax.psum(jnp.sum(mixed_sum * mixed_sum, axis=1), "heads")
    normed = (
        mixed_sum
        * lax.rsqrt(total_sq / D + 1e-05)[:, None]
        * norm_gain.astype(jnp.float32)[None, :]
    ).astype(jnp.bfloat16)
    projected = jnp.dot(
        lax.all_gather(normed, "heads", axis=1, tiled=True),
        projection,
        preferred_element_type=jnp.float32,
    )
    projected = projected.astype(jnp.bfloat16)
    queries = projected[:, :head_width].reshape(tok_rows, heads_here, DH)
    keys_values = projected[:, head_width:]
    position = lax.axis_index("seq")
    query_pos = position * tok_rows + jnp.arange(tok_rows)
    score_scale = float(DH) ** (-0.5)

    def attend(state_in, kv_block, key_start):
        old_max, row_total, weighted = state_in
        key_count = kv_block.shape[0]
        key_part = kv_block[:, :DH]
        value_part = kv_block[:, DH:]
        scores = (
            jnp.einsum("thd,sd->hts", queries, key_part, preferred_element_type=jnp.float32)
            * score_scale
        )
        key_pos = key_start + jnp.arange(key_count)
        allowed = ((key_pos[None, :] <= query_pos[:, None]) & (key_pos[None, :] >= 0))[None, :, :]
        scores = jnp.where(allowed, scores, -1e30)
        new_max = jnp.maximum(old_max, jnp.max(scores, axis=-1))
        expos = jnp.where(allowed, jnp.exp(scores - new_max[:, :, None]), 0.0)
        rescale = jnp.exp(old_max - new_max)
        row_total = row_total * rescale + jnp.sum(expos, axis=-1)
        prob_bf16 = expos.astype(jnp.bfloat16)
        weighted = weighted * rescale[:, :, None] + jnp.einsum(
            "hts,sd->htd", prob_bf16, value_part, preferred_element_type=jnp.float32
        )
        return (new_max, row_total, weighted)

    initial = (
        jnp.full((heads_here, tok_rows), -1e30, jnp.float32),
        jnp.zeros((heads_here, tok_rows), jnp.float32),
        jnp.zeros((heads_here, tok_rows, DH), jnp.float32),
    )
    first_state = attend(initial, keys_values, position * tok_rows)
    seq_count = lax.axis_size("seq")

    def cycle_turn(turn_index, loop_state):
        moving, inner_state = loop_state
        moving = from_behind(moving, "seq", 1)
        source = position - turn_index
        return (moving, attend(inner_state, moving, source * tok_rows))

    _, final_state = lax.fori_loop(1, seq_count, cycle_turn, (keys_values, first_state))
    _, row_total, weighted = final_state
    attended = (
        jnp.transpose(weighted / row_total[:, :, None], (1, 0, 2))
        .reshape(tok_rows, head_width)
        .astype(jnp.bfloat16)
    )
    return (stream_next, attended)


def lightning_local(lin_query, lin_key, lin_value, log_decay):
    tok_rows = lin_query.shape[0]
    heads_here = log_decay.shape[1]
    nblocks = tok_rows // BLOCK
    shape4 = (tok_rows, heads_here, DH)
    q4, k4, v4 = (x.reshape(shape4) for x in (lin_query, lin_key, lin_value))
    state = jnp.zeros((heads_here, DH, DH), jnp.float32)
    outs = []
    for blk in range(nblocks):
        rows = slice(blk * BLOCK, (blk + 1) * BLOCK)
        state, out = lightning_block(state, (q4[rows], k4[rows], v4[rows], log_decay[rows]))
        outs.append(out)
    local_out = jnp.concatenate(outs, axis=0)
    decay_total = jnp.sum(log_decay, axis=0)
    pad_rows = 16
    total_rows = jnp.broadcast_to(decay_total[:, None, None], (heads_here, pad_rows, DH))
    packed = jnp.concatenate([state, total_rows], axis=1).astype(jnp.bfloat16)
    gathered = lax.all_gather(packed[None], "seq", axis=0, tiled=True)
    gathered = gathered.astype(jnp.float32)
    states = gathered[:, :, :DH, :]
    totals = gathered[:, :, DH, 0]
    position = lax.axis_index("seq")
    device_order = jnp.arange(totals.shape[0])
    earlier = (device_order < position)[:, None]
    before = jnp.sum(jnp.where(earlier, totals, 0.0), axis=0)
    inclusive = jnp.cumsum(totals, axis=0)
    factors = jnp.where(earlier, jnp.exp(jnp.where(earlier, before[None, :] - inclusive, 0.0)), 0.0)
    incoming = jnp.einsum("jh,jhde->hde", factors, states, precision=lax.Precision.HIGHEST)
    running = jnp.cumsum(log_decay, axis=0)
    query_f = q4.astype(jnp.float32) * jnp.exp(running)[:, :, None]
    carried = jnp.einsum("thd,hde->the", query_f, incoming, precision=lax.Precision.HIGHEST)
    lin_raw = local_out + carried
    lin_out = (
        (lin_raw * lax.rsqrt(jnp.mean(lin_raw * lin_raw, axis=-1, keepdims=True) + 1e-06))
        .astype(jnp.bfloat16)
        .reshape(tok_rows, heads_here * DH)
    )
    return lin_out


def heads_reduce_scatter(part, n_heads):
    if n_heads != 4:
        return lax.psum_scatter(part, "heads", scatter_dimension=0, tiled=True).astype(jnp.float32)
    mine = lax.axis_index("heads")
    core = mine % 2
    chip = mine // 2
    rows = part.shape[0] // n_heads
    grid = part.reshape(2, 2, rows, part.shape[1])
    keep1 = lax.dynamic_index_in_dim(grid, core, axis=1, keepdims=False)
    send1 = lax.dynamic_index_in_dim(grid, 1 - core, axis=1, keepdims=False)
    recv1 = lax.ppermute(send1, "heads", [(i, i ^ 1) for i in range(n_heads)])
    chip_sum = keep1.astype(jnp.float32) + recv1.astype(jnp.float32)
    keep2 = lax.dynamic_index_in_dim(chip_sum, chip, axis=0, keepdims=False)
    send2 = lax.dynamic_index_in_dim(chip_sum, 1 - chip, axis=0, keepdims=False)
    recv2 = lax.ppermute(send2.astype(jnp.bfloat16), "heads", [(i, i ^ 2) for i in range(n_heads)])
    return keep2 + recv2.astype(jnp.float32)


def attention_kernel(pos_ref, q_ref, kv_ref, o_ref, s_ref):
    position = pos_ref[0]
    n_blk = kv_ref.shape[0]
    rows = q_ref.shape[0]
    score_scale = float(DH) ** (-0.5)
    query = q_ref[...]
    row_id = lax.broadcasted_iota(jnp.int32, (rows, rows), 0)
    col_id = lax.broadcasted_iota(jnp.int32, (rows, rows), 1)

    def allowed_of(dist):
        if dist == 0:
            return col_id <= row_id
        return jnp.broadcast_to(dist <= position, (rows, rows))

    row_max = jnp.full((rows, 1), -1e30, jnp.float32)
    for dist in range(n_blk):
        key = kv_ref[dist, :, :DH]
        scores = lax.dot_general(
            query, key, (((1,), (1,)), ((), ())), preferred_element_type=jnp.float32
        ) * score_scale
        scores = jnp.where(allowed_of(dist), scores, -1e30)
        s_ref[dist] = scores
        row_max = jnp.maximum(row_max, jnp.max(scores, axis=1, keepdims=True))
    row_total = jnp.zeros((rows, 1), jnp.float32)
    weighted = jnp.zeros((rows, DH), jnp.float32)
    for dist in range(n_blk):
        expos = jnp.where(allowed_of(dist), jnp.exp(s_ref[dist] - row_max), 0.0)
        row_total = row_total + jnp.sum(expos, axis=1, keepdims=True)
        weighted = weighted + jnp.dot(
            expos.astype(jnp.bfloat16), kv_ref[dist, :, DH:], preferred_element_type=jnp.float32
        )
    o_ref[...] = (weighted / row_total).astype(o_ref.dtype)


def attention_pallas(queries, kv_stack, position):
    rows, width = queries.shape
    n_blk = kv_stack.shape[0]
    local_heads = width // DH
    flops = 4 * local_heads * n_blk * rows * rows * DH
    grid_spec = pltpu.PrefetchScalarGridSpec(
        num_scalar_prefetch=1,
        grid=(local_heads,),
        in_specs=[
            pl.BlockSpec((rows, DH), lambda h, pos: (0, h)),
            pl.BlockSpec((n_blk, rows, 2 * DH), lambda h, pos: (0, 0, 0)),
        ],
        out_specs=pl.BlockSpec((rows, DH), lambda h, pos: (0, h)),
        scratch_shapes=[pltpu.VMEM((n_blk, rows, rows), jnp.float32)],
    )
    return pl.pallas_call(
        attention_kernel,
        grid_spec=grid_spec,
        out_shape=jax.ShapeDtypeStruct((rows, width), jnp.bfloat16),
        compiler_params=pltpu.CompilerParams(dimension_semantics=("arbitrary",)),
        cost_estimate=pl.CostEstimate(
            flops=flops,
            transcendentals=local_heads * n_blk * rows * rows,
            bytes_accessed=2 * queries.size * 2 + kv_stack.size * 2,
        ),
    )(jnp.reshape(position, (1,)).astype(jnp.int32), queries, kv_stack)


def shards_fast(*args):
    return shards_fast_body(*args)


def shards_fast_body(
    lin_query, lin_key, lin_value, log_decay, stream, out_weight, norm_gain, query_weight, kv_weight
):
    n_heads = lax.axis_size("heads")
    n_seq = lax.axis_size("seq")
    tok_rows = lin_query.shape[0]
    heads_here = log_decay.shape[1]
    mine_a = lax.axis_index("heads")
    mine_b = lax.axis_index("seq")
    swap = [(x * n_seq + y, y * n_seq + x) for x in range(n_heads) for y in range(n_seq)]
    gain_rows = jnp.broadcast_to(norm_gain[None, :], (16, norm_gain.shape[0]))
    packed = lax.ppermute(
        jnp.concatenate([stream, gain_rows], axis=0), ("heads", "seq"), swap
    )
    stream_t = packed[:tok_rows]
    gain_b = packed[tok_rows]

    lin_out = lightning_local(lin_query, lin_key, lin_value, log_decay)
    halves = []
    half_rows = tok_rows // 2
    for half in range(2):
        lin_all = lax.all_gather(
            lin_out[half * half_rows : (half + 1) * half_rows], "seq", axis=0, tiled=True
        )
        part = jnp.dot(lin_all, out_weight, preferred_element_type=jnp.float32)
        halves.append(heads_reduce_scatter(part.astype(jnp.bfloat16), n_heads))
    own_sum = jnp.concatenate(halves, axis=0)
    mixed_sum = stream_t.astype(jnp.float32) + own_sum
    stream_next = lax.ppermute(mixed_sum.astype(jnp.bfloat16), ("heads", "seq"), swap)
    total_sq = lax.psum(jnp.sum(mixed_sum * mixed_sum, axis=1), "seq")
    normed = (
        mixed_sum
        * lax.rsqrt(total_sq / D + 1e-05)[:, None]
        * gain_b.astype(jnp.float32)[None, :]
    ).astype(jnp.bfloat16)
    normed_all = lax.all_gather(normed, "heads", axis=0, tiled=True)
    kv_group = mine_a * heads_here // (QUERY_HEADS // KVH)
    kv_mine = lax.dynamic_index_in_dim(kv_weight, kv_group, 0, keepdims=False)
    q_part = jnp.dot(normed_all, query_weight, preferred_element_type=jnp.float32)
    kv_part = jnp.dot(normed_all, kv_mine, preferred_element_type=jnp.float32)
    queries = lax.psum_scatter(
        q_part.astype(jnp.bfloat16), "seq", scatter_dimension=0, tiled=True
    )
    kv_own = lax.psum_scatter(kv_part.astype(jnp.bfloat16), "seq", scatter_dimension=0, tiled=True)
    earlier_kv = [from_behind(kv_own, "seq", dist) for dist in range(1, n_seq)]
    kv_stack = jnp.stack([kv_own] + earlier_kv, axis=0)
    attended = attention_pallas(queries, kv_stack, mine_b)
    return (stream_next, attended)


def solution(mesh):
    n_heads = mesh.shape["heads"]
    n_seq = mesh.shape["seq"]
    fast_ok = n_heads == n_seq and QUERY_HEADS % n_heads == 0
    if fast_ok:
        heads_here = QUERY_HEADS // n_heads
        fast_ok = (QUERY_HEADS // KVH) % heads_here == 0 and D % n_seq == 0
    shards = shards_fast if fast_ok else shards_base

    return jax.shard_map(
        shards,
        mesh=mesh,
        in_specs=(
            P(("groups", "seq"), "heads"),
            P(("groups", "seq"), "heads"),
            P(("groups", "seq"), "heads"),
            P(("groups", "seq"), "heads"),
            P(("groups", "seq"), "heads"),
            P("heads", "seq"),
            P("heads"),
            P("seq", "heads"),
            P(None, "seq", None),
        ),
        out_specs=(P(("groups", "seq"), "heads"), P(("groups", "seq"), "heads")),
        check_vma=False,
    )
```

```python
import jax
import jax.numpy as jnp
from jax import lax
from jax.experimental import pallas as pl
from jax.experimental.pallas import tpu as pltpu
from jax.sharding import PartitionSpec as P

D = 6144
QUERY_HEADS = 32
KVH = 4
DH = 128
BLOCK = 256


def from_behind(value, axis, steps):
    count = lax.axis_size(axis)
    leading, last = (max(0, -steps), min(count, count - steps))
    return lax.ppermute(value, axis, [(source, source + steps) for source in range(leading, last)])


def lightning_block(kv_state, block_inputs):
    query_blk, key_blk, value_blk, decay_blk = block_inputs
    block_len = query_blk.shape[0]
    local_cum = jnp.cumsum(decay_blk, axis=0)
    causal_mask = (jnp.arange(block_len)[:, None] >= jnp.arange(block_len)[None, :])[:, :, None]
    decay_diff = local_cum[:, None, :] - local_cum[None, :, :]
    decays = jnp.where(causal_mask, jnp.exp(jnp.where(causal_mask, decay_diff, 0.0)), 0.0)
    scores = jnp.einsum("thd,shd->hts", query_blk, key_blk, preferred_element_type=jnp.float32)
    weights = (scores * jnp.transpose(decays, (2, 0, 1))).astype(jnp.bfloat16)
    intra_out = jnp.einsum("hts,shd->thd", weights, value_blk, preferred_element_type=jnp.float32)
    query_f = query_blk.astype(jnp.float32)
    inter_out = jnp.einsum(
        "thd,hde->the",
        query_f * jnp.exp(local_cum)[:, :, None],
        kv_state,
        precision=lax.Precision.HIGHEST,
    )
    tail_decay = jnp.exp(local_cum[-1][None, :] - local_cum)
    key_f = key_blk.astype(jnp.float32) * tail_decay[:, :, None]
    kv_state = jnp.exp(local_cum[-1])[:, None, None] * kv_state + jnp.einsum(
        "shd,she->hde", key_f, value_blk.astype(jnp.float32), precision=lax.Precision.HIGHEST
    )
    return (kv_state, intra_out + inter_out)


def shards_base(
    lin_query, lin_key, lin_value, log_decay, stream, out_weight, norm_gain, query_weight, kv_weight
):
    tok_rows = lin_query.shape[0]
    heads_here = log_decay.shape[1]
    head_width = heads_here * DH
    nblocks = tok_rows // BLOCK
    block_shape = (nblocks, BLOCK, heads_here, DH)
    inputs = (
        lin_query.reshape(block_shape),
        lin_key.reshape(block_shape),
        lin_value.reshape(block_shape),
        log_decay.reshape(nblocks, BLOCK, heads_here),
    )
    start_state = jnp.zeros((heads_here, DH, DH), jnp.float32)
    local_state, local_out = lax.scan(lightning_block, start_state, inputs)
    local_out = local_out.reshape(tok_rows, heads_here, DH)
    decay_total = jnp.sum(log_decay, axis=0)
    totals, states = (
        lax.all_gather(decay_total[None].astype(jnp.bfloat16), "seq", axis=0, tiled=True).astype(
            jnp.float32
        ),
        lax.all_gather(local_state[None].astype(jnp.bfloat16), "seq", axis=0, tiled=True).astype(
            jnp.float32
        ),
    )
    position = lax.axis_index("seq")
    device_order = jnp.arange(totals.shape[0])
    earlier = (device_order < position)[:, None]
    before = jnp.sum(jnp.where(earlier, totals, 0.0), axis=0)
    inclusive = jnp.cumsum(totals, axis=0)
    factors = jnp.where(earlier, jnp.exp(jnp.where(earlier, before[None, :] - inclusive, 0.0)), 0.0)
    incoming = jnp.einsum("jh,jhde->hde", factors, states, precision=lax.Precision.HIGHEST)
    running = jnp.cumsum(log_decay, axis=0)
    query_f = (
        lin_query.reshape(tok_rows, heads_here, DH).astype(jnp.float32)
        * jnp.exp(running)[:, :, None]
    )
    carried = jnp.einsum("thd,hde->the", query_f, incoming, precision=lax.Precision.HIGHEST)
    lin_raw = local_out + carried
    lin_out = (
        (lin_raw * lax.rsqrt(jnp.mean(lin_raw * lin_raw, axis=-1, keepdims=True) + 1e-06))
        .astype(jnp.bfloat16)
        .reshape(tok_rows, head_width)
    )
    branch = jnp.dot(
        lin_out,
        lax.all_gather(out_weight, "seq", axis=1, tiled=True),
        preferred_element_type=jnp.float32,
    )
    kv_group = lax.axis_index("heads") * heads_here // (QUERY_HEADS // KVH)
    kv_mine = lax.dynamic_index_in_dim(kv_weight, kv_group, 0, keepdims=False)
    query_rows, kv_rows = (
        lax.all_gather(query_weight, "seq", axis=0, tiled=True),
        lax.all_gather(kv_mine, "seq", axis=0, tiled=True),
    )
    projection = jnp.concatenate([query_rows, kv_rows], axis=1)
    own_sum = lax.psum_scatter(
        branch.astype(jnp.bfloat16), "heads", scatter_dimension=1, tiled=True
    ).astype(jnp.float32)
    mixed_sum = stream.astype(jnp.float32) + own_sum
    stream_next = mixed_sum.astype(jnp.bfloat16)
    total_sq = lax.psum(jnp.sum(mixed_sum * mixed_sum, axis=1), "heads")
    normed = (
        mixed_sum
        * lax.rsqrt(total_sq / D + 1e-05)[:, None]
        * norm_gain.astype(jnp.float32)[None, :]
    ).astype(jnp.bfloat16)
    projected = jnp.dot(
        lax.all_gather(normed, "heads", axis=1, tiled=True),
        projection,
        preferred_element_type=jnp.float32,
    )
    projected = projected.astype(jnp.bfloat16)
    queries = projected[:, :head_width].reshape(tok_rows, heads_here, DH)
    keys_values = projected[:, head_width:]
    position = lax.axis_index("seq")
    query_pos = position * tok_rows + jnp.arange(tok_rows)
    score_scale = float(DH) ** (-0.5)

    def attend(state_in, kv_block, key_start):
        old_max, row_total, weighted = state_in
        key_count = kv_block.shape[0]
        key_part = kv_block[:, :DH]
        value_part = kv_block[:, DH:]
        scores = (
            jnp.einsum("thd,sd->hts", queries, key_part, preferred_element_type=jnp.float32)
            * score_scale
        )
        key_pos = key_start + jnp.arange(key_count)
        allowed = ((key_pos[None, :] <= query_pos[:, None]) & (key_pos[None, :] >= 0))[None, :, :]
        scores = jnp.where(allowed, scores, -1e30)
        new_max = jnp.maximum(old_max, jnp.max(scores, axis=-1))
        expos = jnp.where(allowed, jnp.exp(scores - new_max[:, :, None]), 0.0)
        rescale = jnp.exp(old_max - new_max)
        row_total = row_total * rescale + jnp.sum(expos, axis=-1)
        prob_bf16 = expos.astype(jnp.bfloat16)
        weighted = weighted * rescale[:, :, None] + jnp.einsum(
            "hts,sd->htd", prob_bf16, value_part, preferred_element_type=jnp.float32
        )
        return (new_max, row_total, weighted)

    initial = (
        jnp.full((heads_here, tok_rows), -1e30, jnp.float32),
        jnp.zeros((heads_here, tok_rows), jnp.float32),
        jnp.zeros((heads_here, tok_rows, DH), jnp.float32),
    )
    first_state = attend(initial, keys_values, position * tok_rows)
    seq_count = lax.axis_size("seq")

    def cycle_turn(turn_index, loop_state):
        moving, inner_state = loop_state
        moving = from_behind(moving, "seq", 1)
        source = position - turn_index
        return (moving, attend(inner_state, moving, source * tok_rows))

    _, final_state = lax.fori_loop(1, seq_count, cycle_turn, (keys_values, first_state))
    _, row_total, weighted = final_state
    attended = (
        jnp.transpose(weighted / row_total[:, :, None], (1, 0, 2))
        .reshape(tok_rows, head_width)
        .astype(jnp.bfloat16)
    )
    return (stream_next, attended)


def lightning_local(lin_query, lin_key, lin_value, log_decay):
    tok_rows = lin_query.shape[0]
    heads_here = log_decay.shape[1]
    nblocks = tok_rows // BLOCK
    shape4 = (tok_rows, heads_here, DH)
    q4, k4, v4 = (x.reshape(shape4) for x in (lin_query, lin_key, lin_value))
    state = jnp.zeros((heads_here, DH, DH), jnp.float32)
    outs = []
    for blk in range(nblocks):
        rows = slice(blk * BLOCK, (blk + 1) * BLOCK)
        state, out = lightning_block(state, (q4[rows], k4[rows], v4[rows], log_decay[rows]))
        outs.append(out)
    local_out = jnp.concatenate(outs, axis=0)
    decay_total = jnp.sum(log_decay, axis=0)
    pad_rows = 16
    total_rows = jnp.broadcast_to(decay_total[:, None, None], (heads_here, pad_rows, DH))
    packed = jnp.concatenate([state, total_rows], axis=1).astype(jnp.bfloat16)
    gathered = lax.all_gather(packed[None], "seq", axis=0, tiled=True)
    gathered = gathered.astype(jnp.float32)
    states = gathered[:, :, :DH, :]
    totals = gathered[:, :, DH, 0]
    position = lax.axis_index("seq")
    device_order = jnp.arange(totals.shape[0])
    earlier = (device_order < position)[:, None]
    before = jnp.sum(jnp.where(earlier, totals, 0.0), axis=0)
    inclusive = jnp.cumsum(totals, axis=0)
    factors = jnp.where(earlier, jnp.exp(jnp.where(earlier, before[None, :] - inclusive, 0.0)), 0.0)
    incoming = jnp.einsum("jh,jhde->hde", factors, states, precision=lax.Precision.HIGHEST)
    running = jnp.cumsum(log_decay, axis=0)
    query_f = q4.astype(jnp.float32) * jnp.exp(running)[:, :, None]
    carried = jnp.einsum("thd,hde->the", query_f, incoming, precision=lax.Precision.HIGHEST)
    lin_raw = local_out + carried
    lin_out = (
        (lin_raw * lax.rsqrt(jnp.mean(lin_raw * lin_raw, axis=-1, keepdims=True) + 1e-06))
        .astype(jnp.bfloat16)
        .reshape(tok_rows, heads_here * DH)
    )
    return lin_out


def heads_reduce_scatter(part, n_heads):
    if n_heads != 4:
        return lax.psum_scatter(part, "heads", scatter_dimension=0, tiled=True).astype(jnp.float32)
    mine = lax.axis_index("heads")
    core = mine % 2
    chip = mine // 2
    rows = part.shape[0] // n_heads
    grid = part.reshape(2, 2, rows, part.shape[1])
    keep1 = lax.dynamic_index_in_dim(grid, core, axis=1, keepdims=False)
    send1 = lax.dynamic_index_in_dim(grid, 1 - core, axis=1, keepdims=False)
    recv1 = lax.ppermute(send1, "heads", [(i, i ^ 1) for i in range(n_heads)])
    chip_sum = keep1.astype(jnp.float32) + recv1.astype(jnp.float32)
    keep2 = lax.dynamic_index_in_dim(chip_sum, chip, axis=0, keepdims=False)
    send2 = lax.dynamic_index_in_dim(chip_sum, 1 - chip, axis=0, keepdims=False)
    recv2 = lax.ppermute(send2.astype(jnp.bfloat16), "heads", [(i, i ^ 2) for i in range(n_heads)])
    return keep2 + recv2.astype(jnp.float32)


def attention_kernel(pos_ref, q_ref, kv_ref, o_ref, s_ref):
    position = pos_ref[0]
    n_blk = kv_ref.shape[0]
    rows = q_ref.shape[0]
    score_scale = float(DH) ** (-0.5)
    query = q_ref[...]
    row_id = lax.broadcasted_iota(jnp.int32, (rows, rows), 0)
    col_id = lax.broadcasted_iota(jnp.int32, (rows, rows), 1)

    def allowed_of(dist):
        if dist == 0:
            return col_id <= row_id
        return jnp.broadcast_to(dist <= position, (rows, rows))

    row_max = jnp.full((rows, 1), -1e30, jnp.float32)
    for dist in range(n_blk):
        key = kv_ref[dist, :, :DH]
        scores = lax.dot_general(
            query, key, (((1,), (1,)), ((), ())), preferred_element_type=jnp.float32
        ) * score_scale
        scores = jnp.where(allowed_of(dist), scores, -1e30)
        s_ref[dist] = scores
        row_max = jnp.maximum(row_max, jnp.max(scores, axis=1, keepdims=True))
    row_total = jnp.zeros((rows, 1), jnp.float32)
    weighted = jnp.zeros((rows, DH), jnp.float32)
    for dist in range(n_blk):
        expos = jnp.where(allowed_of(dist), jnp.exp(s_ref[dist] - row_max), 0.0)
        row_total = row_total + jnp.sum(expos, axis=1, keepdims=True)
        weighted = weighted + jnp.dot(
            expos.astype(jnp.bfloat16), kv_ref[dist, :, DH:], preferred_element_type=jnp.float32
        )
    o_ref[...] = (weighted / row_total).astype(o_ref.dtype)


def attention_pallas(queries, kv_stack, position):
    rows, width = queries.shape
    n_blk = kv_stack.shape[0]
    local_heads = width // DH
    flops = 4 * local_heads * n_blk * rows * rows * DH
    grid_spec = pltpu.PrefetchScalarGridSpec(
        num_scalar_prefetch=1,
        grid=(local_heads,),
        in_specs=[
            pl.BlockSpec((rows, DH), lambda h, pos: (0, h)),
            pl.BlockSpec((n_blk, rows, 2 * DH), lambda h, pos: (0, 0, 0)),
        ],
        out_specs=pl.BlockSpec((rows, DH), lambda h, pos: (0, h)),
        scratch_shapes=[pltpu.VMEM((n_blk, rows, rows), jnp.float32)],
    )
    return pl.pallas_call(
        attention_kernel,
        grid_spec=grid_spec,
        out_shape=jax.ShapeDtypeStruct((rows, width), jnp.bfloat16),
        compiler_params=pltpu.CompilerParams(dimension_semantics=("arbitrary",)),
        cost_estimate=pl.CostEstimate(
            flops=flops,
            transcendentals=local_heads * n_blk * rows * rows,
            bytes_accessed=2 * queries.size * 2 + kv_stack.size * 2,
        ),
    )(jnp.reshape(position, (1,)).astype(jnp.int32), queries, kv_stack)


def shards_fast(*args):
    return shards_fast_body(*args)


def shards_fast_body(
    lin_query, lin_key, lin_value, log_decay, stream, out_weight, norm_gain, query_weight, kv_weight
):
    n_heads = lax.axis_size("heads")
    n_seq = lax.axis_size("seq")
    tok_rows = lin_query.shape[0]
    heads_here = log_decay.shape[1]
    mine_a = lax.axis_index("heads")
    mine_b = lax.axis_index("seq")
    swap = [(x * n_seq + y, y * n_seq + x) for x in range(n_heads) for y in range(n_seq)]
    gain_rows = jnp.broadcast_to(norm_gain[None, :], (16, norm_gain.shape[0]))
    packed = lax.ppermute(
        jnp.concatenate([stream, gain_rows], axis=0), ("heads", "seq"), swap
    )
    stream_t = packed[:tok_rows]
    gain_b = packed[tok_rows]

    lin_out = lightning_local(lin_query, lin_key, lin_value, log_decay)
    halves = []
    half_rows = tok_rows // 2
    for half in range(2):
        lin_all = lax.all_gather(
            lin_out[half * half_rows : (half + 1) * half_rows], "seq", axis=0, tiled=True
        )
        part = jnp.dot(lin_all, out_weight, preferred_element_type=jnp.float32)
        halves.append(heads_reduce_scatter(part.astype(jnp.bfloat16), n_heads))
    own_sum = jnp.concatenate(halves, axis=0)
    mixed_sum = stream_t.astype(jnp.float32) + own_sum
    next_t = mixed_sum.astype(jnp.bfloat16)
    next_early = lax.ppermute(next_t[:half_rows], ("heads", "seq"), swap)
    next_late = lax.ppermute(next_t[half_rows:], ("heads", "seq"), swap)
    stream_next = jnp.concatenate([next_early, next_late], axis=0)
    total_sq = lax.psum(jnp.sum(mixed_sum * mixed_sum, axis=1), "seq")
    normed = (
        mixed_sum
        * lax.rsqrt(total_sq / D + 1e-05)[:, None]
        * gain_b.astype(jnp.float32)[None, :]
    ).astype(jnp.bfloat16)
    normed_all = lax.all_gather(normed, "heads", axis=0, tiled=True)
    kv_group = mine_a * heads_here // (QUERY_HEADS // KVH)
    kv_mine = lax.dynamic_index_in_dim(kv_weight, kv_group, 0, keepdims=False)
    q_part = jnp.dot(normed_all, query_weight, preferred_element_type=jnp.float32)
    kv_part = jnp.dot(normed_all, kv_mine, preferred_element_type=jnp.float32)
    queries = lax.psum_scatter(q_part.astype(jnp.bfloat16), "seq", scatter_dimension=0, tiled=True)
    kv_own = lax.psum_scatter(kv_part.astype(jnp.bfloat16), "seq", scatter_dimension=0, tiled=True)
    earlier_kv = [from_behind(kv_own, "seq", dist) for dist in range(1, n_seq)]
    kv_stack = jnp.stack([kv_own] + earlier_kv, axis=0)
    attended = attention_pallas(queries, kv_stack, mine_b)
    return (stream_next, attended)


def solution(mesh):
    n_heads = mesh.shape["heads"]
    n_seq = mesh.shape["seq"]
    fast_ok = n_heads == n_seq and QUERY_HEADS % n_heads == 0
    if fast_ok:
        heads_here = QUERY_HEADS // n_heads
        fast_ok = (QUERY_HEADS // KVH) % heads_here == 0 and D % n_seq == 0
    shards = shards_fast if fast_ok else shards_base

    return jax.shard_map(
        shards,
        mesh=mesh,
        in_specs=(
            P(("groups", "seq"), "heads"),
            P(("groups", "seq"), "heads"),
            P(("groups", "seq"), "heads"),
            P(("groups", "seq"), "heads"),
            P(("groups", "seq"), "heads"),
            P("heads", "seq"),
            P("heads"),
            P("seq", "heads"),
            P(None, "seq", None),
        ),
        out_specs=(P(("groups", "seq"), "heads"), P(("groups", "seq"), "heads")),
        check_vma=False,
    )
```

```python
import jax
import jax.numpy as jnp
from jax import lax
from jax.experimental import pallas as pl
from jax.experimental.pallas import tpu as pltpu
from jax.sharding import PartitionSpec as P

D = 6144
QUERY_HEADS = 32
KVH = 4
DH = 128
BLOCK = 256


def from_behind(value, axis, steps):
    count = lax.axis_size(axis)
    leading, last = (max(0, -steps), min(count, count - steps))
    return lax.ppermute(value, axis, [(source, source + steps) for source in range(leading, last)])


def lightning_block(kv_state, block_inputs):
    query_blk, key_blk, value_blk, decay_blk = block_inputs
    block_len = query_blk.shape[0]
    local_cum = jnp.cumsum(decay_blk, axis=0)
    causal_mask = (jnp.arange(block_len)[:, None] >= jnp.arange(block_len)[None, :])[:, :, None]
    decay_diff = local_cum[:, None, :] - local_cum[None, :, :]
    decays = jnp.where(causal_mask, jnp.exp(jnp.where(causal_mask, decay_diff, 0.0)), 0.0)
    scores = jnp.einsum("thd,shd->hts", query_blk, key_blk, preferred_element_type=jnp.float32)
    weights = (scores * jnp.transpose(decays, (2, 0, 1))).astype(jnp.bfloat16)
    intra_out = jnp.einsum("hts,shd->thd", weights, value_blk, preferred_element_type=jnp.float32)
    query_f = query_blk.astype(jnp.float32)
    inter_out = jnp.einsum(
        "thd,hde->the",
        query_f * jnp.exp(local_cum)[:, :, None],
        kv_state,
        precision=lax.Precision.HIGHEST,
    )
    tail_decay = jnp.exp(local_cum[-1][None, :] - local_cum)
    key_f = key_blk.astype(jnp.float32) * tail_decay[:, :, None]
    kv_state = jnp.exp(local_cum[-1])[:, None, None] * kv_state + jnp.einsum(
        "shd,she->hde", key_f, value_blk.astype(jnp.float32), precision=lax.Precision.HIGHEST
    )
    return (kv_state, intra_out + inter_out)


def block_state(kv_state, key_blk, value_blk, decay_blk):
    local_cum = jnp.cumsum(decay_blk, axis=0)
    tail_decay = jnp.exp(local_cum[-1][None, :] - local_cum)
    key_f = key_blk.astype(jnp.float32) * tail_decay[:, :, None]
    return jnp.exp(local_cum[-1])[:, None, None] * kv_state + jnp.einsum(
        "shd,she->hde", key_f, value_blk.astype(jnp.float32), precision=lax.Precision.HIGHEST
    )


def shards_base(
    lin_query, lin_key, lin_value, log_decay, stream, out_weight, norm_gain, query_weight, kv_weight
):
    tok_rows = lin_query.shape[0]
    heads_here = log_decay.shape[1]
    head_width = heads_here * DH
    nblocks = tok_rows // BLOCK
    block_shape = (nblocks, BLOCK, heads_here, DH)
    inputs = (
        lin_query.reshape(block_shape),
        lin_key.reshape(block_shape),
        lin_value.reshape(block_shape),
        log_decay.reshape(nblocks, BLOCK, heads_here),
    )
    start_state = jnp.zeros((heads_here, DH, DH), jnp.float32)
    local_state, local_out = lax.scan(lightning_block, start_state, inputs)
    local_out = local_out.reshape(tok_rows, heads_here, DH)
    decay_total = jnp.sum(log_decay, axis=0)
    totals, states = (
        lax.all_gather(decay_total[None].astype(jnp.bfloat16), "seq", axis=0, tiled=True).astype(
            jnp.float32
        ),
        lax.all_gather(local_state[None].astype(jnp.bfloat16), "seq", axis=0, tiled=True).astype(
            jnp.float32
        ),
    )
    position = lax.axis_index("seq")
    device_order = jnp.arange(totals.shape[0])
    earlier = (device_order < position)[:, None]
    before = jnp.sum(jnp.where(earlier, totals, 0.0), axis=0)
    inclusive = jnp.cumsum(totals, axis=0)
    factors = jnp.where(earlier, jnp.exp(jnp.where(earlier, before[None, :] - inclusive, 0.0)), 0.0)
    incoming = jnp.einsum("jh,jhde->hde", factors, states, precision=lax.Precision.HIGHEST)
    running = jnp.cumsum(log_decay, axis=0)
    query_f = (
        lin_query.reshape(tok_rows, heads_here, DH).astype(jnp.float32)
        * jnp.exp(running)[:, :, None]
    )
    carried = jnp.einsum("thd,hde->the", query_f, incoming, precision=lax.Precision.HIGHEST)
    lin_raw = local_out + carried
    lin_out = (
        (lin_raw * lax.rsqrt(jnp.mean(lin_raw * lin_raw, axis=-1, keepdims=True) + 1e-06))
        .astype(jnp.bfloat16)
        .reshape(tok_rows, head_width)
    )
    branch = jnp.dot(
        lin_out,
        lax.all_gather(out_weight, "seq", axis=1, tiled=True),
        preferred_element_type=jnp.float32,
    )
    kv_group = lax.axis_index("heads") * heads_here // (QUERY_HEADS // KVH)
    kv_mine = lax.dynamic_index_in_dim(kv_weight, kv_group, 0, keepdims=False)
    query_rows, kv_rows = (
        lax.all_gather(query_weight, "seq", axis=0, tiled=True),
        lax.all_gather(kv_mine, "seq", axis=0, tiled=True),
    )
    projection = jnp.concatenate([query_rows, kv_rows], axis=1)
    own_sum = lax.psum_scatter(
        branch.astype(jnp.bfloat16), "heads", scatter_dimension=1, tiled=True
    ).astype(jnp.float32)
    mixed_sum = stream.astype(jnp.float32) + own_sum
    stream_next = mixed_sum.astype(jnp.bfloat16)
    total_sq = lax.psum(jnp.sum(mixed_sum * mixed_sum, axis=1), "heads")
    normed = (
        mixed_sum
        * lax.rsqrt(total_sq / D + 1e-05)[:, None]
        * norm_gain.astype(jnp.float32)[None, :]
    ).astype(jnp.bfloat16)
    projected = jnp.dot(
        lax.all_gather(normed, "heads", axis=1, tiled=True),
        projection,
        preferred_element_type=jnp.float32,
    )
    projected = projected.astype(jnp.bfloat16)
    queries = projected[:, :head_width].reshape(tok_rows, heads_here, DH)
    keys_values = projected[:, head_width:]
    position = lax.axis_index("seq")
    query_pos = position * tok_rows + jnp.arange(tok_rows)
    score_scale = float(DH) ** (-0.5)

    def attend(state_in, kv_block, key_start):
        old_max, row_total, weighted = state_in
        key_count = kv_block.shape[0]
        key_part = kv_block[:, :DH]
        value_part = kv_block[:, DH:]
        scores = (
            jnp.einsum("thd,sd->hts", queries, key_part, preferred_element_type=jnp.float32)
            * score_scale
        )
        key_pos = key_start + jnp.arange(key_count)
        allowed = ((key_pos[None, :] <= query_pos[:, None]) & (key_pos[None, :] >= 0))[None, :, :]
        scores = jnp.where(allowed, scores, -1e30)
        new_max = jnp.maximum(old_max, jnp.max(scores, axis=-1))
        expos = jnp.where(allowed, jnp.exp(scores - new_max[:, :, None]), 0.0)
        rescale = jnp.exp(old_max - new_max)
        row_total = row_total * rescale + jnp.sum(expos, axis=-1)
        prob_bf16 = expos.astype(jnp.bfloat16)
        weighted = weighted * rescale[:, :, None] + jnp.einsum(
            "hts,sd->htd", prob_bf16, value_part, preferred_element_type=jnp.float32
        )
        return (new_max, row_total, weighted)

    initial = (
        jnp.full((heads_here, tok_rows), -1e30, jnp.float32),
        jnp.zeros((heads_here, tok_rows), jnp.float32),
        jnp.zeros((heads_here, tok_rows, DH), jnp.float32),
    )
    first_state = attend(initial, keys_values, position * tok_rows)
    seq_count = lax.axis_size("seq")

    def cycle_turn(turn_index, loop_state):
        moving, inner_state = loop_state
        moving = from_behind(moving, "seq", 1)
        source = position - turn_index
        return (moving, attend(inner_state, moving, source * tok_rows))

    _, final_state = lax.fori_loop(1, seq_count, cycle_turn, (keys_values, first_state))
    _, row_total, weighted = final_state
    attended = (
        jnp.transpose(weighted / row_total[:, :, None], (1, 0, 2))
        .reshape(tok_rows, head_width)
        .astype(jnp.bfloat16)
    )
    return (stream_next, attended)


def lightning_local(lin_query, lin_key, lin_value, log_decay):
    tok_rows = lin_query.shape[0]
    heads_here = log_decay.shape[1]
    nblocks = tok_rows // BLOCK
    shape4 = (tok_rows, heads_here, DH)
    q4, k4, v4 = (x.reshape(shape4) for x in (lin_query, lin_key, lin_value))
    state = jnp.zeros((heads_here, DH, DH), jnp.float32)
    starts = []
    for blk in range(nblocks):
        rows = slice(blk * BLOCK, (blk + 1) * BLOCK)
        starts.append(state)
        state = block_state(state, k4[rows], v4[rows], log_decay[rows])
    decay_total = jnp.sum(log_decay, axis=0)
    pad_rows = 16
    total_rows = jnp.broadcast_to(decay_total[:, None, None], (heads_here, pad_rows, DH))
    packed = jnp.concatenate([state, total_rows], axis=1).astype(jnp.bfloat16)
    packed, starts, q4, k4, v4 = lax.optimization_barrier((packed, starts, q4, k4, v4))
    outs = []
    for blk in range(nblocks):
        rows = slice(blk * BLOCK, (blk + 1) * BLOCK)
        _, out = lightning_block(starts[blk], (q4[rows], k4[rows], v4[rows], log_decay[rows]))
        outs.append(out)
    local_out = jnp.concatenate(outs, axis=0)
    gathered = lax.all_gather(packed[None], "seq", axis=0, tiled=True)
    gathered = gathered.astype(jnp.float32)
    states = gathered[:, :, :DH, :]
    totals = gathered[:, :, DH, 0]
    position = lax.axis_index("seq")
    device_order = jnp.arange(totals.shape[0])
    earlier = (device_order < position)[:, None]
    before = jnp.sum(jnp.where(earlier, totals, 0.0), axis=0)
    inclusive = jnp.cumsum(totals, axis=0)
    factors = jnp.where(earlier, jnp.exp(jnp.where(earlier, before[None, :] - inclusive, 0.0)), 0.0)
    incoming = jnp.einsum("jh,jhde->hde", factors, states, precision=lax.Precision.HIGHEST)
    running = jnp.cumsum(log_decay, axis=0)
    query_f = q4.astype(jnp.float32) * jnp.exp(running)[:, :, None]
    carried = jnp.einsum("thd,hde->the", query_f, incoming, precision=lax.Precision.HIGHEST)
    lin_raw = local_out + carried
    lin_out = (
        (lin_raw * lax.rsqrt(jnp.mean(lin_raw * lin_raw, axis=-1, keepdims=True) + 1e-06))
        .astype(jnp.bfloat16)
        .reshape(tok_rows, heads_here * DH)
    )
    return lin_out


def heads_reduce_scatter(part, n_heads):
    if n_heads != 4:
        return lax.psum_scatter(part, "heads", scatter_dimension=0, tiled=True).astype(jnp.float32)
    mine = lax.axis_index("heads")
    core = mine % 2
    chip = mine // 2
    rows = part.shape[0] // n_heads
    grid = part.reshape(2, 2, rows, part.shape[1])
    keep1 = lax.dynamic_index_in_dim(grid, core, axis=1, keepdims=False)
    send1 = lax.dynamic_index_in_dim(grid, 1 - core, axis=1, keepdims=False)
    recv1 = lax.ppermute(send1, "heads", [(i, i ^ 1) for i in range(n_heads)])
    chip_sum = keep1.astype(jnp.float32) + recv1.astype(jnp.float32)
    keep2 = lax.dynamic_index_in_dim(chip_sum, chip, axis=0, keepdims=False)
    send2 = lax.dynamic_index_in_dim(chip_sum, 1 - chip, axis=0, keepdims=False)
    recv2 = lax.ppermute(send2.astype(jnp.bfloat16), "heads", [(i, i ^ 2) for i in range(n_heads)])
    return keep2 + recv2.astype(jnp.float32)


def attention_kernel(pos_ref, q_ref, kv_ref, o_ref, s_ref):
    position = pos_ref[0]
    n_blk = kv_ref.shape[0]
    rows = q_ref.shape[0]
    score_scale = float(DH) ** (-0.5)
    query = q_ref[...]
    row_id = lax.broadcasted_iota(jnp.int32, (rows, rows), 0)
    col_id = lax.broadcasted_iota(jnp.int32, (rows, rows), 1)

    def allowed_of(dist):
        if dist == 0:
            return col_id <= row_id
        return jnp.broadcast_to(dist <= position, (rows, rows))

    row_max = jnp.full((rows, 1), -1e30, jnp.float32)
    for dist in range(n_blk):
        key = kv_ref[dist, :, :DH]
        scores = lax.dot_general(
            query, key, (((1,), (1,)), ((), ())), preferred_element_type=jnp.float32
        ) * score_scale
        scores = jnp.where(allowed_of(dist), scores, -1e30)
        s_ref[dist] = scores
        row_max = jnp.maximum(row_max, jnp.max(scores, axis=1, keepdims=True))
    row_total = jnp.zeros((rows, 1), jnp.float32)
    weighted = jnp.zeros((rows, DH), jnp.float32)
    for dist in range(n_blk):
        expos = jnp.where(allowed_of(dist), jnp.exp(s_ref[dist] - row_max), 0.0)
        row_total = row_total + jnp.sum(expos, axis=1, keepdims=True)
        weighted = weighted + jnp.dot(
            expos.astype(jnp.bfloat16), kv_ref[dist, :, DH:], preferred_element_type=jnp.float32
        )
    o_ref[...] = (weighted / row_total).astype(o_ref.dtype)


def attention_pallas(queries, kv_stack, position):
    rows, width = queries.shape
    n_blk = kv_stack.shape[0]
    local_heads = width // DH
    flops = 4 * local_heads * n_blk * rows * rows * DH
    grid_spec = pltpu.PrefetchScalarGridSpec(
        num_scalar_prefetch=1,
        grid=(local_heads,),
        in_specs=[
            pl.BlockSpec((rows, DH), lambda h, pos: (0, h)),
            pl.BlockSpec((n_blk, rows, 2 * DH), lambda h, pos: (0, 0, 0)),
        ],
        out_specs=pl.BlockSpec((rows, DH), lambda h, pos: (0, h)),
        scratch_shapes=[pltpu.VMEM((n_blk, rows, rows), jnp.float32)],
    )
    return pl.pallas_call(
        attention_kernel,
        grid_spec=grid_spec,
        out_shape=jax.ShapeDtypeStruct((rows, width), jnp.bfloat16),
        compiler_params=pltpu.CompilerParams(dimension_semantics=("arbitrary",)),
        cost_estimate=pl.CostEstimate(
            flops=flops,
            transcendentals=local_heads * n_blk * rows * rows,
            bytes_accessed=2 * queries.size * 2 + kv_stack.size * 2,
        ),
    )(jnp.reshape(position, (1,)).astype(jnp.int32), queries, kv_stack)


def shards_fast(*args):
    return shards_fast_body(*args)


def shards_fast_body(
    lin_query, lin_key, lin_value, log_decay, stream, out_weight, norm_gain, query_weight, kv_weight
):
    n_heads = lax.axis_size("heads")
    n_seq = lax.axis_size("seq")
    tok_rows = lin_query.shape[0]
    heads_here = log_decay.shape[1]
    mine_a = lax.axis_index("heads")
    mine_b = lax.axis_index("seq")
    swap = [(x * n_seq + y, y * n_seq + x) for x in range(n_heads) for y in range(n_seq)]
    gain_rows = jnp.broadcast_to(norm_gain[None, :], (16, norm_gain.shape[0]))
    packed = lax.ppermute(
        jnp.concatenate([stream, gain_rows], axis=0), ("heads", "seq"), swap
    )
    stream_t = packed[:tok_rows]
    gain_b = packed[tok_rows]

    lin_out = lightning_local(lin_query, lin_key, lin_value, log_decay)
    halves = []
    half_rows = tok_rows // 2
    for half in range(2):
        lin_all = lax.all_gather(
            lin_out[half * half_rows : (half + 1) * half_rows], "seq", axis=0, tiled=True
        )
        part = jnp.dot(lin_all, out_weight, preferred_element_type=jnp.float32)
        halves.append(heads_reduce_scatter(part.astype(jnp.bfloat16), n_heads))
    own_sum = jnp.concatenate(halves, axis=0)
    mixed_sum = stream_t.astype(jnp.float32) + own_sum
    next_t = mixed_sum.astype(jnp.bfloat16)
    next_early = lax.ppermute(next_t[:half_rows], ("heads", "seq"), swap)
    next_late = lax.ppermute(next_t[half_rows:], ("heads", "seq"), swap)
    stream_next = jnp.concatenate([next_early, next_late], axis=0)
    total_sq = lax.psum(jnp.sum(mixed_sum * mixed_sum, axis=1), "seq")
    normed = (
        mixed_sum
        * lax.rsqrt(total_sq / D + 1e-05)[:, None]
        * gain_b.astype(jnp.float32)[None, :]
    ).astype(jnp.bfloat16)
    normed_all = lax.all_gather(normed, "heads", axis=0, tiled=True)
    kv_group = mine_a * heads_here // (QUERY_HEADS // KVH)
    kv_mine = lax.dynamic_index_in_dim(kv_weight, kv_group, 0, keepdims=False)
    q_part = jnp.dot(normed_all, query_weight, preferred_element_type=jnp.float32)
    kv_part = jnp.dot(normed_all, kv_mine, preferred_element_type=jnp.float32)
    queries = lax.psum_scatter(q_part.astype(jnp.bfloat16), "seq", scatter_dimension=0, tiled=True)
    kv_own = lax.psum_scatter(kv_part.astype(jnp.bfloat16), "seq", scatter_dimension=0, tiled=True)
    earlier_kv = [from_behind(kv_own, "seq", dist) for dist in range(1, n_seq)]
    kv_stack = jnp.stack([kv_own] + earlier_kv, axis=0)
    attended = attention_pallas(queries, kv_stack, mine_b)
    return (stream_next, attended)


def solution(mesh):
    n_heads = mesh.shape["heads"]
    n_seq = mesh.shape["seq"]
    fast_ok = n_heads == n_seq and QUERY_HEADS % n_heads == 0
    if fast_ok:
        heads_here = QUERY_HEADS // n_heads
        fast_ok = (QUERY_HEADS // KVH) % heads_here == 0 and D % n_seq == 0
    shards = shards_fast if fast_ok else shards_base

    return jax.shard_map(
        shards,
        mesh=mesh,
        in_specs=(
            P(("groups", "seq"), "heads"),
            P(("groups", "seq"), "heads"),
            P(("groups", "seq"), "heads"),
            P(("groups", "seq"), "heads"),
            P(("groups", "seq"), "heads"),
            P("heads", "seq"),
            P("heads"),
            P("seq", "heads"),
            P(None, "seq", None),
        ),
        out_specs=(P(("groups", "seq"), "heads"), P(("groups", "seq"), "heads")),
        check_vma=False,
    )
```

```python
import jax
import jax.numpy as jnp
from jax import lax
from jax.experimental import pallas as pl
from jax.experimental.pallas import tpu as pltpu
from jax.sharding import PartitionSpec as P

D = 6144
QUERY_HEADS = 32
KVH = 4
DH = 128
BLOCK = 256


def from_behind(value, axis, steps):
    count = lax.axis_size(axis)
    leading, last = (max(0, -steps), min(count, count - steps))
    return lax.ppermute(value, axis, [(source, source + steps) for source in range(leading, last)])


def lightning_block(kv_state, block_inputs):
    query_blk, key_blk, value_blk, decay_blk = block_inputs
    block_len = query_blk.shape[0]
    local_cum = jnp.cumsum(decay_blk, axis=0)
    causal_mask = (jnp.arange(block_len)[:, None] >= jnp.arange(block_len)[None, :])[:, :, None]
    decay_diff = local_cum[:, None, :] - local_cum[None, :, :]
    decays = jnp.where(causal_mask, jnp.exp(jnp.where(causal_mask, decay_diff, 0.0)), 0.0)
    scores = jnp.einsum("thd,shd->hts", query_blk, key_blk, preferred_element_type=jnp.float32)
    weights = (scores * jnp.transpose(decays, (2, 0, 1))).astype(jnp.bfloat16)
    intra_out = jnp.einsum("hts,shd->thd", weights, value_blk, preferred_element_type=jnp.float32)
    query_f = query_blk.astype(jnp.float32)
    inter_out = jnp.einsum(
        "thd,hde->the",
        query_f * jnp.exp(local_cum)[:, :, None],
        kv_state,
        precision=lax.Precision.HIGHEST,
    )
    tail_decay = jnp.exp(local_cum[-1][None, :] - local_cum)
    key_f = key_blk.astype(jnp.float32) * tail_decay[:, :, None]
    kv_state = jnp.exp(local_cum[-1])[:, None, None] * kv_state + jnp.einsum(
        "shd,she->hde", key_f, value_blk.astype(jnp.float32), precision=lax.Precision.HIGHEST
    )
    return (kv_state, intra_out + inter_out)


def block_state(kv_state, key_blk, value_blk, decay_blk):
    local_cum = jnp.cumsum(decay_blk, axis=0)
    tail_decay = jnp.exp(local_cum[-1][None, :] - local_cum)
    key_f = key_blk.astype(jnp.float32) * tail_decay[:, :, None]
    return jnp.exp(local_cum[-1])[:, None, None] * kv_state + jnp.einsum(
        "shd,she->hde", key_f, value_blk.astype(jnp.float32), precision=lax.Precision.HIGHEST
    )


def shards_base(
    lin_query, lin_key, lin_value, log_decay, stream, out_weight, norm_gain, query_weight, kv_weight
):
    tok_rows = lin_query.shape[0]
    heads_here = log_decay.shape[1]
    head_width = heads_here * DH
    nblocks = tok_rows // BLOCK
    block_shape = (nblocks, BLOCK, heads_here, DH)
    inputs = (
        lin_query.reshape(block_shape),
        lin_key.reshape(block_shape),
        lin_value.reshape(block_shape),
        log_decay.reshape(nblocks, BLOCK, heads_here),
    )
    start_state = jnp.zeros((heads_here, DH, DH), jnp.float32)
    local_state, local_out = lax.scan(lightning_block, start_state, inputs)
    local_out = local_out.reshape(tok_rows, heads_here, DH)
    decay_total = jnp.sum(log_decay, axis=0)
    totals, states = (
        lax.all_gather(decay_total[None].astype(jnp.bfloat16), "seq", axis=0, tiled=True).astype(
            jnp.float32
        ),
        lax.all_gather(local_state[None].astype(jnp.bfloat16), "seq", axis=0, tiled=True).astype(
            jnp.float32
        ),
    )
    position = lax.axis_index("seq")
    device_order = jnp.arange(totals.shape[0])
    earlier = (device_order < position)[:, None]
    before = jnp.sum(jnp.where(earlier, totals, 0.0), axis=0)
    inclusive = jnp.cumsum(totals, axis=0)
    factors = jnp.where(earlier, jnp.exp(jnp.where(earlier, before[None, :] - inclusive, 0.0)), 0.0)
    incoming = jnp.einsum("jh,jhde->hde", factors, states, precision=lax.Precision.HIGHEST)
    running = jnp.cumsum(log_decay, axis=0)
    query_f = (
        lin_query.reshape(tok_rows, heads_here, DH).astype(jnp.float32)
        * jnp.exp(running)[:, :, None]
    )
    carried = jnp.einsum("thd,hde->the", query_f, incoming, precision=lax.Precision.HIGHEST)
    lin_raw = local_out + carried
    lin_out = (
        (lin_raw * lax.rsqrt(jnp.mean(lin_raw * lin_raw, axis=-1, keepdims=True) + 1e-06))
        .astype(jnp.bfloat16)
        .reshape(tok_rows, head_width)
    )
    branch = jnp.dot(
        lin_out,
        lax.all_gather(out_weight, "seq", axis=1, tiled=True),
        preferred_element_type=jnp.float32,
    )
    kv_group = lax.axis_index("heads") * heads_here // (QUERY_HEADS // KVH)
    kv_mine = lax.dynamic_index_in_dim(kv_weight, kv_group, 0, keepdims=False)
    query_rows, kv_rows = (
        lax.all_gather(query_weight, "seq", axis=0, tiled=True),
        lax.all_gather(kv_mine, "seq", axis=0, tiled=True),
    )
    projection = jnp.concatenate([query_rows, kv_rows], axis=1)
    own_sum = lax.psum_scatter(
        branch.astype(jnp.bfloat16), "heads", scatter_dimension=1, tiled=True
    ).astype(jnp.float32)
    mixed_sum = stream.astype(jnp.float32) + own_sum
    stream_next = mixed_sum.astype(jnp.bfloat16)
    total_sq = lax.psum(jnp.sum(mixed_sum * mixed_sum, axis=1), "heads")
    normed = (
        mixed_sum
        * lax.rsqrt(total_sq / D + 1e-05)[:, None]
        * norm_gain.astype(jnp.float32)[None, :]
    ).astype(jnp.bfloat16)
    projected = jnp.dot(
        lax.all_gather(normed, "heads", axis=1, tiled=True),
        projection,
        preferred_element_type=jnp.float32,
    )
    projected = projected.astype(jnp.bfloat16)
    queries = projected[:, :head_width].reshape(tok_rows, heads_here, DH)
    keys_values = projected[:, head_width:]
    position = lax.axis_index("seq")
    query_pos = position * tok_rows + jnp.arange(tok_rows)
    score_scale = float(DH) ** (-0.5)

    def attend(state_in, kv_block, key_start):
        old_max, row_total, weighted = state_in
        key_count = kv_block.shape[0]
        key_part = kv_block[:, :DH]
        value_part = kv_block[:, DH:]
        scores = (
            jnp.einsum("thd,sd->hts", queries, key_part, preferred_element_type=jnp.float32)
            * score_scale
        )
        key_pos = key_start + jnp.arange(key_count)
        allowed = ((key_pos[None, :] <= query_pos[:, None]) & (key_pos[None, :] >= 0))[None, :, :]
        scores = jnp.where(allowed, scores, -1e30)
        new_max = jnp.maximum(old_max, jnp.max(scores, axis=-1))
        expos = jnp.where(allowed, jnp.exp(scores - new_max[:, :, None]), 0.0)
        rescale = jnp.exp(old_max - new_max)
        row_total = row_total * rescale + jnp.sum(expos, axis=-1)
        prob_bf16 = expos.astype(jnp.bfloat16)
        weighted = weighted * rescale[:, :, None] + jnp.einsum(
            "hts,sd->htd", prob_bf16, value_part, preferred_element_type=jnp.float32
        )
        return (new_max, row_total, weighted)

    initial = (
        jnp.full((heads_here, tok_rows), -1e30, jnp.float32),
        jnp.zeros((heads_here, tok_rows), jnp.float32),
        jnp.zeros((heads_here, tok_rows, DH), jnp.float32),
    )
    first_state = attend(initial, keys_values, position * tok_rows)
    seq_count = lax.axis_size("seq")

    def cycle_turn(turn_index, loop_state):
        moving, inner_state = loop_state
        moving = from_behind(moving, "seq", 1)
        source = position - turn_index
        return (moving, attend(inner_state, moving, source * tok_rows))

    _, final_state = lax.fori_loop(1, seq_count, cycle_turn, (keys_values, first_state))
    _, row_total, weighted = final_state
    attended = (
        jnp.transpose(weighted / row_total[:, :, None], (1, 0, 2))
        .reshape(tok_rows, head_width)
        .astype(jnp.bfloat16)
    )
    return (stream_next, attended)


def lightning_local(lin_query, lin_key, lin_value, log_decay):
    tok_rows = lin_query.shape[0]
    heads_here = log_decay.shape[1]
    nblocks = tok_rows // BLOCK
    shape4 = (tok_rows, heads_here, DH)
    q4, k4, v4 = (x.reshape(shape4) for x in (lin_query, lin_key, lin_value))
    state = jnp.zeros((heads_here, DH, DH), jnp.float32)
    starts = []
    for blk in range(nblocks):
        rows = slice(blk * BLOCK, (blk + 1) * BLOCK)
        starts.append(state)
        state = block_state(state, k4[rows], v4[rows], log_decay[rows])
    decay_total = jnp.sum(log_decay, axis=0)
    pad_rows = 16
    total_rows = jnp.broadcast_to(decay_total[:, None, None], (heads_here, pad_rows, DH))
    packed = jnp.concatenate([state, total_rows], axis=1).astype(jnp.bfloat16)
    packed, starts, q4, k4, v4 = lax.optimization_barrier((packed, starts, q4, k4, v4))
    outs = []
    for blk in range(nblocks):
        rows = slice(blk * BLOCK, (blk + 1) * BLOCK)
        _, out = lightning_block(starts[blk], (q4[rows], k4[rows], v4[rows], log_decay[rows]))
        outs.append(out)
    local_out = jnp.concatenate(outs, axis=0)
    gathered = lax.all_gather(packed[None], "seq", axis=0, tiled=True)
    gathered = gathered.astype(jnp.float32)
    states = gathered[:, :, :DH, :]
    totals = gathered[:, :, DH, 0]
    position = lax.axis_index("seq")
    device_order = jnp.arange(totals.shape[0])
    earlier = (device_order < position)[:, None]
    before = jnp.sum(jnp.where(earlier, totals, 0.0), axis=0)
    inclusive = jnp.cumsum(totals, axis=0)
    factors = jnp.where(earlier, jnp.exp(jnp.where(earlier, before[None, :] - inclusive, 0.0)), 0.0)
    incoming = jnp.einsum("jh,jhde->hde", factors, states, precision=lax.Precision.HIGHEST)
    running = jnp.cumsum(log_decay, axis=0)
    query_f = q4.astype(jnp.float32) * jnp.exp(running)[:, :, None]
    carried = jnp.einsum("thd,hde->the", query_f, incoming, precision=lax.Precision.HIGHEST)
    lin_raw = local_out + carried
    lin_out = (
        (lin_raw * lax.rsqrt(jnp.mean(lin_raw * lin_raw, axis=-1, keepdims=True) + 1e-06))
        .astype(jnp.bfloat16)
        .reshape(tok_rows, heads_here * DH)
    )
    return lin_out


def heads_reduce_scatter(part, n_heads):
    if n_heads != 4:
        return lax.psum_scatter(part, "heads", scatter_dimension=0, tiled=True).astype(jnp.float32)
    mine = lax.axis_index("heads")
    core = mine % 2
    chip = mine // 2
    rows = part.shape[0] // n_heads
    grid = part.reshape(2, 2, rows, part.shape[1])
    keep1 = lax.dynamic_index_in_dim(grid, core, axis=1, keepdims=False)
    send1 = lax.dynamic_index_in_dim(grid, 1 - core, axis=1, keepdims=False)
    recv1 = lax.ppermute(send1, "heads", [(i, i ^ 1) for i in range(n_heads)])
    chip_sum = keep1.astype(jnp.float32) + recv1.astype(jnp.float32)
    keep2 = lax.dynamic_index_in_dim(chip_sum, chip, axis=0, keepdims=False)
    send2 = lax.dynamic_index_in_dim(chip_sum, 1 - chip, axis=0, keepdims=False)
    recv2 = lax.ppermute(send2.astype(jnp.bfloat16), "heads", [(i, i ^ 2) for i in range(n_heads)])
    return keep2 + recv2.astype(jnp.float32)


def attention_kernel(pos_ref, q_ref, kv_ref, o_ref, s_ref):
    position = pos_ref[0]
    n_blk = kv_ref.shape[0]
    rows = q_ref.shape[0]
    score_scale = float(DH) ** (-0.5)
    query = q_ref[...]
    row_id = lax.broadcasted_iota(jnp.int32, (rows, rows), 0)
    col_id = lax.broadcasted_iota(jnp.int32, (rows, rows), 1)

    def allowed_of(dist):
        if dist == 0:
            return col_id <= row_id
        return jnp.broadcast_to(dist <= position, (rows, rows))

    row_max = jnp.full((rows, 1), -1e30, jnp.float32)
    for dist in range(n_blk):
        key = kv_ref[dist, :, :DH]
        scores = lax.dot_general(
            query, key, (((1,), (1,)), ((), ())), preferred_element_type=jnp.float32
        ) * score_scale
        scores = jnp.where(allowed_of(dist), scores, -1e30)
        s_ref[dist] = scores
        row_max = jnp.maximum(row_max, jnp.max(scores, axis=1, keepdims=True))
    row_total = jnp.zeros((rows, 1), jnp.float32)
    weighted = jnp.zeros((rows, DH), jnp.float32)
    for dist in range(n_blk):
        expos = jnp.where(allowed_of(dist), jnp.exp(s_ref[dist] - row_max), 0.0)
        row_total = row_total + jnp.sum(expos, axis=1, keepdims=True)
        weighted = weighted + jnp.dot(
            expos.astype(jnp.bfloat16), kv_ref[dist, :, DH:], preferred_element_type=jnp.float32
        )
    o_ref[...] = (weighted / row_total).astype(o_ref.dtype)


def attention_pallas(queries, kv_stack, position):
    rows, width = queries.shape
    n_blk = kv_stack.shape[0]
    local_heads = width // DH
    flops = 4 * local_heads * n_blk * rows * rows * DH
    grid_spec = pltpu.PrefetchScalarGridSpec(
        num_scalar_prefetch=1,
        grid=(local_heads,),
        in_specs=[
            pl.BlockSpec((rows, DH), lambda h, pos: (0, h)),
            pl.BlockSpec((n_blk, rows, 2 * DH), lambda h, pos: (0, 0, 0)),
        ],
        out_specs=pl.BlockSpec((rows, DH), lambda h, pos: (0, h)),
        scratch_shapes=[pltpu.VMEM((n_blk, rows, rows), jnp.float32)],
    )
    return pl.pallas_call(
        attention_kernel,
        grid_spec=grid_spec,
        out_shape=jax.ShapeDtypeStruct((rows, width), jnp.bfloat16),
        compiler_params=pltpu.CompilerParams(dimension_semantics=("arbitrary",)),
        cost_estimate=pl.CostEstimate(
            flops=flops,
            transcendentals=local_heads * n_blk * rows * rows,
            bytes_accessed=2 * queries.size * 2 + kv_stack.size * 2,
        ),
    )(jnp.reshape(position, (1,)).astype(jnp.int32), queries, kv_stack)


def shards_fast(*args):
    return shards_fast_body(*args)


def shards_fast_body(
    lin_query, lin_key, lin_value, log_decay, stream, out_weight, norm_gain, query_weight, kv_weight
):
    n_heads = lax.axis_size("heads")
    n_seq = lax.axis_size("seq")
    tok_rows = lin_query.shape[0]
    heads_here = log_decay.shape[1]
    mine_a = lax.axis_index("heads")
    mine_b = lax.axis_index("seq")
    swap = [(x * n_seq + y, y * n_seq + x) for x in range(n_heads) for y in range(n_seq)]
    gain_rows = jnp.broadcast_to(norm_gain[None, :], (16, norm_gain.shape[0]))
    packed = lax.ppermute(
        jnp.concatenate([stream, gain_rows], axis=0), ("heads", "seq"), swap
    )
    stream_t = packed[:tok_rows]
    gain_b = packed[tok_rows]

    lin_out = lightning_local(lin_query, lin_key, lin_value, log_decay)
    halves = []
    half_rows = tok_rows // 2
    cut = 3 * tok_rows // 4 if tok_rows % 32 == 0 else half_rows
    for lo, hi in ((0, cut), (cut, tok_rows)):
        lin_all = lax.all_gather(lin_out[lo:hi], "seq", axis=0, tiled=True)
        part = jnp.dot(lin_all, out_weight, preferred_element_type=jnp.float32)
        halves.append(heads_reduce_scatter(part.astype(jnp.bfloat16), n_heads))
    own_sum = jnp.concatenate(halves, axis=0)
    mixed_sum = stream_t.astype(jnp.float32) + own_sum
    next_t = mixed_sum.astype(jnp.bfloat16)
    next_early = lax.ppermute(next_t[:half_rows], ("heads", "seq"), swap)
    next_late = lax.ppermute(next_t[half_rows:], ("heads", "seq"), swap)
    stream_next = jnp.concatenate([next_early, next_late], axis=0)
    total_sq = lax.psum(jnp.sum(mixed_sum * mixed_sum, axis=1), "seq")
    normed = (
        mixed_sum
        * lax.rsqrt(total_sq / D + 1e-05)[:, None]
        * gain_b.astype(jnp.float32)[None, :]
    ).astype(jnp.bfloat16)
    normed_all = lax.all_gather(normed, "heads", axis=0, tiled=True)
    kv_group = mine_a * heads_here // (QUERY_HEADS // KVH)
    kv_mine = lax.dynamic_index_in_dim(kv_weight, kv_group, 0, keepdims=False)
    q_part = jnp.dot(normed_all, query_weight, preferred_element_type=jnp.float32)
    kv_part = jnp.dot(normed_all, kv_mine, preferred_element_type=jnp.float32)
    queries = lax.psum_scatter(q_part.astype(jnp.bfloat16), "seq", scatter_dimension=0, tiled=True)
    kv_own = lax.psum_scatter(kv_part.astype(jnp.bfloat16), "seq", scatter_dimension=0, tiled=True)
    earlier_kv = [from_behind(kv_own, "seq", dist) for dist in range(1, n_seq)]
    kv_stack = jnp.stack([kv_own] + earlier_kv, axis=0)
    attended = attention_pallas(queries, kv_stack, mine_b)
    return (stream_next, attended)


def solution(mesh):
    n_heads = mesh.shape["heads"]
    n_seq = mesh.shape["seq"]
    fast_ok = n_heads == n_seq and QUERY_HEADS % n_heads == 0
    if fast_ok:
        heads_here = QUERY_HEADS // n_heads
        fast_ok = (QUERY_HEADS // KVH) % heads_here == 0 and D % n_seq == 0
    shards = shards_fast if fast_ok else shards_base

    return jax.shard_map(
        shards,
        mesh=mesh,
        in_specs=(
            P(("groups", "seq"), "heads"),
            P(("groups", "seq"), "heads"),
            P(("groups", "seq"), "heads"),
            P(("groups", "seq"), "heads"),
            P(("groups", "seq"), "heads"),
            P("heads", "seq"),
            P("heads"),
            P("seq", "heads"),
            P(None, "seq", None),
        ),
        out_specs=(P(("groups", "seq"), "heads"), P(("groups", "seq"), "heads")),
        check_vma=False,
    )
```

```python
import jax
import jax.numpy as jnp
from jax import lax
from jax.experimental import pallas as pl
from jax.experimental.pallas import tpu as pltpu
from jax.sharding import PartitionSpec as P

D = 6144
QUERY_HEADS = 32
KVH = 4
DH = 128
BLOCK = 256


def from_behind(value, axis, steps):
    count = lax.axis_size(axis)
    leading, last = (max(0, -steps), min(count, count - steps))
    return lax.ppermute(value, axis, [(source, source + steps) for source in range(leading, last)])


def lightning_block(kv_state, block_inputs):
    query_blk, key_blk, value_blk, decay_blk = block_inputs
    block_len = query_blk.shape[0]
    local_cum = jnp.cumsum(decay_blk, axis=0)
    causal_mask = (jnp.arange(block_len)[:, None] >= jnp.arange(block_len)[None, :])[:, :, None]
    decay_diff = local_cum[:, None, :] - local_cum[None, :, :]
    decays = jnp.where(causal_mask, jnp.exp(jnp.where(causal_mask, decay_diff, 0.0)), 0.0)
    scores = jnp.einsum("thd,shd->hts", query_blk, key_blk, preferred_element_type=jnp.float32)
    weights = (scores * jnp.transpose(decays, (2, 0, 1))).astype(jnp.bfloat16)
    intra_out = jnp.einsum("hts,shd->thd", weights, value_blk, preferred_element_type=jnp.float32)
    query_f = query_blk.astype(jnp.float32)
    inter_out = jnp.einsum(
        "thd,hde->the",
        query_f * jnp.exp(local_cum)[:, :, None],
        kv_state,
        precision=lax.Precision.HIGHEST,
    )
    tail_decay = jnp.exp(local_cum[-1][None, :] - local_cum)
    key_f = key_blk.astype(jnp.float32) * tail_decay[:, :, None]
    kv_state = jnp.exp(local_cum[-1])[:, None, None] * kv_state + jnp.einsum(
        "shd,she->hde", key_f, value_blk.astype(jnp.float32), precision=lax.Precision.HIGHEST
    )
    return (kv_state, intra_out + inter_out)


def block_state(kv_state, key_blk, value_blk, decay_blk):
    local_cum = jnp.cumsum(decay_blk, axis=0)
    tail_decay = jnp.exp(local_cum[-1][None, :] - local_cum)
    key_f = key_blk.astype(jnp.float32) * tail_decay[:, :, None]
    return jnp.exp(local_cum[-1])[:, None, None] * kv_state + jnp.einsum(
        "shd,she->hde", key_f, value_blk.astype(jnp.float32), precision=lax.Precision.HIGHEST
    )


def shards_base(
    lin_query, lin_key, lin_value, log_decay, stream, out_weight, norm_gain, query_weight, kv_weight
):
    tok_rows = lin_query.shape[0]
    heads_here = log_decay.shape[1]
    head_width = heads_here * DH
    nblocks = tok_rows // BLOCK
    block_shape = (nblocks, BLOCK, heads_here, DH)
    inputs = (
        lin_query.reshape(block_shape),
        lin_key.reshape(block_shape),
        lin_value.reshape(block_shape),
        log_decay.reshape(nblocks, BLOCK, heads_here),
    )
    start_state = jnp.zeros((heads_here, DH, DH), jnp.float32)
    local_state, local_out = lax.scan(lightning_block, start_state, inputs)
    local_out = local_out.reshape(tok_rows, heads_here, DH)
    decay_total = jnp.sum(log_decay, axis=0)
    totals, states = (
        lax.all_gather(decay_total[None].astype(jnp.bfloat16), "seq", axis=0, tiled=True).astype(
            jnp.float32
        ),
        lax.all_gather(local_state[None].astype(jnp.bfloat16), "seq", axis=0, tiled=True).astype(
            jnp.float32
        ),
    )
    position = lax.axis_index("seq")
    device_order = jnp.arange(totals.shape[0])
    earlier = (device_order < position)[:, None]
    before = jnp.sum(jnp.where(earlier, totals, 0.0), axis=0)
    inclusive = jnp.cumsum(totals, axis=0)
    factors = jnp.where(earlier, jnp.exp(jnp.where(earlier, before[None, :] - inclusive, 0.0)), 0.0)
    incoming = jnp.einsum("jh,jhde->hde", factors, states, precision=lax.Precision.HIGHEST)
    running = jnp.cumsum(log_decay, axis=0)
    query_f = (
        lin_query.reshape(tok_rows, heads_here, DH).astype(jnp.float32)
        * jnp.exp(running)[:, :, None]
    )
    carried = jnp.einsum("thd,hde->the", query_f, incoming, precision=lax.Precision.HIGHEST)
    lin_raw = local_out + carried
    lin_out = (
        (lin_raw * lax.rsqrt(jnp.mean(lin_raw * lin_raw, axis=-1, keepdims=True) + 1e-06))
        .astype(jnp.bfloat16)
        .reshape(tok_rows, head_width)
    )
    branch = jnp.dot(
        lin_out,
        lax.all_gather(out_weight, "seq", axis=1, tiled=True),
        preferred_element_type=jnp.float32,
    )
    kv_group = lax.axis_index("heads") * heads_here // (QUERY_HEADS // KVH)
    kv_mine = lax.dynamic_index_in_dim(kv_weight, kv_group, 0, keepdims=False)
    query_rows, kv_rows = (
        lax.all_gather(query_weight, "seq", axis=0, tiled=True),
        lax.all_gather(kv_mine, "seq", axis=0, tiled=True),
    )
    projection = jnp.concatenate([query_rows, kv_rows], axis=1)
    own_sum = lax.psum_scatter(
        branch.astype(jnp.bfloat16), "heads", scatter_dimension=1, tiled=True
    ).astype(jnp.float32)
    mixed_sum = stream.astype(jnp.float32) + own_sum
    stream_next = mixed_sum.astype(jnp.bfloat16)
    total_sq = lax.psum(jnp.sum(mixed_sum * mixed_sum, axis=1), "heads")
    normed = (
        mixed_sum
        * lax.rsqrt(total_sq / D + 1e-05)[:, None]
        * norm_gain.astype(jnp.float32)[None, :]
    ).astype(jnp.bfloat16)
    projected = jnp.dot(
        lax.all_gather(normed, "heads", axis=1, tiled=True),
        projection,
        preferred_element_type=jnp.float32,
    )
    projected = projected.astype(jnp.bfloat16)
    queries = projected[:, :head_width].reshape(tok_rows, heads_here, DH)
    keys_values = projected[:, head_width:]
    position = lax.axis_index("seq")
    query_pos = position * tok_rows + jnp.arange(tok_rows)
    score_scale = float(DH) ** (-0.5)

    def attend(state_in, kv_block, key_start):
        old_max, row_total, weighted = state_in
        key_count = kv_block.shape[0]
        key_part = kv_block[:, :DH]
        value_part = kv_block[:, DH:]
        scores = (
            jnp.einsum("thd,sd->hts", queries, key_part, preferred_element_type=jnp.float32)
            * score_scale
        )
        key_pos = key_start + jnp.arange(key_count)
        allowed = ((key_pos[None, :] <= query_pos[:, None]) & (key_pos[None, :] >= 0))[None, :, :]
        scores = jnp.where(allowed, scores, -1e30)
        new_max = jnp.maximum(old_max, jnp.max(scores, axis=-1))
        expos = jnp.where(allowed, jnp.exp(scores - new_max[:, :, None]), 0.0)
        rescale = jnp.exp(old_max - new_max)
        row_total = row_total * rescale + jnp.sum(expos, axis=-1)
        prob_bf16 = expos.astype(jnp.bfloat16)
        weighted = weighted * rescale[:, :, None] + jnp.einsum(
            "hts,sd->htd", prob_bf16, value_part, preferred_element_type=jnp.float32
        )
        return (new_max, row_total, weighted)

    initial = (
        jnp.full((heads_here, tok_rows), -1e30, jnp.float32),
        jnp.zeros((heads_here, tok_rows), jnp.float32),
        jnp.zeros((heads_here, tok_rows, DH), jnp.float32),
    )
    first_state = attend(initial, keys_values, position * tok_rows)
    seq_count = lax.axis_size("seq")

    def cycle_turn(turn_index, loop_state):
        moving, inner_state = loop_state
        moving = from_behind(moving, "seq", 1)
        source = position - turn_index
        return (moving, attend(inner_state, moving, source * tok_rows))

    _, final_state = lax.fori_loop(1, seq_count, cycle_turn, (keys_values, first_state))
    _, row_total, weighted = final_state
    attended = (
        jnp.transpose(weighted / row_total[:, :, None], (1, 0, 2))
        .reshape(tok_rows, head_width)
        .astype(jnp.bfloat16)
    )
    return (stream_next, attended)


def lightning_local(lin_query, lin_key, lin_value, log_decay):
    tok_rows = lin_query.shape[0]
    heads_here = log_decay.shape[1]
    nblocks = tok_rows // BLOCK
    shape4 = (tok_rows, heads_here, DH)
    q4, k4, v4 = (x.reshape(shape4) for x in (lin_query, lin_key, lin_value))
    state = jnp.zeros((heads_here, DH, DH), jnp.float32)
    starts = []
    for blk in range(nblocks):
        rows = slice(blk * BLOCK, (blk + 1) * BLOCK)
        starts.append(state)
        state = block_state(state, k4[rows], v4[rows], log_decay[rows])
    decay_total = jnp.sum(log_decay, axis=0)
    pad_rows = 16
    total_rows = jnp.broadcast_to(decay_total[:, None, None], (heads_here, pad_rows, DH))
    packed = jnp.concatenate([state, total_rows], axis=1).astype(jnp.bfloat16)
    packed, starts, lin_query, k4, v4 = lax.optimization_barrier(
        (packed, starts, lin_query, k4, v4)
    )
    q4 = lin_query.reshape(shape4)
    outs = []
    for blk in range(nblocks):
        rows = slice(blk * BLOCK, (blk + 1) * BLOCK)
        _, out = lightning_block(starts[blk], (q4[rows], k4[rows], v4[rows], log_decay[rows]))
        outs.append(out)
    local_out = jnp.concatenate(outs, axis=0)
    gathered = lax.all_gather(packed[None], "seq", axis=0, tiled=True)
    gathered = gathered.astype(jnp.float32)
    states = gathered[:, :, :DH, :]
    totals = gathered[:, :, DH, 0]
    position = lax.axis_index("seq")
    device_order = jnp.arange(totals.shape[0])
    earlier = (device_order < position)[:, None]
    before = jnp.sum(jnp.where(earlier, totals, 0.0), axis=0)
    inclusive = jnp.cumsum(totals, axis=0)
    factors = jnp.where(earlier, jnp.exp(jnp.where(earlier, before[None, :] - inclusive, 0.0)), 0.0)
    incoming = jnp.einsum("jh,jhde->hde", factors, states, precision=lax.Precision.HIGHEST)
    running = jnp.cumsum(log_decay, axis=0)
    query_f = q4.astype(jnp.float32) * jnp.exp(running)[:, :, None]
    carried = jnp.einsum("thd,hde->the", query_f, incoming, precision=lax.Precision.HIGHEST)
    lin_raw = local_out + carried
    lin_out = (
        (lin_raw * lax.rsqrt(jnp.mean(lin_raw * lin_raw, axis=-1, keepdims=True) + 1e-06))
        .astype(jnp.bfloat16)
        .reshape(tok_rows, heads_here * DH)
    )
    return lin_out


def heads_reduce_scatter(part, n_heads):
    if n_heads != 4:
        return lax.psum_scatter(part, "heads", scatter_dimension=0, tiled=True).astype(jnp.float32)
    mine = lax.axis_index("heads")
    core = mine % 2
    chip = mine // 2
    rows = part.shape[0] // n_heads
    grid = part.reshape(2, 2, rows, part.shape[1])
    keep1 = lax.dynamic_index_in_dim(grid, core, axis=1, keepdims=False)
    send1 = lax.dynamic_index_in_dim(grid, 1 - core, axis=1, keepdims=False)
    recv1 = lax.ppermute(send1, "heads", [(i, i ^ 1) for i in range(n_heads)])
    chip_sum = keep1.astype(jnp.float32) + recv1.astype(jnp.float32)
    keep2 = lax.dynamic_index_in_dim(chip_sum, chip, axis=0, keepdims=False)
    send2 = lax.dynamic_index_in_dim(chip_sum, 1 - chip, axis=0, keepdims=False)
    recv2 = lax.ppermute(send2.astype(jnp.bfloat16), "heads", [(i, i ^ 2) for i in range(n_heads)])
    return keep2 + recv2.astype(jnp.float32)


def attention_kernel(pos_ref, q_ref, kv_ref, o_ref, s_ref):
    position = pos_ref[0]
    n_blk = kv_ref.shape[0]
    rows = q_ref.shape[0]
    score_scale = float(DH) ** (-0.5)
    query = q_ref[...]
    row_id = lax.broadcasted_iota(jnp.int32, (rows, rows), 0)
    col_id = lax.broadcasted_iota(jnp.int32, (rows, rows), 1)

    def allowed_of(dist):
        if dist == 0:
            return col_id <= row_id
        return jnp.broadcast_to(dist <= position, (rows, rows))

    row_max = jnp.full((rows, 1), -1e30, jnp.float32)
    for dist in range(n_blk):
        key = kv_ref[dist, :, :DH]
        scores = lax.dot_general(
            query, key, (((1,), (1,)), ((), ())), preferred_element_type=jnp.float32
        ) * score_scale
        scores = jnp.where(allowed_of(dist), scores, -1e30)
        s_ref[dist] = scores
        row_max = jnp.maximum(row_max, jnp.max(scores, axis=1, keepdims=True))
    row_total = jnp.zeros((rows, 1), jnp.float32)
    weighted = jnp.zeros((rows, DH), jnp.float32)
    for dist in range(n_blk):
        expos = jnp.exp(s_ref[dist] - row_max)
        row_total = row_total + jnp.sum(expos, axis=1, keepdims=True)
        weighted = weighted + jnp.dot(
            expos.astype(jnp.bfloat16), kv_ref[dist, :, DH:], preferred_element_type=jnp.float32
        )
    o_ref[...] = (weighted / row_total).astype(o_ref.dtype)


def attention_pallas(queries, kv_stack, position):
    rows, width = queries.shape
    n_blk = kv_stack.shape[0]
    local_heads = width // DH
    flops = 4 * local_heads * n_blk * rows * rows * DH
    grid_spec = pltpu.PrefetchScalarGridSpec(
        num_scalar_prefetch=1,
        grid=(local_heads,),
        in_specs=[
            pl.BlockSpec((rows, DH), lambda h, pos: (0, h)),
            pl.BlockSpec((n_blk, rows, 2 * DH), lambda h, pos: (0, 0, 0)),
        ],
        out_specs=pl.BlockSpec((rows, DH), lambda h, pos: (0, h)),
        scratch_shapes=[pltpu.VMEM((n_blk, rows, rows), jnp.float32)],
    )
    return pl.pallas_call(
        attention_kernel,
        grid_spec=grid_spec,
        out_shape=jax.ShapeDtypeStruct((rows, width), jnp.bfloat16),
        compiler_params=pltpu.CompilerParams(dimension_semantics=("arbitrary",)),
        cost_estimate=pl.CostEstimate(
            flops=flops,
            transcendentals=local_heads * n_blk * rows * rows,
            bytes_accessed=2 * queries.size * 2 + kv_stack.size * 2,
        ),
    )(jnp.reshape(position, (1,)).astype(jnp.int32), queries, kv_stack)


def shards_fast(*args):
    return shards_fast_body(*args)


def shards_fast_body(
    lin_query, lin_key, lin_value, log_decay, stream, out_weight, norm_gain, query_weight, kv_weight
):
    n_heads = lax.axis_size("heads")
    n_seq = lax.axis_size("seq")
    tok_rows = lin_query.shape[0]
    heads_here = log_decay.shape[1]
    mine_a = lax.axis_index("heads")
    mine_b = lax.axis_index("seq")
    swap = [(x * n_seq + y, y * n_seq + x) for x in range(n_heads) for y in range(n_seq)]
    gain_rows = jnp.broadcast_to(norm_gain[None, :], (16, norm_gain.shape[0]))
    packed = lax.ppermute(
        jnp.concatenate([stream, gain_rows], axis=0), ("heads", "seq"), swap
    )
    stream_t = packed[:tok_rows]
    gain_b = packed[tok_rows]

    lin_out = lightning_local(lin_query, lin_key, lin_value, log_decay)
    halves = []
    half_rows = tok_rows // 2
    for half in range(2):
        lin_all = lax.all_gather(
            lin_out[half * half_rows : (half + 1) * half_rows], "seq", axis=0, tiled=True
        )
        part = jnp.dot(lin_all, out_weight, preferred_element_type=jnp.float32)
        halves.append(heads_reduce_scatter(part.astype(jnp.bfloat16), n_heads))
    own_sum = jnp.concatenate(halves, axis=0)
    mixed_sum = stream_t.astype(jnp.float32) + own_sum
    next_t = mixed_sum.astype(jnp.bfloat16)
    next_early = lax.ppermute(next_t[:half_rows], ("heads", "seq"), swap)
    next_late = lax.ppermute(next_t[half_rows:], ("heads", "seq"), swap)
    stream_next = jnp.concatenate([next_early, next_late], axis=0)
    total_sq = lax.psum(jnp.sum(mixed_sum * mixed_sum, axis=1), "seq")
    normed = (
        mixed_sum
        * lax.rsqrt(total_sq / D + 1e-05)[:, None]
        * gain_b.astype(jnp.float32)[None, :]
    ).astype(jnp.bfloat16)
    normed_all = lax.all_gather(normed, "heads", axis=0, tiled=True)
    kv_group = mine_a * heads_here // (QUERY_HEADS // KVH)
    kv_mine = lax.dynamic_index_in_dim(kv_weight, kv_group, 0, keepdims=False)
    q_part = jnp.dot(normed_all, query_weight, preferred_element_type=jnp.float32)
    kv_part = jnp.dot(normed_all, kv_mine, preferred_element_type=jnp.float32)
    queries = lax.psum_scatter(q_part.astype(jnp.bfloat16), "seq", scatter_dimension=0, tiled=True)
    kv_own = lax.psum_scatter(kv_part.astype(jnp.bfloat16), "seq", scatter_dimension=0, tiled=True)
    earlier_kv = [from_behind(kv_own, "seq", dist) for dist in range(1, n_seq)]
    kv_stack = jnp.stack([kv_own] + earlier_kv, axis=0)
    attended = attention_pallas(queries, kv_stack, mine_b)
    return (stream_next, attended)


def solution(mesh):
    n_heads = mesh.shape["heads"]
    n_seq = mesh.shape["seq"]
    fast_ok = n_heads == n_seq and QUERY_HEADS % n_heads == 0
    if fast_ok:
        heads_here = QUERY_HEADS // n_heads
        fast_ok = (QUERY_HEADS // KVH) % heads_here == 0 and D % n_seq == 0
    shards = shards_fast if fast_ok else shards_base

    return jax.shard_map(
        shards,
        mesh=mesh,
        in_specs=(
            P(("groups", "seq"), "heads"),
            P(("groups", "seq"), "heads"),
            P(("groups", "seq"), "heads"),
            P(("groups", "seq"), "heads"),
            P(("groups", "seq"), "heads"),
            P("heads", "seq"),
            P("heads"),
            P("seq", "heads"),
            P(None, "seq", None),
        ),
        out_specs=(P(("groups", "seq"), "heads"), P(("groups", "seq"), "heads")),
        check_vma=False,
    )
```

```python
import jax
import jax.numpy as jnp
from jax import lax
from jax.experimental import pallas as pl
from jax.experimental.pallas import tpu as pltpu
from jax.sharding import PartitionSpec as P

D = 6144
QUERY_HEADS = 32
KVH = 4
DH = 128
BLOCK = 256


def from_behind(value, axis, steps):
    count = lax.axis_size(axis)
    leading, last = (max(0, -steps), min(count, count - steps))
    return lax.ppermute(value, axis, [(source, source + steps) for source in range(leading, last)])


def lightning_block(kv_state, block_inputs):
    query_blk, key_blk, value_blk, decay_blk = block_inputs
    block_len = query_blk.shape[0]
    local_cum = jnp.cumsum(decay_blk, axis=0)
    causal_mask = (jnp.arange(block_len)[:, None] >= jnp.arange(block_len)[None, :])[:, :, None]
    decay_diff = local_cum[:, None, :] - local_cum[None, :, :]
    decays = jnp.where(causal_mask, jnp.exp(jnp.where(causal_mask, decay_diff, 0.0)), 0.0)
    scores = jnp.einsum("thd,shd->hts", query_blk, key_blk, preferred_element_type=jnp.float32)
    weights = (scores * jnp.transpose(decays, (2, 0, 1))).astype(jnp.bfloat16)
    intra_out = jnp.einsum("hts,shd->thd", weights, value_blk, preferred_element_type=jnp.float32)
    query_f = query_blk.astype(jnp.float32)
    inter_out = jnp.einsum(
        "thd,hde->the",
        query_f * jnp.exp(local_cum)[:, :, None],
        kv_state,
        precision=lax.Precision.HIGHEST,
    )
    tail_decay = jnp.exp(local_cum[-1][None, :] - local_cum)
    key_f = key_blk.astype(jnp.float32) * tail_decay[:, :, None]
    kv_state = jnp.exp(local_cum[-1])[:, None, None] * kv_state + jnp.einsum(
        "shd,she->hde", key_f, value_blk.astype(jnp.float32), precision=lax.Precision.HIGHEST
    )
    return (kv_state, intra_out + inter_out)


def block_state(kv_state, key_blk, value_blk, decay_blk):
    local_cum = jnp.cumsum(decay_blk, axis=0)
    tail_decay = jnp.exp(local_cum[-1][None, :] - local_cum)
    key_f = key_blk.astype(jnp.float32) * tail_decay[:, :, None]
    return jnp.exp(local_cum[-1])[:, None, None] * kv_state + jnp.einsum(
        "shd,she->hde", key_f, value_blk.astype(jnp.float32), precision=lax.Precision.HIGHEST
    )


def shards_base(
    lin_query, lin_key, lin_value, log_decay, stream, out_weight, norm_gain, query_weight, kv_weight
):
    tok_rows = lin_query.shape[0]
    heads_here = log_decay.shape[1]
    head_width = heads_here * DH
    nblocks = tok_rows // BLOCK
    block_shape = (nblocks, BLOCK, heads_here, DH)
    inputs = (
        lin_query.reshape(block_shape),
        lin_key.reshape(block_shape),
        lin_value.reshape(block_shape),
        log_decay.reshape(nblocks, BLOCK, heads_here),
    )
    start_state = jnp.zeros((heads_here, DH, DH), jnp.float32)
    local_state, local_out = lax.scan(lightning_block, start_state, inputs)
    local_out = local_out.reshape(tok_rows, heads_here, DH)
    decay_total = jnp.sum(log_decay, axis=0)
    totals, states = (
        lax.all_gather(decay_total[None].astype(jnp.bfloat16), "seq", axis=0, tiled=True).astype(
            jnp.float32
        ),
        lax.all_gather(local_state[None].astype(jnp.bfloat16), "seq", axis=0, tiled=True).astype(
            jnp.float32
        ),
    )
    position = lax.axis_index("seq")
    device_order = jnp.arange(totals.shape[0])
    earlier = (device_order < position)[:, None]
    before = jnp.sum(jnp.where(earlier, totals, 0.0), axis=0)
    inclusive = jnp.cumsum(totals, axis=0)
    factors = jnp.where(earlier, jnp.exp(jnp.where(earlier, before[None, :] - inclusive, 0.0)), 0.0)
    incoming = jnp.einsum("jh,jhde->hde", factors, states, precision=lax.Precision.HIGHEST)
    running = jnp.cumsum(log_decay, axis=0)
    query_f = (
        lin_query.reshape(tok_rows, heads_here, DH).astype(jnp.float32)
        * jnp.exp(running)[:, :, None]
    )
    carried = jnp.einsum("thd,hde->the", query_f, incoming, precision=lax.Precision.HIGHEST)
    lin_raw = local_out + carried
    lin_out = (
        (lin_raw * lax.rsqrt(jnp.mean(lin_raw * lin_raw, axis=-1, keepdims=True) + 1e-06))
        .astype(jnp.bfloat16)
        .reshape(tok_rows, head_width)
    )
    branch = jnp.dot(
        lin_out,
        lax.all_gather(out_weight, "seq", axis=1, tiled=True),
        preferred_element_type=jnp.float32,
    )
    kv_group = lax.axis_index("heads") * heads_here // (QUERY_HEADS // KVH)
    kv_mine = lax.dynamic_index_in_dim(kv_weight, kv_group, 0, keepdims=False)
    query_rows, kv_rows = (
        lax.all_gather(query_weight, "seq", axis=0, tiled=True),
        lax.all_gather(kv_mine, "seq", axis=0, tiled=True),
    )
    projection = jnp.concatenate([query_rows, kv_rows], axis=1)
    own_sum = lax.psum_scatter(
        branch.astype(jnp.bfloat16), "heads", scatter_dimension=1, tiled=True
    ).astype(jnp.float32)
    mixed_sum = stream.astype(jnp.float32) + own_sum
    stream_next = mixed_sum.astype(jnp.bfloat16)
    total_sq = lax.psum(jnp.sum(mixed_sum * mixed_sum, axis=1), "heads")
    normed = (
        mixed_sum
        * lax.rsqrt(total_sq / D + 1e-05)[:, None]
        * norm_gain.astype(jnp.float32)[None, :]
    ).astype(jnp.bfloat16)
    projected = jnp.dot(
        lax.all_gather(normed, "heads", axis=1, tiled=True),
        projection,
        preferred_element_type=jnp.float32,
    )
    projected = projected.astype(jnp.bfloat16)
    queries = projected[:, :head_width].reshape(tok_rows, heads_here, DH)
    keys_values = projected[:, head_width:]
    position = lax.axis_index("seq")
    query_pos = position * tok_rows + jnp.arange(tok_rows)
    score_scale = float(DH) ** (-0.5)

    def attend(state_in, kv_block, key_start):
        old_max, row_total, weighted = state_in
        key_count = kv_block.shape[0]
        key_part = kv_block[:, :DH]
        value_part = kv_block[:, DH:]
        scores = (
            jnp.einsum("thd,sd->hts", queries, key_part, preferred_element_type=jnp.float32)
            * score_scale
        )
        key_pos = key_start + jnp.arange(key_count)
        allowed = ((key_pos[None, :] <= query_pos[:, None]) & (key_pos[None, :] >= 0))[None, :, :]
        scores = jnp.where(allowed, scores, -1e30)
        new_max = jnp.maximum(old_max, jnp.max(scores, axis=-1))
        expos = jnp.where(allowed, jnp.exp(scores - new_max[:, :, None]), 0.0)
        rescale = jnp.exp(old_max - new_max)
        row_total = row_total * rescale + jnp.sum(expos, axis=-1)
        prob_bf16 = expos.astype(jnp.bfloat16)
        weighted = weighted * rescale[:, :, None] + jnp.einsum(
            "hts,sd->htd", prob_bf16, value_part, preferred_element_type=jnp.float32
        )
        return (new_max, row_total, weighted)

    initial = (
        jnp.full((heads_here, tok_rows), -1e30, jnp.float32),
        jnp.zeros((heads_here, tok_rows), jnp.float32),
        jnp.zeros((heads_here, tok_rows, DH), jnp.float32),
    )
    first_state = attend(initial, keys_values, position * tok_rows)
    seq_count = lax.axis_size("seq")

    def cycle_turn(turn_index, loop_state):
        moving, inner_state = loop_state
        moving = from_behind(moving, "seq", 1)
        source = position - turn_index
        return (moving, attend(inner_state, moving, source * tok_rows))

    _, final_state = lax.fori_loop(1, seq_count, cycle_turn, (keys_values, first_state))
    _, row_total, weighted = final_state
    attended = (
        jnp.transpose(weighted / row_total[:, :, None], (1, 0, 2))
        .reshape(tok_rows, head_width)
        .astype(jnp.bfloat16)
    )
    return (stream_next, attended)


def lightning_local(lin_query, lin_key, lin_value, log_decay):
    tok_rows = lin_query.shape[0]
    heads_here = log_decay.shape[1]
    nblocks = tok_rows // BLOCK
    shape4 = (tok_rows, heads_here, DH)
    q4, k4, v4 = (x.reshape(shape4) for x in (lin_query, lin_key, lin_value))
    state = jnp.zeros((heads_here, DH, DH), jnp.float32)
    starts = []
    for blk in range(nblocks):
        rows = slice(blk * BLOCK, (blk + 1) * BLOCK)
        starts.append(state)
        state = block_state(state, k4[rows], v4[rows], log_decay[rows])
    decay_total = jnp.sum(log_decay, axis=0)
    pad_rows = 16
    total_rows = jnp.broadcast_to(decay_total[:, None, None], (heads_here, pad_rows, DH))
    packed = jnp.concatenate([state, total_rows], axis=1).astype(jnp.bfloat16)
    packed, starts, lin_query, k4, v4 = lax.optimization_barrier(
        (packed, starts, lin_query, k4, v4)
    )
    q4 = lin_query.reshape(shape4)
    outs = []
    for blk in range(nblocks):
        rows = slice(blk * BLOCK, (blk + 1) * BLOCK)
        _, out = lightning_block(starts[blk], (q4[rows], k4[rows], v4[rows], log_decay[rows]))
        outs.append(out)
    local_out = jnp.concatenate(outs, axis=0)
    gathered = lax.all_gather(packed[None], "seq", axis=0, tiled=True)
    gathered = gathered.astype(jnp.float32)
    states = gathered[:, :, :DH, :]
    totals = gathered[:, :, DH, 0]
    position = lax.axis_index("seq")
    device_order = jnp.arange(totals.shape[0])
    earlier = (device_order < position)[:, None]
    before = jnp.sum(jnp.where(earlier, totals, 0.0), axis=0)
    inclusive = jnp.cumsum(totals, axis=0)
    factors = jnp.where(earlier, jnp.exp(jnp.where(earlier, before[None, :] - inclusive, 0.0)), 0.0)
    incoming = jnp.einsum("jh,jhde->hde", factors, states, precision=lax.Precision.HIGHEST)
    running = jnp.cumsum(log_decay, axis=0)
    query_f = q4.astype(jnp.float32) * jnp.exp(running)[:, :, None]
    carried = jnp.einsum("thd,hde->the", query_f, incoming, precision=lax.Precision.HIGHEST)
    lin_raw = local_out + carried
    lin_out = (
        (lin_raw * lax.rsqrt(jnp.mean(lin_raw * lin_raw, axis=-1, keepdims=True) + 1e-06))
        .astype(jnp.bfloat16)
        .reshape(tok_rows, heads_here * DH)
    )
    return lin_out


def heads_reduce_scatter(part, n_heads):
    if n_heads != 4:
        return lax.psum_scatter(part, "heads", scatter_dimension=0, tiled=True).astype(jnp.float32)
    mine = lax.axis_index("heads")
    core = mine % 2
    chip = mine // 2
    rows = part.shape[0] // n_heads
    grid = part.reshape(2, 2, rows, part.shape[1])
    keep1 = lax.dynamic_index_in_dim(grid, core, axis=1, keepdims=False)
    send1 = lax.dynamic_index_in_dim(grid, 1 - core, axis=1, keepdims=False)
    recv1 = lax.ppermute(send1, "heads", [(i, i ^ 1) for i in range(n_heads)])
    chip_sum = keep1.astype(jnp.float32) + recv1.astype(jnp.float32)
    keep2 = lax.dynamic_index_in_dim(chip_sum, chip, axis=0, keepdims=False)
    send2 = lax.dynamic_index_in_dim(chip_sum, 1 - chip, axis=0, keepdims=False)
    recv2 = lax.ppermute(send2.astype(jnp.bfloat16), "heads", [(i, i ^ 2) for i in range(n_heads)])
    return keep2 + recv2.astype(jnp.float32)


def attention_kernel(pos_ref, q_ref, kv_ref, o_ref, s_ref):
    position = pos_ref[0]
    n_blk = kv_ref.shape[0]
    rows = q_ref.shape[0]
    score_scale = float(DH) ** (-0.5)
    query = q_ref[...]
    row_id = lax.broadcasted_iota(jnp.int32, (rows, rows), 0)
    col_id = lax.broadcasted_iota(jnp.int32, (rows, rows), 1)

    def allowed_of(dist):
        if dist == 0:
            return col_id <= row_id
        return jnp.broadcast_to(dist <= position, (rows, rows))

    row_max = jnp.full((rows, 1), -1e30, jnp.float32)
    for dist in range(n_blk):
        key = kv_ref[dist, :, :DH]
        scores = lax.dot_general(
            query, key, (((1,), (1,)), ((), ())), preferred_element_type=jnp.float32
        ) * score_scale
        scores = jnp.where(allowed_of(dist), scores, -1e30)
        s_ref[dist] = scores
        row_max = jnp.maximum(row_max, jnp.max(scores, axis=1, keepdims=True))
    row_total = jnp.zeros((rows, 1), jnp.float32)
    weighted = jnp.zeros((rows, DH), jnp.float32)
    for dist in range(n_blk):
        expos = jnp.where(allowed_of(dist), jnp.exp(s_ref[dist] - row_max), 0.0)
        row_total = row_total + jnp.sum(expos, axis=1, keepdims=True)
        weighted = weighted + jnp.dot(
            expos.astype(jnp.bfloat16), kv_ref[dist, :, DH:], preferred_element_type=jnp.float32
        )
    o_ref[...] = (weighted / row_total).astype(o_ref.dtype)


def attention_pallas(queries, kv_stack, position):
    rows, width = queries.shape
    n_blk = kv_stack.shape[0]
    local_heads = width // DH
    flops = 4 * local_heads * n_blk * rows * rows * DH
    grid_spec = pltpu.PrefetchScalarGridSpec(
        num_scalar_prefetch=1,
        grid=(local_heads,),
        in_specs=[
            pl.BlockSpec((rows, DH), lambda h, pos: (0, h)),
            pl.BlockSpec((n_blk, rows, 2 * DH), lambda h, pos: (0, 0, 0)),
        ],
        out_specs=pl.BlockSpec((rows, DH), lambda h, pos: (0, h)),
        scratch_shapes=[pltpu.VMEM((n_blk, rows, rows), jnp.float32)],
    )
    return pl.pallas_call(
        attention_kernel,
        grid_spec=grid_spec,
        out_shape=jax.ShapeDtypeStruct((rows, width), jnp.bfloat16),
        compiler_params=pltpu.CompilerParams(dimension_semantics=("arbitrary",)),
        cost_estimate=pl.CostEstimate(
            flops=flops,
            transcendentals=local_heads * n_blk * rows * rows,
            bytes_accessed=2 * queries.size * 2 + kv_stack.size * 2,
        ),
    )(jnp.reshape(position, (1,)).astype(jnp.int32), queries, kv_stack)


def shards_fast(*args):
    return shards_fast_body(*args)


def shards_fast_body(
    lin_query, lin_key, lin_value, log_decay, stream, out_weight, norm_gain, query_weight, kv_weight
):
    n_heads = lax.axis_size("heads")
    n_seq = lax.axis_size("seq")
    tok_rows = lin_query.shape[0]
    heads_here = log_decay.shape[1]
    mine_a = lax.axis_index("heads")
    mine_b = lax.axis_index("seq")
    swap = [(x * n_seq + y, y * n_seq + x) for x in range(n_heads) for y in range(n_seq)]
    gain_rows = jnp.broadcast_to(norm_gain[None, :], (16, norm_gain.shape[0]))
    split_rows = tok_rows // 2
    packed = lax.ppermute(
        jnp.concatenate([stream[:split_rows], gain_rows], axis=0), ("heads", "seq"), swap
    )
    rest = lax.ppermute(stream[split_rows:], ("heads", "seq"), swap)
    stream_t = jnp.concatenate([packed[:split_rows], rest], axis=0)
    gain_b = packed[split_rows]

    lin_out = lightning_local(lin_query, lin_key, lin_value, log_decay)
    halves = []
    half_rows = tok_rows // 2
    for half in range(2):
        lin_all = lax.all_gather(
            lin_out[half * half_rows : (half + 1) * half_rows], "seq", axis=0, tiled=True
        )
        part = jnp.dot(lin_all, out_weight, preferred_element_type=jnp.float32)
        halves.append(heads_reduce_scatter(part.astype(jnp.bfloat16), n_heads))
    own_sum = jnp.concatenate(halves, axis=0)
    mixed_sum = stream_t.astype(jnp.float32) + own_sum
    next_t = mixed_sum.astype(jnp.bfloat16)
    next_early = lax.ppermute(next_t[:half_rows], ("heads", "seq"), swap)
    next_late = lax.ppermute(next_t[half_rows:], ("heads", "seq"), swap)
    stream_next = jnp.concatenate([next_early, next_late], axis=0)
    total_sq = lax.psum(jnp.sum(mixed_sum * mixed_sum, axis=1), "seq")
    normed = (
        mixed_sum
        * lax.rsqrt(total_sq / D + 1e-05)[:, None]
        * gain_b.astype(jnp.float32)[None, :]
    ).astype(jnp.bfloat16)
    normed_all = lax.all_gather(normed, "heads", axis=0, tiled=True)
    kv_group = mine_a * heads_here // (QUERY_HEADS // KVH)
    kv_mine = lax.dynamic_index_in_dim(kv_weight, kv_group, 0, keepdims=False)
    q_part = jnp.dot(normed_all, query_weight, preferred_element_type=jnp.float32)
    kv_part = jnp.dot(normed_all, kv_mine, preferred_element_type=jnp.float32)
    queries = lax.psum_scatter(q_part.astype(jnp.bfloat16), "seq", scatter_dimension=0, tiled=True)
    kv_own = lax.psum_scatter(kv_part.astype(jnp.bfloat16), "seq", scatter_dimension=0, tiled=True)
    earlier_kv = [from_behind(kv_own, "seq", dist) for dist in range(1, n_seq)]
    kv_stack = jnp.stack([kv_own] + earlier_kv, axis=0)
    attended = attention_pallas(queries, kv_stack, mine_b)
    return (stream_next, attended)


def solution(mesh):
    n_heads = mesh.shape["heads"]
    n_seq = mesh.shape["seq"]
    fast_ok = n_heads == n_seq and QUERY_HEADS % n_heads == 0
    if fast_ok:
        heads_here = QUERY_HEADS // n_heads
        fast_ok = (QUERY_HEADS // KVH) % heads_here == 0 and D % n_seq == 0
    shards = shards_fast if fast_ok else shards_base

    return jax.shard_map(
        shards,
        mesh=mesh,
        in_specs=(
            P(("groups", "seq"), "heads"),
            P(("groups", "seq"), "heads"),
            P(("groups", "seq"), "heads"),
            P(("groups", "seq"), "heads"),
            P(("groups", "seq"), "heads"),
            P("heads", "seq"),
            P("heads"),
            P("seq", "heads"),
            P(None, "seq", None),
        ),
        out_specs=(P(("groups", "seq"), "heads"), P(("groups", "seq"), "heads")),
        check_vma=False,
    )
```

```python
import jax
import jax.numpy as jnp
from jax import lax
from jax.experimental import pallas as pl
from jax.experimental.pallas import tpu as pltpu
from jax.sharding import PartitionSpec as P

D = 6144
QUERY_HEADS = 32
KVH = 4
DH = 128
BLOCK = 256


def from_behind(value, axis, steps):
    count = lax.axis_size(axis)
    leading, last = (max(0, -steps), min(count, count - steps))
    return lax.ppermute(value, axis, [(source, source + steps) for source in range(leading, last)])


def lightning_block(kv_state, block_inputs):
    query_blk, key_blk, value_blk, decay_blk = block_inputs
    block_len = query_blk.shape[0]
    local_cum = jnp.cumsum(decay_blk, axis=0)
    causal_mask = (jnp.arange(block_len)[:, None] >= jnp.arange(block_len)[None, :])[:, :, None]
    decay_diff = local_cum[:, None, :] - local_cum[None, :, :]
    decays = jnp.where(causal_mask, jnp.exp(jnp.where(causal_mask, decay_diff, 0.0)), 0.0)
    scores = jnp.einsum("thd,shd->hts", query_blk, key_blk, preferred_element_type=jnp.float32)
    weights = (scores * jnp.transpose(decays, (2, 0, 1))).astype(jnp.bfloat16)
    intra_out = jnp.einsum("hts,shd->thd", weights, value_blk, preferred_element_type=jnp.float32)
    query_f = query_blk.astype(jnp.float32)
    inter_out = jnp.einsum(
        "thd,hde->the",
        query_f * jnp.exp(local_cum)[:, :, None],
        kv_state,
        precision=lax.Precision.HIGHEST,
    )
    tail_decay = jnp.exp(local_cum[-1][None, :] - local_cum)
    key_f = key_blk.astype(jnp.float32) * tail_decay[:, :, None]
    kv_state = jnp.exp(local_cum[-1])[:, None, None] * kv_state + jnp.einsum(
        "shd,she->hde", key_f, value_blk.astype(jnp.float32), precision=lax.Precision.HIGHEST
    )
    return (kv_state, intra_out + inter_out)


def block_state(kv_state, key_blk, value_blk, decay_blk):
    local_cum = jnp.cumsum(decay_blk, axis=0)
    tail_decay = jnp.exp(local_cum[-1][None, :] - local_cum)
    key_f = key_blk.astype(jnp.float32) * tail_decay[:, :, None]
    return jnp.exp(local_cum[-1])[:, None, None] * kv_state + jnp.einsum(
        "shd,she->hde", key_f, value_blk.astype(jnp.float32), precision=lax.Precision.HIGHEST
    )


def shards_base(
    lin_query, lin_key, lin_value, log_decay, stream, out_weight, norm_gain, query_weight, kv_weight
):
    tok_rows = lin_query.shape[0]
    heads_here = log_decay.shape[1]
    head_width = heads_here * DH
    nblocks = tok_rows // BLOCK
    block_shape = (nblocks, BLOCK, heads_here, DH)
    inputs = (
        lin_query.reshape(block_shape),
        lin_key.reshape(block_shape),
        lin_value.reshape(block_shape),
        log_decay.reshape(nblocks, BLOCK, heads_here),
    )
    start_state = jnp.zeros((heads_here, DH, DH), jnp.float32)
    local_state, local_out = lax.scan(lightning_block, start_state, inputs)
    local_out = local_out.reshape(tok_rows, heads_here, DH)
    decay_total = jnp.sum(log_decay, axis=0)
    totals, states = (
        lax.all_gather(decay_total[None].astype(jnp.bfloat16), "seq", axis=0, tiled=True).astype(
            jnp.float32
        ),
        lax.all_gather(local_state[None].astype(jnp.bfloat16), "seq", axis=0, tiled=True).astype(
            jnp.float32
        ),
    )
    position = lax.axis_index("seq")
    device_order = jnp.arange(totals.shape[0])
    earlier = (device_order < position)[:, None]
    before = jnp.sum(jnp.where(earlier, totals, 0.0), axis=0)
    inclusive = jnp.cumsum(totals, axis=0)
    factors = jnp.where(earlier, jnp.exp(jnp.where(earlier, before[None, :] - inclusive, 0.0)), 0.0)
    incoming = jnp.einsum("jh,jhde->hde", factors, states, precision=lax.Precision.HIGHEST)
    running = jnp.cumsum(log_decay, axis=0)
    query_f = (
        lin_query.reshape(tok_rows, heads_here, DH).astype(jnp.float32)
        * jnp.exp(running)[:, :, None]
    )
    carried = jnp.einsum("thd,hde->the", query_f, incoming, precision=lax.Precision.HIGHEST)
    lin_raw = local_out + carried
    lin_out = (
        (lin_raw * lax.rsqrt(jnp.mean(lin_raw * lin_raw, axis=-1, keepdims=True) + 1e-06))
        .astype(jnp.bfloat16)
        .reshape(tok_rows, head_width)
    )
    branch = jnp.dot(
        lin_out,
        lax.all_gather(out_weight, "seq", axis=1, tiled=True),
        preferred_element_type=jnp.float32,
    )
    kv_group = lax.axis_index("heads") * heads_here // (QUERY_HEADS // KVH)
    kv_mine = lax.dynamic_index_in_dim(kv_weight, kv_group, 0, keepdims=False)
    query_rows, kv_rows = (
        lax.all_gather(query_weight, "seq", axis=0, tiled=True),
        lax.all_gather(kv_mine, "seq", axis=0, tiled=True),
    )
    projection = jnp.concatenate([query_rows, kv_rows], axis=1)
    own_sum = lax.psum_scatter(
        branch.astype(jnp.bfloat16), "heads", scatter_dimension=1, tiled=True
    ).astype(jnp.float32)
    mixed_sum = stream.astype(jnp.float32) + own_sum
    stream_next = mixed_sum.astype(jnp.bfloat16)
    total_sq = lax.psum(jnp.sum(mixed_sum * mixed_sum, axis=1), "heads")
    normed = (
        mixed_sum
        * lax.rsqrt(total_sq / D + 1e-05)[:, None]
        * norm_gain.astype(jnp.float32)[None, :]
    ).astype(jnp.bfloat16)
    projected = jnp.dot(
        lax.all_gather(normed, "heads", axis=1, tiled=True),
        projection,
        preferred_element_type=jnp.float32,
    )
    projected = projected.astype(jnp.bfloat16)
    queries = projected[:, :head_width].reshape(tok_rows, heads_here, DH)
    keys_values = projected[:, head_width:]
    position = lax.axis_index("seq")
    query_pos = position * tok_rows + jnp.arange(tok_rows)
    score_scale = float(DH) ** (-0.5)

    def attend(state_in, kv_block, key_start):
        old_max, row_total, weighted = state_in
        key_count = kv_block.shape[0]
        key_part = kv_block[:, :DH]
        value_part = kv_block[:, DH:]
        scores = (
            jnp.einsum("thd,sd->hts", queries, key_part, preferred_element_type=jnp.float32)
            * score_scale
        )
        key_pos = key_start + jnp.arange(key_count)
        allowed = ((key_pos[None, :] <= query_pos[:, None]) & (key_pos[None, :] >= 0))[None, :, :]
        scores = jnp.where(allowed, scores, -1e30)
        new_max = jnp.maximum(old_max, jnp.max(scores, axis=-1))
        expos = jnp.where(allowed, jnp.exp(scores - new_max[:, :, None]), 0.0)
        rescale = jnp.exp(old_max - new_max)
        row_total = row_total * rescale + jnp.sum(expos, axis=-1)
        prob_bf16 = expos.astype(jnp.bfloat16)
        weighted = weighted * rescale[:, :, None] + jnp.einsum(
            "hts,sd->htd", prob_bf16, value_part, preferred_element_type=jnp.float32
        )
        return (new_max, row_total, weighted)

    initial = (
        jnp.full((heads_here, tok_rows), -1e30, jnp.float32),
        jnp.zeros((heads_here, tok_rows), jnp.float32),
        jnp.zeros((heads_here, tok_rows, DH), jnp.float32),
    )
    first_state = attend(initial, keys_values, position * tok_rows)
    seq_count = lax.axis_size("seq")

    def cycle_turn(turn_index, loop_state):
        moving, inner_state = loop_state
        moving = from_behind(moving, "seq", 1)
        source = position - turn_index
        return (moving, attend(inner_state, moving, source * tok_rows))

    _, final_state = lax.fori_loop(1, seq_count, cycle_turn, (keys_values, first_state))
    _, row_total, weighted = final_state
    attended = (
        jnp.transpose(weighted / row_total[:, :, None], (1, 0, 2))
        .reshape(tok_rows, head_width)
        .astype(jnp.bfloat16)
    )
    return (stream_next, attended)


def lightning_local(lin_query, lin_key, lin_value, log_decay):
    tok_rows = lin_query.shape[0]
    heads_here = log_decay.shape[1]
    nblocks = tok_rows // BLOCK
    shape4 = (tok_rows, heads_here, DH)
    q4, k4, v4 = (x.reshape(shape4) for x in (lin_query, lin_key, lin_value))
    state = jnp.zeros((heads_here, DH, DH), jnp.float32)
    starts = []
    for blk in range(nblocks):
        rows = slice(blk * BLOCK, (blk + 1) * BLOCK)
        starts.append(state)
        state = block_state(state, k4[rows], v4[rows], log_decay[rows])
    decay_total = jnp.sum(log_decay, axis=0)
    pad_rows = 16
    total_rows = jnp.broadcast_to(decay_total[:, None, None], (heads_here, pad_rows, DH))
    packed = jnp.concatenate([state, total_rows], axis=1).astype(jnp.bfloat16)
    packed, starts, lin_query, k4, v4 = lax.optimization_barrier(
        (packed, starts, lin_query, k4, v4)
    )
    q4 = lin_query.reshape(shape4)
    outs = []
    for blk in range(nblocks):
        rows = slice(blk * BLOCK, (blk + 1) * BLOCK)
        _, out = lightning_block(starts[blk], (q4[rows], k4[rows], v4[rows], log_decay[rows]))
        outs.append(out)
    local_out = jnp.concatenate(outs, axis=0)
    n_seq = lax.axis_size("seq")
    position = lax.axis_index("seq")
    incoming = jnp.zeros(state.shape, jnp.float32)
    between = jnp.zeros((heads_here,), jnp.float32)
    for dist in range(1, n_seq):
        got = from_behind(packed, "seq", dist).astype(jnp.float32)
        factor = jnp.where(dist <= position, jnp.exp(between), 0.0)
        incoming = incoming + factor[:, None, None] * got[:, :DH, :]
        between = between + got[:, DH, 0]
    running = jnp.cumsum(log_decay, axis=0)
    query_f = q4.astype(jnp.float32) * jnp.exp(running)[:, :, None]
    carried = jnp.einsum("thd,hde->the", query_f, incoming, precision=lax.Precision.HIGHEST)
    lin_raw = local_out + carried
    lin_out = (
        (lin_raw * lax.rsqrt(jnp.mean(lin_raw * lin_raw, axis=-1, keepdims=True) + 1e-06))
        .astype(jnp.bfloat16)
        .reshape(tok_rows, heads_here * DH)
    )
    return lin_out


def heads_reduce_scatter(part, n_heads):
    if n_heads != 4:
        return lax.psum_scatter(part, "heads", scatter_dimension=0, tiled=True).astype(jnp.float32)
    mine = lax.axis_index("heads")
    core = mine % 2
    chip = mine // 2
    rows = part.shape[0] // n_heads
    grid = part.reshape(2, 2, rows, part.shape[1])
    keep1 = lax.dynamic_index_in_dim(grid, core, axis=1, keepdims=False)
    send1 = lax.dynamic_index_in_dim(grid, 1 - core, axis=1, keepdims=False)
    recv1 = lax.ppermute(send1, "heads", [(i, i ^ 1) for i in range(n_heads)])
    chip_sum = keep1.astype(jnp.float32) + recv1.astype(jnp.float32)
    keep2 = lax.dynamic_index_in_dim(chip_sum, chip, axis=0, keepdims=False)
    send2 = lax.dynamic_index_in_dim(chip_sum, 1 - chip, axis=0, keepdims=False)
    recv2 = lax.ppermute(send2.astype(jnp.bfloat16), "heads", [(i, i ^ 2) for i in range(n_heads)])
    return keep2 + recv2.astype(jnp.float32)


def attention_kernel(pos_ref, q_ref, kv_ref, o_ref, s_ref):
    position = pos_ref[0]
    n_blk = kv_ref.shape[0]
    rows = q_ref.shape[0]
    score_scale = float(DH) ** (-0.5)
    query = q_ref[...]
    row_id = lax.broadcasted_iota(jnp.int32, (rows, rows), 0)
    col_id = lax.broadcasted_iota(jnp.int32, (rows, rows), 1)

    def allowed_of(dist):
        if dist == 0:
            return col_id <= row_id
        return jnp.broadcast_to(dist <= position, (rows, rows))

    row_max = jnp.full((rows, 1), -1e30, jnp.float32)
    for dist in range(n_blk):
        key = kv_ref[dist, :, :DH]
        scores = lax.dot_general(
            query, key, (((1,), (1,)), ((), ())), preferred_element_type=jnp.float32
        ) * score_scale
        scores = jnp.where(allowed_of(dist), scores, -1e30)
        s_ref[dist] = scores
        row_max = jnp.maximum(row_max, jnp.max(scores, axis=1, keepdims=True))
    row_total = jnp.zeros((rows, 1), jnp.float32)
    weighted = jnp.zeros((rows, DH), jnp.float32)
    for dist in range(n_blk):
        expos = jnp.where(allowed_of(dist), jnp.exp(s_ref[dist] - row_max), 0.0)
        row_total = row_total + jnp.sum(expos, axis=1, keepdims=True)
        weighted = weighted + jnp.dot(
            expos.astype(jnp.bfloat16), kv_ref[dist, :, DH:], preferred_element_type=jnp.float32
        )
    o_ref[...] = (weighted / row_total).astype(o_ref.dtype)


def attention_pallas(queries, kv_stack, position):
    rows, width = queries.shape
    n_blk = kv_stack.shape[0]
    local_heads = width // DH
    flops = 4 * local_heads * n_blk * rows * rows * DH
    grid_spec = pltpu.PrefetchScalarGridSpec(
        num_scalar_prefetch=1,
        grid=(local_heads,),
        in_specs=[
            pl.BlockSpec((rows, DH), lambda h, pos: (0, h)),
            pl.BlockSpec((n_blk, rows, 2 * DH), lambda h, pos: (0, 0, 0)),
        ],
        out_specs=pl.BlockSpec((rows, DH), lambda h, pos: (0, h)),
        scratch_shapes=[pltpu.VMEM((n_blk, rows, rows), jnp.float32)],
    )
    return pl.pallas_call(
        attention_kernel,
        grid_spec=grid_spec,
        out_shape=jax.ShapeDtypeStruct((rows, width), jnp.bfloat16),
        compiler_params=pltpu.CompilerParams(dimension_semantics=("arbitrary",)),
        cost_estimate=pl.CostEstimate(
            flops=flops,
            transcendentals=local_heads * n_blk * rows * rows,
            bytes_accessed=2 * queries.size * 2 + kv_stack.size * 2,
        ),
    )(jnp.reshape(position, (1,)).astype(jnp.int32), queries, kv_stack)


def shards_fast(*args):
    return shards_fast_body(*args)


def shards_fast_body(
    lin_query, lin_key, lin_value, log_decay, stream, out_weight, norm_gain, query_weight, kv_weight
):
    n_heads = lax.axis_size("heads")
    n_seq = lax.axis_size("seq")
    tok_rows = lin_query.shape[0]
    heads_here = log_decay.shape[1]
    mine_a = lax.axis_index("heads")
    mine_b = lax.axis_index("seq")
    swap = [(x * n_seq + y, y * n_seq + x) for x in range(n_heads) for y in range(n_seq)]
    gain_rows = jnp.broadcast_to(norm_gain[None, :], (16, norm_gain.shape[0]))
    split_rows = tok_rows // 2
    packed = lax.ppermute(
        jnp.concatenate([stream[:split_rows], gain_rows], axis=0), ("heads", "seq"), swap
    )
    rest = lax.ppermute(stream[split_rows:], ("heads", "seq"), swap)
    stream_t = jnp.concatenate([packed[:split_rows], rest], axis=0)
    gain_b = packed[split_rows]

    lin_out = lightning_local(lin_query, lin_key, lin_value, log_decay)
    halves = []
    half_rows = tok_rows // 2
    for half in range(2):
        lin_all = lax.all_gather(
            lin_out[half * half_rows : (half + 1) * half_rows], "seq", axis=0, tiled=True
        )
        part = jnp.dot(lin_all, out_weight, preferred_element_type=jnp.float32)
        halves.append(heads_reduce_scatter(part.astype(jnp.bfloat16), n_heads))
    own_sum = jnp.concatenate(halves, axis=0)
    mixed_sum = stream_t.astype(jnp.float32) + own_sum
    next_t = mixed_sum.astype(jnp.bfloat16)
    next_early = lax.ppermute(next_t[:half_rows], ("heads", "seq"), swap)
    next_late = lax.ppermute(next_t[half_rows:], ("heads", "seq"), swap)
    stream_next = jnp.concatenate([next_early, next_late], axis=0)
    total_sq = lax.psum(jnp.sum(mixed_sum * mixed_sum, axis=1), "seq")
    normed = (
        mixed_sum
        * lax.rsqrt(total_sq / D + 1e-05)[:, None]
        * gain_b.astype(jnp.float32)[None, :]
    ).astype(jnp.bfloat16)
    normed_all = lax.all_gather(normed, "heads", axis=0, tiled=True)
    kv_group = mine_a * heads_here // (QUERY_HEADS // KVH)
    kv_mine = lax.dynamic_index_in_dim(kv_weight, kv_group, 0, keepdims=False)
    q_part = jnp.dot(normed_all, query_weight, preferred_element_type=jnp.float32)
    kv_part = jnp.dot(normed_all, kv_mine, preferred_element_type=jnp.float32)
    queries = lax.psum_scatter(q_part.astype(jnp.bfloat16), "seq", scatter_dimension=0, tiled=True)
    kv_own = lax.psum_scatter(kv_part.astype(jnp.bfloat16), "seq", scatter_dimension=0, tiled=True)
    earlier_kv = [from_behind(kv_own, "seq", dist) for dist in range(1, n_seq)]
    kv_stack = jnp.stack([kv_own] + earlier_kv, axis=0)
    attended = attention_pallas(queries, kv_stack, mine_b)
    return (stream_next, attended)


def solution(mesh):
    n_heads = mesh.shape["heads"]
    n_seq = mesh.shape["seq"]
    fast_ok = n_heads == n_seq and QUERY_HEADS % n_heads == 0
    if fast_ok:
        heads_here = QUERY_HEADS // n_heads
        fast_ok = (QUERY_HEADS // KVH) % heads_here == 0 and D % n_seq == 0
    shards = shards_fast if fast_ok else shards_base

    return jax.shard_map(
        shards,
        mesh=mesh,
        in_specs=(
            P(("groups", "seq"), "heads"),
            P(("groups", "seq"), "heads"),
            P(("groups", "seq"), "heads"),
            P(("groups", "seq"), "heads"),
            P(("groups", "seq"), "heads"),
            P("heads", "seq"),
            P("heads"),
            P("seq", "heads"),
            P(None, "seq", None),
        ),
        out_specs=(P(("groups", "seq"), "heads"), P(("groups", "seq"), "heads")),
        check_vma=False,
    )
```
